32 devices in a mesh: grp: 4 (over z), patch: 8 (over y, x, core).
Axes of the slice: x: 2, y: 2, z: 4, core: 2. Of those that a mesh axis runs over, the one named last changes fastest.
Arguments:
- adjoint_init: float32 [4, 16, 3, 128, 128], P('grp', 'patch'), may hold values from -6 to 6
- depth: float32 [4, 16, 128, 128], P('grp', 'patch'), may hold values from 0.5 to 2
- wet_mask: int32 [4, 16, 128, 128], P('grp', 'patch'), may hold values 0 or 1
- levels: int32 [4, 16], P('grp', 'patch'), may hold values from 0 to 2
- readers: int32 [4, 16, 4], P('grp'), may hold values from -1 to 15, as said below
- green: bfloat16 [4, 512, 8192], P('grp', 'patch'), may hold values from -0.0625 to 0.0625
- fault_ids: int32 [4, 512], P('grp', 'patch'), may hold values from 0 to 2047, as said below
Outputs:
- adjoint_out: float32 [4, 16, 3, 128, 128], P('grp', 'patch')
- fault_grad: float32 [2048], replicated
The draws below stay inside these ranges and needn't reach their ends.
Inputs may be any that keep to these rules, and one draw needn't show every extreme that they name: `fault_ids`: the 512 ids of one group are distinct; different groups share ids. `readers`: within a group, patches are held 2 to an index of patch in order; the faces of the patches of one index of patch are read by the patches of any one index of patch at most 2 times, and exactly 2 times for some pair in every draw. A patch may read several faces, its own ones too; -1 marks a face that nobody reads.
All inputs are finite; a program needn't handle non-finite values. No bound on the sum of `wet_mask` on one device may be relied on, other than what follows from the above.
Results may differ from the reference program's by a relative error of at most 0.0032.
Values may be sent and summed in bfloat16 or wider, within the bound.
No kernel may reach another device: no remote copies, remote signals or barrier semaphores. Data moves between devices by JAX's collectives and lax.ppermute only.
A program may use at most 64 MiB of HBM per device.

```python
import math
import jax
import jax.numpy as jnp
from jax import lax

CELLS = 128
PATCH_DEV = 2
SRC_ROWS = 4
STEPS = 4
PEER_CAP = 2
SUBFAULTS = 512
FAULTS = 2048
PATCH_GRP = 16
SRC_GRP = 8192
N_GRP = 4
N_PATCH = 8


def pick_ids(subkey):
    return jax.random.permutation(subkey, FAULTS)[:SUBFAULTS]


def draw_fault_ids(key, part):
    group_keys = jax.random.split(jax.random.fold_in(key, 11), N_GRP)
    chosen = jax.vmap(pick_ids)(group_keys)
    return chosen.astype(jnp.int32)


def pick_peers(subkey):
    return jax.random.permutation(subkey, N_PATCH)[:(4 * PATCH_DEV + PEER_CAP - 1) // PEER_CAP]


def draw_readers(key, part):
    base = jax.random.fold_in(key, 23)
    peer_keys = jax.random.split(jax.random.fold_in(base, 1), N_GRP * N_PATCH)
    peers = jax.vmap(pick_peers)(peer_keys).astype(jnp.int32)
    face_count = 4 * PATCH_DEV
    slot_index = jnp.arange(face_count, dtype=jnp.int32) // PEER_CAP
    dest = peers[:, slot_index]
    local = jax.random.randint(jax.random.fold_in(base, 2), (N_GRP * N_PATCH, face_count), 0, PATCH_DEV).astype(jnp.int32)
    target = dest * PATCH_DEV + local
    coin = jax.random.randint(jax.random.fold_in(base, 3), (N_GRP * N_PATCH, face_count), 0, 4)
    keep_first = (jnp.arange(face_count, dtype=jnp.int32) < PEER_CAP)[None, :]
    dropped = (coin == 0) & jnp.logical_not(keep_first)
    result = jnp.where(dropped, -1, target)
    return result.reshape(N_GRP, N_PATCH * PATCH_DEV, 4).astype(jnp.int32)


def touch_ends(drawn, key, low, high):
    longest = drawn.shape.index(max(drawn.shape))
    spots = []
    for shift in (0, 1):
        where = [jax.random.randint(jax.random.fold_in(key, axis), (), 0, length) for axis, length in enumerate(drawn.shape)]
        where[longest] = (where[longest] + shift) % drawn.shape[longest]
        spots.append(tuple(where))
    return drawn.at[spots[0]].set(low).at[spots[1]].set(high)


def level_of(stream_key, dims, cuts, low, largest):
    def one(position, blocks):
        draws = jax.random.uniform(jax.random.fold_in(jax.random.fold_in(stream_key, 6), position), (blocks,), jnp.float32, low / len(cuts), largest / len(cuts))
        return jnp.repeat(jnp.exp(draws), dims[position] // blocks).reshape((-1,) + (1,) * (len(dims) - position - 1))

    gain = one(*cuts[0])
    for cut in cuts[1:]:
        gain = gain * one(*cut)
    return gain


def centred(key, shape, scale, limit, shards=(), kind=jnp.bfloat16):
    drawn = scale * jax.random.normal(key, shape, jnp.float32)
    if shards:
        drawn = drawn * level_of(key, shape, shards, -0.22, 0.18)
    return jnp.clip(drawn, -limit, limit).astype(kind)


def setup_inputs(seed: int = 0) -> dict:
    key_of = jax.random.split(jax.random.key(seed), 8)
    adjoint_init = centred(key_of[0], (N_GRP, PATCH_GRP, 3, CELLS, CELLS), 1.0, 6.0, ((0, 4), (1, 8)), jnp.float32)
    depth = jnp.clip(jnp.exp(math.log(2.0) - 1.3862944 * jax.random.uniform(key_of[1], (N_GRP, PATCH_GRP, CELLS, CELLS), jnp.float32) ** level_of(key_of[1], (N_GRP, PATCH_GRP, CELLS, CELLS), ((0, 4), (1, 8)), -0.2, 0.2)), 0.5, 2.0)
    wet_mask = touch_ends((jax.random.randint(key_of[2], (N_GRP, PATCH_GRP, CELLS, CELLS), 0, 8) < 7).astype(jnp.int32), jax.random.fold_in(key_of[2], 1), 0, 1)
    levels = touch_ends(jax.random.randint(key_of[3], (N_GRP, PATCH_GRP), 0, 3), jax.random.fold_in(key_of[3], 1), 0, 2).astype(jnp.int32)
    readers = draw_readers(jax.random.fold_in(key_of[7], 71), 0)
    green = centred(key_of[5], (N_GRP, SUBFAULTS, SRC_GRP), SRC_GRP ** -0.5, 0.0625, ((0, 4), (1, 8)))
    fault_ids = draw_fault_ids(jax.random.fold_in(key_of[7], 71), 0)
    return dict(adjoint_init=adjoint_init, depth=depth, wet_mask=wet_mask, levels=levels, readers=readers, green=green, fault_ids=fault_ids)


def level_coef(levels):
    upper = (levels >= 1).astype(jnp.float32) + 2.0 * (levels >= 2).astype(jnp.float32)
    return 0.1 * (1.0 + upper)


def diff_cols(field, west, east):
    right = jnp.concatenate([field[..., 1:], east[..., None]], axis=-1)
    left = jnp.concatenate([west[..., None], field[..., :-1]], axis=-1)
    return right - left


def diff_rows(field, south, north):
    upper = jnp.concatenate([field[..., 1:, :], north[..., None, :]], axis=-2)
    lower = jnp.concatenate([south[..., None, :], field[..., :-1, :]], axis=-2)
    return upper - lower


def face_stack(flux_x, flux_y, height):
    west = jnp.stack([flux_x[..., :, 0], height[..., :, 0]], axis=-2)
    east = jnp.stack([flux_x[..., :, -1], height[..., :, -1]], axis=-2)
    south = jnp.stack([flux_y[..., 0, :], height[..., 0, :]], axis=-2)
    north = jnp.stack([flux_y[..., -1, :], height[..., -1, :]], axis=-2)
    return jnp.stack([west, east, south, north], axis=-3)


def update(state, ghost, flux_x, flux_y, wet_float, coef):
    height = state[..., 0, :, :]
    east_flow = state[..., 1, :, :]
    north_flow = state[..., 2, :, :]
    half_coef = 0.5 * coef[..., None, None]
    grad_fx = diff_cols(flux_x, ghost[..., 0, 0, :], ghost[..., 1, 0, :])
    grad_fy = diff_rows(flux_y, ghost[..., 2, 0, :], ghost[..., 3, 0, :])
    grad_hx = diff_cols(height, ghost[..., 0, 1, :], ghost[..., 1, 1, :])
    grad_hy = diff_rows(height, ghost[..., 2, 1, :], ghost[..., 3, 1, :])
    new_height = height + half_coef * (grad_fx + grad_fy)
    new_east = wet_float * (east_flow + half_coef * grad_hx)
    new_north = wet_float * (north_flow + half_coef * grad_hy)
    return jnp.stack([new_height, new_east, new_north], axis=-3)


def reference(adjoint_init, depth, wet_mask, levels, readers, green, fault_ids):
    wet_float = wet_mask.astype(jnp.float32)
    depth_wet = wet_float * depth
    coef = level_coef(levels)
    targets = jnp.arange(PATCH_GRP, dtype=jnp.int32)
    state = adjoint_init
    for sweep in range(STEPS):
        flux_x = depth_wet * state[:, :, 1]
        flux_y = depth_wet * state[:, :, 2]
        faces = face_stack(flux_x, flux_y, state[:, :, 0])
        pieces = []
        for target in range(4):
            source = target ^ 1
            match = (readers[:, :, source][:, :, None] == targets[None, None, :]).astype(jnp.float32)
            pieces.append(jnp.einsum("gjk,gjfn->gkfn", match, faces[:, :, source], precision=lax.Precision.HIGHEST))
        ghost = jnp.stack(pieces, axis=2)
        state = update(state, ghost, flux_x, flux_y, wet_float, coef)
    deformation = state[:, :, 0, :SRC_ROWS, :].reshape(N_GRP, SRC_GRP).astype(jnp.bfloat16)
    slip = jnp.einsum("gsc,gc->gs", green.astype(jnp.float32), deformation.astype(jnp.float32), precision=lax.Precision.HIGHEST)
    fault_grad = jax.ops.segment_sum(slip.reshape(-1), fault_ids.reshape(-1), num_segments=FAULTS)
    return state, fault_grad
```

```python
import functools

import jax
import jax.numpy as jnp
from jax import lax
from jax.experimental import pallas as pl
from jax.experimental.pallas import tpu as pltpu
from jax.sharding import PartitionSpec as P

SRC_ROWS = 4
STEPS = 4
FAULTS = 2048


def level_coef(levels):
    upper = (levels >= 1).astype(jnp.float32) + 2.0 * (levels >= 2).astype(jnp.float32)
    return 0.1 * (1.0 + upper)


def _store_faces(faces_ref, k, fx, fy, h):
    n = fx.shape[-1]
    fx_t = fx.T
    h_t = h.T
    faces_ref[k, 0, 0:1, :] = fx_t[0:1, :]
    faces_ref[k, 0, 1:2, :] = h_t[0:1, :]
    faces_ref[k, 1, 0:1, :] = fx_t[n - 1:n, :]
    faces_ref[k, 1, 1:2, :] = h_t[n - 1:n, :]
    faces_ref[k, 2, 0:1, :] = fy[0:1, :]
    faces_ref[k, 2, 1:2, :] = h[0:1, :]
    faces_ref[k, 3, 0:1, :] = fy[n - 1:n, :]
    faces_ref[k, 3, 1:2, :] = h[n - 1:n, :]


def faces_kernel(state_ref, depth_ref, wet_ref, faces_ref):
    for k in range(state_ref.shape[0]):
        wet = wet_ref[k].astype(jnp.float32)
        depth_wet = wet * depth_ref[k]
        fx = depth_wet * state_ref[k, 1]
        fy = depth_wet * state_ref[k, 2]
        _store_faces(faces_ref, k, fx, fy, state_ref[k, 0])


def step_kernel(readers_ref, base_ref, hc_ref, every_ref, state_ref, depth_ref, wet_ref,
                out_ref, faces_ref, ghost_ref, turn_ref):
    local, _, n, _ = state_ref.shape
    group = every_ref.shape[0]
    base = base_ref[0]
    ghost_ref[...] = jnp.zeros_like(ghost_ref)
    turn_ref[...] = jnp.zeros_like(turn_ref)

    def gather(j, carry):
        for t in range(4):
            source = t ^ 1
            reader = readers_ref[j, source]
            face = every_ref[j, source]
            for k in range(local):
                @pl.when(reader == base + k)
                def _():
                    ghost_ref[k, t] += face
        return carry

    lax.fori_loop(0, group, gather, 0)

    col = lax.broadcasted_iota(jnp.int32, (n, n), 1)
    row = lax.broadcasted_iota(jnp.int32, (n, n), 0)

    def diff_cols(f, west, east):
        right = jnp.where(col == n - 1, east, pltpu.roll(f, n - 1, 1))
        left = jnp.where(col == 0, west, pltpu.roll(f, 1, 1))
        return right - left

    def diff_rows(f, south, north):
        upper = jnp.where(row == n - 1, north, pltpu.roll(f, n - 1, 0))
        lower = jnp.where(row == 0, south, pltpu.roll(f, 1, 0))
        return upper - lower

    for k in range(local):
        turn_ref[0:2, :] = ghost_ref[k, 0]
        turn_ref[2:4, :] = ghost_ref[k, 1]
        sides = turn_ref[...].T
        west_fx, west_h = sides[:, 0:1], sides[:, 1:2]
        east_fx, east_h = sides[:, 2:3], sides[:, 3:4]
        south_fy, south_h = ghost_ref[k, 2, 0:1, :], ghost_ref[k, 2, 1:2, :]
        north_fy, north_h = ghost_ref[k, 3, 0:1, :], ghost_ref[k, 3, 1:2, :]

        wet = wet_ref[k].astype(jnp.float32)
        depth_wet = wet * depth_ref[k]
        height = state_ref[k, 0]
        east_flow = state_ref[k, 1]
        north_flow = state_ref[k, 2]
        flux_x = depth_wet * east_flow
        flux_y = depth_wet * north_flow
        half_coef = hc_ref[k]
        new_height = height + half_coef * (
            diff_cols(flux_x, west_fx, east_fx) + diff_rows(flux_y, south_fy, north_fy)
        )
        new_east = wet * (east_flow + half_coef * diff_cols(height, west_h, east_h))
        new_north = wet * (north_flow + half_coef * diff_rows(height, south_h, north_h))
        out_ref[k, 0] = new_height
        out_ref[k, 1] = new_east
        out_ref[k, 2] = new_north
        _store_faces(faces_ref, k, depth_wet * new_east, depth_wet * new_north, new_height)


def _vmem():
    return pl.BlockSpec(memory_space=pltpu.VMEM)


def _smem():
    return pl.BlockSpec(memory_space=pltpu.SMEM)


def initial_faces(state, depth, wet_mask):
    local, _, n, _ = state.shape
    return pl.pallas_call(
        faces_kernel,
        out_shape=jax.ShapeDtypeStruct((local, 4, 2, n), jnp.float32),
        in_specs=[_vmem()] * 3,
        out_specs=_vmem(),
    )(state, depth, wet_mask)


def step(readers, base, half_coef, every_face, state, depth, wet_mask):
    local, _, n, _ = state.shape
    return pl.pallas_call(
        step_kernel,
        out_shape=(
            jax.ShapeDtypeStruct(state.shape, jnp.float32),
            jax.ShapeDtypeStruct((local, 4, 2, n), jnp.float32),
        ),
        in_specs=[_smem(), _smem(), _smem()] + [_vmem()] * 4,
        out_specs=(_vmem(), _vmem()),
        scratch_shapes=[
            pltpu.VMEM((local, 4, 2, n), jnp.float32),
            pltpu.VMEM((n, n), jnp.float32),
        ],
    )(readers, base, half_coef, every_face, state, depth, wet_mask)


def shards(adjoint_init, depth, wet_mask, levels, readers, green, fault_ids):
    state = adjoint_init[0]
    local = state.shape[0]
    half_coef = 0.5 * level_coef(levels[0])
    base = (lax.axis_index("patch") * local).astype(jnp.int32).reshape(1)
    group_readers = readers[0]
    faces = initial_faces(state, depth[0], wet_mask[0])
    for sweep in range(STEPS):
        every_face = lax.all_gather(faces, "patch", axis=0, tiled=True)
        state, faces = step(group_readers, base, half_coef, every_face, state, depth[0], wet_mask[0])
    deformation = state[:, 0, :SRC_ROWS, :].reshape(-1).astype(jnp.bfloat16)
    green_rows = green[0]
    slip = jnp.dot(
        green_rows,
        lax.all_gather(deformation, "patch", axis=0, tiled=True),
        preferred_element_type=jnp.float32,
    )
    selector = (fault_ids[0][:, None] == jnp.arange(FAULTS, dtype=jnp.int32)[None, :]).astype(
        jnp.float32
    )
    partial_grad = jnp.dot(slip, selector, precision=lax.Precision.HIGHEST)
    fault_grad = lax.psum(lax.psum(partial_grad, "patch"), "grp")
    return (state[None], fault_grad)


def solution(mesh):
    placed = (
        P("grp", "patch", None, None, None),
        P("grp", "patch", None, None),
        P("grp", "patch", None, None),
        P("grp", "patch"),
        P("grp", None, None),
        P("grp", "patch", None),
        P("grp", "patch"),
    )
    return jax.shard_map(
        shards,
        mesh=mesh,
        in_specs=placed,
        out_specs=(P("grp", "patch", None, None, None), P()),
        check_vma=False,
    )
```

```python
import jax
import jax.numpy as jnp
from jax import lax
from jax.experimental import pallas as pl
from jax.experimental.pallas import tpu as pltpu
from jax.sharding import PartitionSpec as P

SRC_ROWS = 4
STEPS = 4
FAULTS = 2048
WIDTH = 8
FIELDS = 4
KINDS = 4
COEF_ROW = KINDS * FIELDS * WIDTH
PACK_ROWS = COEF_ROW + WIDTH
HIGH = lax.Precision.HIGHEST


def level_coef(levels):
    upper = (levels >= 1).astype(jnp.float32) + 2.0 * (levels >= 2).astype(jnp.float32)
    return 0.1 * (1.0 + upper)


def pack_kernel(hc_ref, state_ref, depth_ref, wet_ref, out_ref):
    local, _, n, _ = state_ref.shape
    for k in range(local):
        wet = wet_ref[k].astype(jnp.float32)
        fields = (state_ref[k, 0], state_ref[k, 1], state_ref[k, 2], wet * depth_ref[k])
        for f, x in enumerate(fields):
            x_t = x.T
            strips = (x_t[0:WIDTH], x_t[n - WIDTH:n], x[0:WIDTH], x[n - WIDTH:n])
            for kind, strip in enumerate(strips):
                at = (kind * FIELDS + f) * WIDTH
                out_ref[k, at:at + WIDTH, :] = strip
        out_ref[k, COEF_ROW:PACK_ROWS, :] = jnp.full((WIDTH, n), hc_ref[k], jnp.float32)


def sim_kernel(base_ref, hc_ref, every_ref, q_ref, state_ref, depth_ref, wet_ref,
               out_ref, south_ref, ghost_ref, turn_ref):
    local, _, n, _ = state_ref.shape
    group = every_ref.shape[0]
    rows = group * WIDTH
    base = base_ref[0]

    def load(kind, f):
        at = (kind * FIELDS + f) * WIDTH
        return every_ref[:, at:at + WIDTH, :].reshape(rows, n)

    strips = [[load(kind, f) for f in range(FIELDS)] for kind in range(KINDS)]
    half_all = every_ref[:, COEF_ROW:PACK_ROWS, :].reshape(rows, n)

    srow = lax.broadcasted_iota(jnp.int32, (rows, n), 0) & (WIDTH - 1)
    slane = lax.broadcasted_iota(jnp.int32, (rows, n), 1)

    def across_low(f, ghost):
        return pltpu.roll(f, rows - 1, 0) - jnp.where(srow == 0, ghost, pltpu.roll(f, 1, 0))

    def across_high(f, ghost):
        return jnp.where(srow == WIDTH - 1, ghost, pltpu.roll(f, rows - 1, 0)) - pltpu.roll(f, 1, 0)

    def pick(ghost, offset):
        return jnp.sum(jnp.where(slane == srow + offset, ghost, 0.0), axis=1, keepdims=True)

    def along(f, low, high):
        right = jnp.where(slane == n - 1, high, pltpu.roll(f, n - 1, 1))
        left = jnp.where(slane == 0, low, pltpu.roll(f, 1, 1))
        return right - left

    col = lax.broadcasted_iota(jnp.int32, (n, n), 1)
    row = lax.broadcasted_iota(jnp.int32, (n, n), 0)

    def diff_cols(f, west, east):
        right = jnp.where(col == n - 1, east, pltpu.roll(f, n - 1, 1))
        left = jnp.where(col == 0, west, pltpu.roll(f, 1, 1))
        return right - left

    def diff_rows(f, south, north):
        upper = jnp.where(row == n - 1, north, pltpu.roll(f, n - 1, 0))
        lower = jnp.where(row == 0, south, pltpu.roll(f, 1, 0))
        return upper - lower

    turn_ref[...] = jnp.zeros_like(turn_ref)
    for k in range(local):
        for c in range(3):
            out_ref[k, c] = state_ref[k, c]

    for sweep in range(STEPS):
        face_data = []
        for kind in range(KINDS):
            h, e, nf, dw = strips[kind]
            flux = dw * (e if kind < 2 else nf)
            face_data.append((flux, h))
        for t in range(4):
            source = t ^ 1
            for c in range(2):
                ghost_ref[t, c] = jnp.dot(
                    q_ref[t], face_data[source][c], precision=HIGH,
                    preferred_element_type=jnp.float32,
                )

        for k in range(local):
            at = (base + k) * WIDTH
            g = [[ghost_ref[t, c, pl.ds(at, 1), :] for c in range(2)] for t in range(4)]
            turn_ref[0:1, :] = g[0][0]
            turn_ref[1:2, :] = g[0][1]
            turn_ref[2:3, :] = g[1][0]
            turn_ref[3:4, :] = g[1][1]
            sides = turn_ref[...].T
            west_fx, west_h = sides[:, 0:1], sides[:, 1:2]
            east_fx, east_h = sides[:, 2:3], sides[:, 3:4]
            wet = wet_ref[k].astype(jnp.float32)
            depth_wet = wet * depth_ref[k]
            height = out_ref[k, 0]
            east_flow = out_ref[k, 1]
            north_flow = out_ref[k, 2]
            flux_x = depth_wet * east_flow
            flux_y = depth_wet * north_flow
            half_coef = hc_ref[k]
            new_height = height + half_coef * (
                diff_cols(flux_x, west_fx, east_fx) + diff_rows(flux_y, g[2][0], g[3][0])
            )
            new_east = wet * (east_flow + half_coef * diff_cols(height, west_h, east_h))
            new_north = wet * (north_flow + half_coef * diff_rows(height, g[2][1], g[3][1]))
            out_ref[k, 0] = new_height
            out_ref[k, 1] = new_east
            out_ref[k, 2] = new_north

        gw = [ghost_ref[0, c] for c in range(2)]
        ge = [ghost_ref[1, c] for c in range(2)]
        gs = [ghost_ref[2, c] for c in range(2)]
        gn = [ghost_ref[3, c] for c in range(2)]
        advanced = []
        for kind in range(KINDS):
            h, e, nf, dw = strips[kind]
            wet = jnp.where(dw > 0.0, 1.0, 0.0)
            fx = dw * e
            fy = dw * nf
            if kind < 2:
                offset = 0 if kind == 0 else n - WIDTH
                across = across_low if kind == 0 else across_high
                ghost = gw if kind == 0 else ge
                d_fx = across(fx, ghost[0])
                d_hx = across(h, ghost[1])
                d_fy = along(fy, pick(gs[0], offset), pick(gn[0], offset))
                d_hy = along(h, pick(gs[1], offset), pick(gn[1], offset))
            else:
                offset = 0 if kind == 2 else n - WIDTH
                across = across_low if kind == 2 else across_high
                ghost = gs if kind == 2 else gn
                d_fy = across(fy, ghost[0])
                d_hy = across(h, ghost[1])
                d_fx = along(fx, pick(gw[0], offset), pick(ge[0], offset))
                d_hx = along(h, pick(gw[1], offset), pick(ge[1], offset))
            new_h = h + half_all * (d_fx + d_fy)
            new_e = wet * (e + half_all * d_hx)
            new_n = wet * (nf + half_all * d_hy)
            advanced.append((new_h, new_e, new_n, dw))
        strips = advanced

    south_ref[...] = strips[2][0]


def _vmem():
    return pl.BlockSpec(memory_space=pltpu.VMEM)


def _smem():
    return pl.BlockSpec(memory_space=pltpu.SMEM)


def pack(half_coef, state, depth, wet_mask):
    local, _, n, _ = state.shape
    return pl.pallas_call(
        pack_kernel,
        out_shape=jax.ShapeDtypeStruct((local, PACK_ROWS, n), jnp.float32),
        in_specs=[_smem()] + [_vmem()] * 3,
        out_specs=_vmem(),
    )(half_coef, state, depth, wet_mask)


def simulate(base, half_coef, every, q, state, depth, wet_mask):
    local, _, n, _ = state.shape
    rows = every.shape[0] * WIDTH
    return pl.pallas_call(
        sim_kernel,
        out_shape=(
            jax.ShapeDtypeStruct(state.shape, jnp.float32),
            jax.ShapeDtypeStruct((rows, n), jnp.float32),
        ),
        in_specs=[_smem(), _smem()] + [_vmem()] * 5,
        out_specs=(_vmem(), _vmem()),
        scratch_shapes=[
            pltpu.VMEM((4, 2, rows, n), jnp.float32),
            pltpu.VMEM((n, n), jnp.float32),
        ],
    )(base, half_coef, every, q, state, depth, wet_mask)


def ghost_selectors(group_readers):
    group = group_readers.shape[0]
    targets = jnp.arange(group, dtype=jnp.int32)
    lane = jnp.arange(WIDTH, dtype=jnp.int32)
    mats = []
    for t in range(4):
        source = t ^ 1
        match = (group_readers[None, :, source] == targets[:, None]).astype(jnp.float32)
        edge = (lane == (0 if source in (0, 2) else WIDTH - 1)).astype(jnp.float32)
        full = match[:, None, :, None] * edge[None, None, None, :]
        mats.append(jnp.broadcast_to(full, (group, WIDTH, group, WIDTH)).reshape(group * WIDTH, group * WIDTH))
    return jnp.stack(mats)


def shards(adjoint_init, depth, wet_mask, levels, readers, green, fault_ids):
    state = adjoint_init[0]
    local, _, n, _ = state.shape
    half_coef = 0.5 * level_coef(levels[0])
    base = (lax.axis_index("patch") * local).astype(jnp.int32).reshape(1)
    q = ghost_selectors(readers[0])
    packed = pack(half_coef, state, depth[0], wet_mask[0])
    every = lax.all_gather(packed, "patch", axis=0, tiled=True)
    state, south = simulate(base, half_coef, every, q, state, depth[0], wet_mask[0])
    group = every.shape[0]
    deformation = south.reshape(group, WIDTH, n)[:, :SRC_ROWS, :].reshape(-1).astype(jnp.bfloat16)
    slip = jnp.dot(green[0], deformation, preferred_element_type=jnp.float32)
    selector = (fault_ids[0][:, None] == jnp.arange(FAULTS, dtype=jnp.int32)[None, :]).astype(
        jnp.float32
    )
    partial_grad = jnp.dot(slip, selector, precision=HIGH)
    fault_grad = lax.psum(lax.psum(partial_grad, "patch"), "grp")
    return (state[None], fault_grad)


def solution(mesh):
    placed = (
        P("grp", "patch", None, None, None),
        P("grp", "patch", None, None),
        P("grp", "patch", None, None),
        P("grp", "patch"),
        P("grp", None, None),
        P("grp", "patch", None),
        P("grp", "patch"),
    )
    return jax.shard_map(
        shards,
        mesh=mesh,
        in_specs=placed,
        out_specs=(P("grp", "patch", None, None, None), P()),
        check_vma=False,
    )
```

```python
import jax
import jax.numpy as jnp
from jax import lax
from jax.experimental import pallas as pl
from jax.experimental.pallas import tpu as pltpu
from jax.sharding import PartitionSpec as P

SRC_ROWS = 4
STEPS = 4
FAULTS = 2048
WIDTH = 8
HALF = WIDTH // 2
FIELDS = 4
KINDS = 4
SOUTH_TILE = 6
COEF_TILE = SOUTH_TILE + FIELDS
PACK_ROWS = (COEF_TILE + 1) * WIDTH
HIGH = lax.Precision.HIGHEST


def level_coef(levels):
    upper = (levels >= 1).astype(jnp.float32) + 2.0 * (levels >= 2).astype(jnp.float32)
    return 0.1 * (1.0 + upper)


def pack_kernel(hc_ref, state_ref, depth_ref, wet_ref, out_ref):
    local, _, n, _ = state_ref.shape
    for k in range(local):
        wet = wet_ref[k].astype(jnp.float32)
        fields = (state_ref[k, 0], state_ref[k, 1], state_ref[k, 2], wet * depth_ref[k])
        for f, x in enumerate(fields):
            x_t = x.T
            pair, half = divmod(f, 2)
            for tile, strip in ((pair, x_t[0:HALF]), (2 + pair, x_t[n - HALF:n]), (4 + pair, x[n - HALF:n])):
                at = tile * WIDTH + half * HALF
                out_ref[k, at:at + HALF, :] = strip
            at = (SOUTH_TILE + f) * WIDTH
            out_ref[k, at:at + WIDTH, :] = x[0:WIDTH]
        at = COEF_TILE * WIDTH
        out_ref[k, at:at + WIDTH, :] = jnp.full((WIDTH, n), hc_ref[k], jnp.float32)


def sim_kernel(base_ref, hc_ref, every_ref, q_ref, state_ref, depth_ref, wet_ref,
               out_ref, south_ref, ghost_ref, turn_ref):
    local, _, n, _ = state_ref.shape
    group = every_ref.shape[0]
    rows = group * WIDTH
    base = base_ref[0]

    def tile(index):
        return every_ref[:, index * WIDTH:(index + 1) * WIDTH, :]

    def load(kind, f):
        pair, half = divmod(f, 2)
        if kind == 2:
            block = tile(SOUTH_TILE + f)
        else:
            block = tile((0, 2, None, 4)[kind] + pair)
            if half != (0 if kind == 0 else 1):
                block = pltpu.roll(block, HALF, 1)
        return block.reshape(rows, n)

    strips = [[load(kind, f) for f in range(FIELDS)] for kind in range(KINDS)]
    half_all = tile(COEF_TILE).reshape(rows, n)

    srow = lax.broadcasted_iota(jnp.int32, (rows, n), 0) & (WIDTH - 1)
    slane = lax.broadcasted_iota(jnp.int32, (rows, n), 1)

    def across_low(f, ghost):
        return pltpu.roll(f, rows - 1, 0) - jnp.where(srow == 0, ghost, pltpu.roll(f, 1, 0))

    def across_high(f, ghost):
        return jnp.where(srow == WIDTH - 1, ghost, pltpu.roll(f, rows - 1, 0)) - pltpu.roll(f, 1, 0)

    def pick(ghost, offset):
        return jnp.sum(jnp.where(slane == srow + offset, ghost, 0.0), axis=1, keepdims=True)

    def along(f, low, high):
        right = jnp.where(slane == n - 1, high, pltpu.roll(f, n - 1, 1))
        left = jnp.where(slane == 0, low, pltpu.roll(f, 1, 1))
        return right - left

    col = lax.broadcasted_iota(jnp.int32, (n, n), 1)
    row = lax.broadcasted_iota(jnp.int32, (n, n), 0)

    def diff_cols(f, west, east):
        right = jnp.where(col == n - 1, east, pltpu.roll(f, n - 1, 1))
        left = jnp.where(col == 0, west, pltpu.roll(f, 1, 1))
        return right - left

    def diff_rows(f, south, north):
        upper = jnp.where(row == n - 1, north, pltpu.roll(f, n - 1, 0))
        lower = jnp.where(row == 0, south, pltpu.roll(f, 1, 0))
        return upper - lower

    turn_ref[...] = jnp.zeros_like(turn_ref)
    for k in range(local):
        for c in range(3):
            out_ref[k, c] = state_ref[k, c]

    for sweep in range(STEPS):
        face_data = []
        for kind in range(KINDS):
            h, e, nf, dw = strips[kind]
            flux = dw * (e if kind < 2 else nf)
            face_data.append((flux, h))
        for t in range(4):
            source = t ^ 1
            for c in range(2):
                ghost_ref[t, c] = jnp.dot(
                    q_ref[t], face_data[source][c], precision=HIGH,
                    preferred_element_type=jnp.float32,
                )

        for k in range(local):
            at = (base + k) * WIDTH
            g = [[ghost_ref[t, c, pl.ds(at, 1), :] for c in range(2)] for t in range(4)]
            turn_ref[0:1, :] = g[0][0]
            turn_ref[1:2, :] = g[0][1]
            turn_ref[2:3, :] = g[1][0]
            turn_ref[3:4, :] = g[1][1]
            sides = turn_ref[...].T
            west_fx, west_h = sides[:, 0:1], sides[:, 1:2]
            east_fx, east_h = sides[:, 2:3], sides[:, 3:4]
            wet = wet_ref[k].astype(jnp.float32)
            depth_wet = wet * depth_ref[k]
            height = out_ref[k, 0]
            east_flow = out_ref[k, 1]
            north_flow = out_ref[k, 2]
            flux_x = depth_wet * east_flow
            flux_y = depth_wet * north_flow
            half_coef = hc_ref[k]
            new_height = height + half_coef * (
                diff_cols(flux_x, west_fx, east_fx) + diff_rows(flux_y, g[2][0], g[3][0])
            )
            new_east = wet * (east_flow + half_coef * diff_cols(height, west_h, east_h))
            new_north = wet * (north_flow + half_coef * diff_rows(height, g[2][1], g[3][1]))
            out_ref[k, 0] = new_height
            out_ref[k, 1] = new_east
            out_ref[k, 2] = new_north

        gw = [ghost_ref[0, c] for c in range(2)]
        ge = [ghost_ref[1, c] for c in range(2)]
        gs = [ghost_ref[2, c] for c in range(2)]
        gn = [ghost_ref[3, c] for c in range(2)]
        advanced = []
        for kind in range(KINDS):
            h, e, nf, dw = strips[kind]
            wet = jnp.where(dw > 0.0, 1.0, 0.0)
            fx = dw * e
            fy = dw * nf
            if kind < 2:
                offset = 0 if kind == 0 else n - WIDTH
                across = across_low if kind == 0 else across_high
                ghost = gw if kind == 0 else ge
                d_fx = across(fx, ghost[0])
                d_hx = across(h, ghost[1])
                d_fy = along(fy, pick(gs[0], offset), pick(gn[0], offset))
                d_hy = along(h, pick(gs[1], offset), pick(gn[1], offset))
            else:
                offset = 0 if kind == 2 else n - WIDTH
                across = across_low if kind == 2 else across_high
                ghost = gs if kind == 2 else gn
                d_fy = across(fy, ghost[0])
                d_hy = across(h, ghost[1])
                d_fx = along(fx, pick(gw[0], offset), pick(ge[0], offset))
                d_hx = along(h, pick(gw[1], offset), pick(ge[1], offset))
            new_h = h + half_all * (d_fx + d_fy)
            new_e = wet * (e + half_all * d_hx)
            new_n = wet * (nf + half_all * d_hy)
            advanced.append((new_h, new_e, new_n, dw))
        strips = advanced

    south_ref[...] = strips[2][0]


def _vmem():
    return pl.BlockSpec(memory_space=pltpu.VMEM)


def _smem():
    return pl.BlockSpec(memory_space=pltpu.SMEM)


def pack(half_coef, state, depth, wet_mask):
    local, _, n, _ = state.shape
    return pl.pallas_call(
        pack_kernel,
        out_shape=jax.ShapeDtypeStruct((local, PACK_ROWS, n), jnp.float32),
        in_specs=[_smem()] + [_vmem()] * 3,
        out_specs=_vmem(),
    )(half_coef, state, depth, wet_mask)


def simulate(base, half_coef, every, q, state, depth, wet_mask):
    local, _, n, _ = state.shape
    rows = every.shape[0] * WIDTH
    return pl.pallas_call(
        sim_kernel,
        out_shape=(
            jax.ShapeDtypeStruct(state.shape, jnp.float32),
            jax.ShapeDtypeStruct((rows, n), jnp.float32),
        ),
        in_specs=[_smem(), _smem()] + [_vmem()] * 5,
        out_specs=(_vmem(), _vmem()),
        scratch_shapes=[
            pltpu.VMEM((4, 2, rows, n), jnp.float32),
            pltpu.VMEM((n, n), jnp.float32),
        ],
    )(base, half_coef, every, q, state, depth, wet_mask)


def ghost_selectors(group_readers):
    group = group_readers.shape[0]
    targets = jnp.arange(group, dtype=jnp.int32)
    lane = jnp.arange(WIDTH, dtype=jnp.int32)
    mats = []
    for t in range(4):
        source = t ^ 1
        match = (group_readers[None, :, source] == targets[:, None]).astype(jnp.float32)
        edge = (lane == (0 if source in (0, 2) else WIDTH - 1)).astype(jnp.float32)
        full = match[:, None, :, None] * edge[None, None, None, :]
        mats.append(jnp.broadcast_to(full, (group, WIDTH, group, WIDTH)).reshape(group * WIDTH, group * WIDTH))
    return jnp.stack(mats)


def shards(adjoint_init, depth, wet_mask, levels, readers, green, fault_ids):
    state = adjoint_init[0]
    local, _, n, _ = state.shape
    half_coef = 0.5 * level_coef(levels[0])
    base = (lax.axis_index("patch") * local).astype(jnp.int32).reshape(1)
    q = ghost_selectors(readers[0])
    packed = pack(half_coef, state, depth[0], wet_mask[0])
    every = lax.all_gather(packed, "patch", axis=0, tiled=True)
    state, south = simulate(base, half_coef, every, q, state, depth[0], wet_mask[0])
    group = every.shape[0]
    deformation = south.reshape(group, WIDTH, n)[:, :SRC_ROWS, :].reshape(-1).astype(jnp.bfloat16)
    slip = jnp.dot(green[0], deformation, preferred_element_type=jnp.float32)
    selector = (fault_ids[0][:, None] == jnp.arange(FAULTS, dtype=jnp.int32)[None, :]).astype(
        jnp.float32
    )
    partial_grad = jnp.dot(slip, selector, precision=HIGH)
    group_grad = lax.all_gather(partial_grad, "patch", axis=0).sum(axis=0)
    groups = lax.axis_size("grp")
    fault_grad = group_grad
    for shift in range(1, groups):
        pairs = [(i, (i + shift) % groups) for i in range(groups)]
        fault_grad = fault_grad + lax.ppermute(group_grad, "grp", pairs)
    return (state[None], fault_grad)


def solution(mesh):
    placed = (
        P("grp", "patch", None, None, None),
        P("grp", "patch", None, None),
        P("grp", "patch", None, None),
        P("grp", "patch"),
        P("grp", None, None),
        P("grp", "patch", None),
        P("grp", "patch"),
    )
    return jax.shard_map(
        shards,
        mesh=mesh,
        in_specs=placed,
        out_specs=(P("grp", "patch", None, None, None), P()),
        check_vma=False,
    )
```

```python
import jax
import jax.numpy as jnp
from jax import lax
from jax.experimental import pallas as pl
from jax.experimental.pallas import tpu as pltpu
from jax.sharding import PartitionSpec as P

SRC_ROWS = 4
STEPS = 4
FAULTS = 2048
WIDTH = 8
HALF = WIDTH // 2
FIELDS = 4
KINDS = 4
SOUTH_TILE = 6
COEF_TILE = SOUTH_TILE + FIELDS
PACK_ROWS = (COEF_TILE + 1) * WIDTH
HIGH = lax.Precision.HIGHEST


def half_coef_rows(level, shape):
    levels = jnp.full(shape, level, jnp.int32)
    upper = (levels >= 1).astype(jnp.float32) + 2.0 * (levels >= 2).astype(jnp.float32)
    return 0.5 * (0.1 * (1.0 + upper))


def pack_kernel(level_ref, state_ref, depth_ref, wet_ref, out_ref):
    local, _, n, _ = state_ref.shape
    for k in range(local):
        wet = wet_ref[k].astype(jnp.float32)
        fields = (state_ref[k, 0], state_ref[k, 1], state_ref[k, 2], wet * depth_ref[k])
        for f, x in enumerate(fields):
            x_t = x.T
            pair, half = divmod(f, 2)
            for tile, strip in ((pair, x_t[0:HALF]), (2 + pair, x_t[n - HALF:n]), (4 + pair, x[n - HALF:n])):
                at = tile * WIDTH + half * HALF
                out_ref[k, at:at + HALF, :] = strip
            at = (SOUTH_TILE + f) * WIDTH
            out_ref[k, at:at + WIDTH, :] = x[0:WIDTH]
        at = COEF_TILE * WIDTH
        out_ref[k, at:at + WIDTH, :] = half_coef_rows(level_ref[k], (WIDTH, n))


def replay_kernel(base_ref, lanes_ref, every_ref, mine_ref, south_ref, q_ref, ghost_ref):
    group, _, n = every_ref.shape
    local = mine_ref.shape[1]
    rows = group * WIDTH
    base = base_ref[0]

    def tile(index):
        return every_ref[:, index * WIDTH:(index + 1) * WIDTH, :]

    def load(kind, f):
        pair, half = divmod(f, 2)
        if kind == 2:
            block = tile(SOUTH_TILE + f)
        else:
            block = tile((0, 2, None, 4)[kind] + pair)
            if half != (0 if kind == 0 else 1):
                block = pltpu.roll(block, HALF, 1)
        return block.reshape(rows, n)

    strips = [[load(kind, f) for f in range(FIELDS)] for kind in range(KINDS)]
    half_all = tile(COEF_TILE).reshape(rows, n)

    owner = lax.broadcasted_iota(jnp.int32, (rows, rows), 0) // WIDTH
    for t in range(4):
        source = t ^ 1
        q_ref[t] = (lanes_ref[source:source + 1, :] == owner).astype(jnp.float32)

    srow = lax.broadcasted_iota(jnp.int32, (rows, n), 0) & (WIDTH - 1)
    slane = lax.broadcasted_iota(jnp.int32, (rows, n), 1)

    def across_low(f, ghost):
        return pltpu.roll(f, rows - 1, 0) - jnp.where(srow == 0, ghost, pltpu.roll(f, 1, 0))

    def across_high(f, ghost):
        return jnp.where(srow == WIDTH - 1, ghost, pltpu.roll(f, rows - 1, 0)) - pltpu.roll(f, 1, 0)

    def pick(ghost, offset):
        return jnp.sum(jnp.where(slane == srow + offset, ghost, 0.0), axis=1, keepdims=True)

    def along(f, low, high):
        right = jnp.where(slane == n - 1, high, pltpu.roll(f, n - 1, 1))
        left = jnp.where(slane == 0, low, pltpu.roll(f, 1, 1))
        return right - left

    for sweep in range(STEPS):
        face_data = []
        for kind in range(KINDS):
            h, e, nf, dw = strips[kind]
            flux = dw * (e if kind < 2 else nf)
            face_data.append((flux, h))
        for t in range(4):
            source = t ^ 1
            for c in range(2):
                ghost_ref[t, c] = jnp.dot(
                    q_ref[t], face_data[source][c], precision=HIGH,
                    preferred_element_type=jnp.float32,
                )
        for k in range(local):
            at = (base + k) * WIDTH
            for t in range(4):
                for c in range(2):
                    mine_ref[sweep, k, 2 * t + c:2 * t + c + 1, :] = ghost_ref[t, c, pl.ds(at, 1), :]

        gw = [ghost_ref[0, c] for c in range(2)]
        ge = [ghost_ref[1, c] for c in range(2)]
        gs = [ghost_ref[2, c] for c in range(2)]
        gn = [ghost_ref[3, c] for c in range(2)]
        advanced = []
        for kind in range(KINDS):
            h, e, nf, dw = strips[kind]
            if sweep == STEPS - 1 and kind != 2:
                advanced.append(strips[kind])
                continue
            wet = jnp.where(dw > 0.0, 1.0, 0.0)
            fx = dw * e
            fy = dw * nf
            if kind < 2:
                offset = 0 if kind == 0 else n - WIDTH
                across = across_low if kind == 0 else across_high
                ghost = gw if kind == 0 else ge
                d_fx = across(fx, ghost[0])
                d_hx = across(h, ghost[1])
                d_fy = along(fy, pick(gs[0], offset), pick(gn[0], offset))
                d_hy = along(h, pick(gs[1], offset), pick(gn[1], offset))
            else:
                offset = 0 if kind == 2 else n - WIDTH
                across = across_low if kind == 2 else across_high
                ghost = gs if kind == 2 else gn
                d_fy = across(fy, ghost[0])
                d_hy = across(h, ghost[1])
                d_fx = along(fx, pick(gw[0], offset), pick(ge[0], offset))
                d_hx = along(h, pick(gw[1], offset), pick(ge[1], offset))
            new_h = h + half_all * (d_fx + d_fy)
            new_e = wet * (e + half_all * d_hx)
            new_n = wet * (nf + half_all * d_hy)
            advanced.append((new_h, new_e, new_n, dw))
        strips = advanced

    south_ref[...] = strips[2][0]


def update_kernel(level_ref, mine_ref, state_ref, depth_ref, wet_ref, out_ref, turn_ref):
    local, _, n, _ = state_ref.shape
    col = lax.broadcasted_iota(jnp.int32, (n, n), 1)
    row = lax.broadcasted_iota(jnp.int32, (n, n), 0)

    def diff_cols(f, west, east):
        right = jnp.where(col == n - 1, east, pltpu.roll(f, n - 1, 1))
        left = jnp.where(col == 0, west, pltpu.roll(f, 1, 1))
        return right - left

    def diff_rows(f, south, north):
        upper = jnp.where(row == n - 1, north, pltpu.roll(f, n - 1, 0))
        lower = jnp.where(row == 0, south, pltpu.roll(f, 1, 0))
        return upper - lower

    turn_ref[...] = jnp.zeros_like(turn_ref)
    for k in range(local):
        half_coef = half_coef_rows(level_ref[k], (1, n))
        wet = wet_ref[k].astype(jnp.float32)
        depth_wet = wet * depth_ref[k]
        height = state_ref[k, 0]
        east_flow = state_ref[k, 1]
        north_flow = state_ref[k, 2]
        for sweep in range(STEPS):
            g = mine_ref[sweep, k]
            turn_ref[0:WIDTH, :] = g
            sides = turn_ref[...].T
            west_fx, west_h = sides[:, 0:1], sides[:, 1:2]
            east_fx, east_h = sides[:, 2:3], sides[:, 3:4]
            flux_x = depth_wet * east_flow
            flux_y = depth_wet * north_flow
            new_height = height + half_coef * (
                diff_cols(flux_x, west_fx, east_fx) + diff_rows(flux_y, g[4:5], g[6:7])
            )
            new_east = wet * (east_flow + half_coef * diff_cols(height, west_h, east_h))
            new_north = wet * (north_flow + half_coef * diff_rows(height, g[5:6], g[7:8]))
            height, east_flow, north_flow = new_height, new_east, new_north
        out_ref[k, 0] = height
        out_ref[k, 1] = east_flow
        out_ref[k, 2] = north_flow


def _vmem():
    return pl.BlockSpec(memory_space=pltpu.VMEM)


def _smem():
    return pl.BlockSpec(memory_space=pltpu.SMEM)


def pack(levels, state, depth, wet_mask):
    local, _, n, _ = state.shape
    return pl.pallas_call(
        pack_kernel,
        out_shape=jax.ShapeDtypeStruct((local, PACK_ROWS, n), jnp.float32),
        in_specs=[_smem()] + [_vmem()] * 3,
        out_specs=_vmem(),
    )(levels, state, depth, wet_mask)


def replay(base, lanes, every, local):
    group, _, n = every.shape
    rows = group * WIDTH
    return pl.pallas_call(
        replay_kernel,
        out_shape=(
            jax.ShapeDtypeStruct((STEPS, local, WIDTH, n), jnp.float32),
            jax.ShapeDtypeStruct((rows, n), jnp.float32),
        ),
        in_specs=[_smem()] + [_vmem()] * 2,
        out_specs=(_vmem(), _vmem()),
        scratch_shapes=[
            pltpu.VMEM((4, rows, rows), jnp.float32),
            pltpu.VMEM((4, 2, rows, n), jnp.float32),
        ],
    )(base, lanes, every)


def update(levels, mine, state, depth, wet_mask):
    local, _, n, _ = state.shape
    cells = local * n * n
    return pl.pallas_call(
        update_kernel,
        out_shape=jax.ShapeDtypeStruct(state.shape, jnp.float32),
        in_specs=[_smem()] + [_vmem()] * 4,
        out_specs=_vmem(),
        scratch_shapes=[pltpu.VMEM((n, n), jnp.float32)],
        cost_estimate=pl.CostEstimate(
            flops=40 * STEPS * cells, transcendentals=0, bytes_accessed=4 * 8 * cells
        ),
    )(levels, mine, state, depth, wet_mask)


def reader_lanes(group_readers):
    group = group_readers.shape[0]
    lane = jnp.arange(WIDTH, dtype=jnp.int32)
    edge = jnp.array([0, WIDTH - 1, 0, WIDTH - 1], jnp.int32)
    spread = jnp.where(lane[None, None, :] == edge[:, None, None], group_readers.T[:, :, None], -1)
    return spread.reshape(4, group * WIDTH)


def all_sum(x, axis):
    size = lax.axis_size(axis)
    total = x
    for shift in range(1, size):
        pairs = [(i, (i + shift) % size) for i in range(size)]
        total = total + lax.ppermute(x, axis, pairs)
    return total


def shards(adjoint_init, depth, wet_mask, levels, readers, green, fault_ids):
    state = adjoint_init[0]
    local, _, n, _ = state.shape
    base = (lax.axis_index("patch") * local).astype(jnp.int32).reshape(1)
    packed = pack(levels[0], state, depth[0], wet_mask[0])
    every = lax.all_gather(packed, "patch", axis=0, tiled=True)
    mine, south = replay(base, reader_lanes(readers[0]), every, local)
    group = every.shape[0]
    deformation = south.reshape(group, WIDTH, n)[:, :SRC_ROWS, :].reshape(-1).astype(jnp.bfloat16)
    slip = jnp.dot(green[0], deformation, preferred_element_type=jnp.float32)
    selector = (fault_ids[0][:, None] == jnp.arange(FAULTS, dtype=jnp.int32)[None, :]).astype(
        jnp.float32
    )
    partial_grad = jnp.dot(slip, selector, precision=HIGH)
    fault_grad = all_sum(all_sum(partial_grad, "patch"), "grp")
    state = update(levels[0], mine, state, depth[0], wet_mask[0])
    return (state[None], fault_grad)


def solution(mesh):
    placed = (
        P("grp", "patch", None, None, None),
        P("grp", "patch", None, None),
        P("grp", "patch", None, None),
        P("grp", "patch"),
        P("grp", None, None),
        P("grp", "patch", None),
        P("grp", "patch"),
    )
    return jax.shard_map(
        shards,
        mesh=mesh,
        in_specs=placed,
        out_specs=(P("grp", "patch", None, None, None), P()),
        check_vma=False,
    )
```

```python
import jax
import jax.numpy as jnp
from jax import lax
from jax.experimental import pallas as pl
from jax.experimental.pallas import tpu as pltpu
from jax.sharding import PartitionSpec as P

SRC_ROWS = 4
STEPS = 4
FAULTS = 2048
WIDTH = 8
HALF = WIDTH // 2
FIELDS = 4
KINDS = 4
SOUTH_TILE = 6
COEF_TILE = SOUTH_TILE + FIELDS
PACK_ROWS = (COEF_TILE + 1) * WIDTH
HIGH = lax.Precision.HIGHEST


def half_coef_rows(level, shape):
    levels = jnp.full(shape, level, jnp.int32)
    upper = (levels >= 1).astype(jnp.float32) + 2.0 * (levels >= 2).astype(jnp.float32)
    return 0.5 * (0.1 * (1.0 + upper))


def pack_kernel(level_ref, state_ref, depth_ref, wet_ref, out_ref):
    local, _, n, _ = state_ref.shape
    for k in range(local):
        wet = wet_ref[k].astype(jnp.float32)
        fields = (state_ref[k, 0], state_ref[k, 1], state_ref[k, 2], wet * depth_ref[k])
        for f, x in enumerate(fields):
            x_t = x.T
            pair, half = divmod(f, 2)
            for tile, strip in ((pair, x_t[0:HALF]), (2 + pair, x_t[n - HALF:n]), (4 + pair, x[n - HALF:n])):
                at = tile * WIDTH + half * HALF
                out_ref[k, at:at + HALF, :] = strip
            at = (SOUTH_TILE + f) * WIDTH
            out_ref[k, at:at + WIDTH, :] = x[0:WIDTH]
        at = COEF_TILE * WIDTH
        out_ref[k, at:at + WIDTH, :] = half_coef_rows(level_ref[k], (WIDTH, n))


def replay_kernel(base_ref, readers_ref, every_ref, mine_ref, south_ref, q_ref, ghost_ref):
    group, _, n = every_ref.shape
    local = mine_ref.shape[1]
    rows = group * WIDTH
    base = base_ref[0]

    def tile(index):
        return every_ref[:, index * WIDTH:(index + 1) * WIDTH, :]

    def load(kind, f):
        pair, half = divmod(f, 2)
        if kind == 2:
            block = tile(SOUTH_TILE + f)
        else:
            block = tile((0, 2, None, 4)[kind] + pair)
            if half != (0 if kind == 0 else 1):
                block = pltpu.roll(block, HALF, 1)
        return block.reshape(rows, n)

    strips = [[load(kind, f) for f in range(FIELDS)] for kind in range(KINDS)]
    half_all = tile(COEF_TILE).reshape(rows, n)

    lane = lax.broadcasted_iota(jnp.int32, (1, rows), 1)

    def spread(j, lanes):
        return tuple(
            jnp.where(lane == j * WIDTH + (0 if s in (0, 2) else WIDTH - 1), readers_ref[j, s], lanes[s])
            for s in range(4)
        )

    empty = jnp.full((1, rows), -1, jnp.int32)
    lanes = lax.fori_loop(0, group, spread, (empty,) * 4)
    owner = lax.broadcasted_iota(jnp.int32, (rows, rows), 0) // WIDTH
    for t in range(4):
        q_ref[t] = (lanes[t ^ 1] == owner).astype(jnp.float32)

    srow = lax.broadcasted_iota(jnp.int32, (rows, n), 0) & (WIDTH - 1)
    slane = lax.broadcasted_iota(jnp.int32, (rows, n), 1)

    def across_low(f, ghost):
        return pltpu.roll(f, rows - 1, 0) - jnp.where(srow == 0, ghost, pltpu.roll(f, 1, 0))

    def across_high(f, ghost):
        return jnp.where(srow == WIDTH - 1, ghost, pltpu.roll(f, rows - 1, 0)) - pltpu.roll(f, 1, 0)

    def pick(ghost, offset):
        return jnp.sum(jnp.where(slane == srow + offset, ghost, 0.0), axis=1, keepdims=True)

    def along(f, low, high):
        right = jnp.where(slane == n - 1, high, pltpu.roll(f, n - 1, 1))
        left = jnp.where(slane == 0, low, pltpu.roll(f, 1, 1))
        return right - left

    for sweep in range(STEPS):
        face_data = []
        for kind in range(KINDS):
            h, e, nf, dw = strips[kind]
            flux = dw * (e if kind < 2 else nf)
            face_data.append((flux, h))
        for t in range(4):
            source = t ^ 1
            for c in range(2):
                ghost_ref[t, c] = jnp.dot(
                    q_ref[t], face_data[source][c], precision=HIGH,
                    preferred_element_type=jnp.float32,
                )
        for k in range(local):
            at = (base + k) * WIDTH
            for t in range(4):
                for c in range(2):
                    mine_ref[sweep, k, 2 * t + c:2 * t + c + 1, :] = ghost_ref[t, c, pl.ds(at, 1), :]

        gw = [ghost_ref[0, c] for c in range(2)]
        ge = [ghost_ref[1, c] for c in range(2)]
        gs = [ghost_ref[2, c] for c in range(2)]
        gn = [ghost_ref[3, c] for c in range(2)]
        advanced = []
        for kind in range(KINDS):
            h, e, nf, dw = strips[kind]
            if sweep == STEPS - 1 and kind != 2:
                advanced.append(strips[kind])
                continue
            wet = jnp.where(dw > 0.0, 1.0, 0.0)
            fx = dw * e
            fy = dw * nf
            if kind < 2:
                offset = 0 if kind == 0 else n - WIDTH
                across = across_low if kind == 0 else across_high
                ghost = gw if kind == 0 else ge
                d_fx = across(fx, ghost[0])
                d_hx = across(h, ghost[1])
                d_fy = along(fy, pick(gs[0], offset), pick(gn[0], offset))
                d_hy = along(h, pick(gs[1], offset), pick(gn[1], offset))
            else:
                offset = 0 if kind == 2 else n - WIDTH
                across = across_low if kind == 2 else across_high
                ghost = gs if kind == 2 else gn
                d_fy = across(fy, ghost[0])
                d_hy = across(h, ghost[1])
                d_fx = along(fx, pick(gw[0], offset), pick(ge[0], offset))
                d_hx = along(h, pick(gw[1], offset), pick(ge[1], offset))
            new_h = h + half_all * (d_fx + d_fy)
            new_e = wet * (e + half_all * d_hx)
            new_n = wet * (nf + half_all * d_hy)
            advanced.append((new_h, new_e, new_n, dw))
        strips = advanced

    south_ref[...] = strips[2][0]


def update_kernel(level_ref, mine_ref, state_ref, depth_ref, wet_ref, out_ref, turn_ref):
    local, _, n, _ = state_ref.shape
    col = lax.broadcasted_iota(jnp.int32, (n, n), 1)
    row = lax.broadcasted_iota(jnp.int32, (n, n), 0)

    def diff_cols(f, west, east):
        right = jnp.where(col == n - 1, east, pltpu.roll(f, n - 1, 1))
        left = jnp.where(col == 0, west, pltpu.roll(f, 1, 1))
        return right - left

    def diff_rows(f, south, north):
        upper = jnp.where(row == n - 1, north, pltpu.roll(f, n - 1, 0))
        lower = jnp.where(row == 0, south, pltpu.roll(f, 1, 0))
        return upper - lower

    turn_ref[...] = jnp.zeros_like(turn_ref)
    for k in range(local):
        half_coef = half_coef_rows(level_ref[k], (1, n))
        wet = wet_ref[k].astype(jnp.float32)
        depth_wet = wet * depth_ref[k]
        height = state_ref[k, 0]
        east_flow = state_ref[k, 1]
        north_flow = state_ref[k, 2]
        for sweep in range(STEPS):
            g = mine_ref[sweep, k]
            turn_ref[0:WIDTH, :] = g
            sides = turn_ref[...].T
            west_fx, west_h = sides[:, 0:1], sides[:, 1:2]
            east_fx, east_h = sides[:, 2:3], sides[:, 3:4]
            flux_x = depth_wet * east_flow
            flux_y = depth_wet * north_flow
            new_height = height + half_coef * (
                diff_cols(flux_x, west_fx, east_fx) + diff_rows(flux_y, g[4:5], g[6:7])
            )
            new_east = wet * (east_flow + half_coef * diff_cols(height, west_h, east_h))
            new_north = wet * (north_flow + half_coef * diff_rows(height, g[5:6], g[7:8]))
            height, east_flow, north_flow = new_height, new_east, new_north
        out_ref[k, 0] = height
        out_ref[k, 1] = east_flow
        out_ref[k, 2] = north_flow


def _vmem():
    return pl.BlockSpec(memory_space=pltpu.VMEM)


def _smem():
    return pl.BlockSpec(memory_space=pltpu.SMEM)


def pack(levels, state, depth, wet_mask):
    local, _, n, _ = state.shape
    return pl.pallas_call(
        pack_kernel,
        out_shape=jax.ShapeDtypeStruct((local, PACK_ROWS, n), jnp.float32),
        in_specs=[_smem()] + [_vmem()] * 3,
        out_specs=_vmem(),
    )(levels, state, depth, wet_mask)


def replay(base, readers, every, local):
    group, _, n = every.shape
    rows = group * WIDTH
    return pl.pallas_call(
        replay_kernel,
        out_shape=(
            jax.ShapeDtypeStruct((STEPS, local, WIDTH, n), jnp.float32),
            jax.ShapeDtypeStruct((rows, n), jnp.float32),
        ),
        in_specs=[_smem(), _smem(), _vmem()],
        out_specs=(_vmem(), _vmem()),
        scratch_shapes=[
            pltpu.VMEM((4, rows, rows), jnp.float32),
            pltpu.VMEM((4, 2, rows, n), jnp.float32),
        ],
    )(base, readers, every)


def update(levels, mine, state, depth, wet_mask):
    local, _, n, _ = state.shape
    cells = local * n * n
    return pl.pallas_call(
        update_kernel,
        out_shape=jax.ShapeDtypeStruct(state.shape, jnp.float32),
        in_specs=[_smem()] + [_vmem()] * 4,
        out_specs=_vmem(),
        scratch_shapes=[pltpu.VMEM((n, n), jnp.float32)],
        cost_estimate=pl.CostEstimate(
            flops=40 * STEPS * cells, transcendentals=0, bytes_accessed=4 * 8 * cells
        ),
    )(levels, mine, state, depth, wet_mask)


def all_sum(x, axis):
    size = lax.axis_size(axis)
    total = x
    for shift in range(1, size):
        pairs = [(i, (i + shift) % size) for i in range(size)]
        total = total + lax.ppermute(x, axis, pairs)
    return total


def shards(adjoint_init, depth, wet_mask, levels, readers, green, fault_ids):
    state = adjoint_init[0]
    local, _, n, _ = state.shape
    base = (lax.axis_index("patch") * local).astype(jnp.int32).reshape(1)
    packed = pack(levels[0], state, depth[0], wet_mask[0])
    every = lax.all_gather(packed, "patch", axis=0, tiled=True)
    mine, south = replay(base, readers[0], every, local)
    group = every.shape[0]
    deformation = south.reshape(group, WIDTH, n)[:, :SRC_ROWS, :].reshape(-1).astype(jnp.bfloat16)
    slip = jnp.dot(green[0], deformation, preferred_element_type=jnp.float32)
    selector = (fault_ids[0][:, None] == jnp.arange(FAULTS, dtype=jnp.int32)[None, :]).astype(
        jnp.float32
    )
    partial_grad = jnp.dot(slip, selector, precision=HIGH)
    group_grad = lax.all_gather(partial_grad, "patch", axis=0).sum(axis=0)
    fault_grad = all_sum(group_grad, "grp")
    state = update(levels[0], mine, state, depth[0], wet_mask[0])
    return (state[None], fault_grad)


def solution(mesh):
    placed = (
        P("grp", "patch", None, None, None),
        P("grp", "patch", None, None),
        P("grp", "patch", None, None),
        P("grp", "patch"),
        P("grp", None, None),
        P("grp", "patch", None),
        P("grp", "patch"),
    )
    return jax.shard_map(
        shards,
        mesh=mesh,
        in_specs=placed,
        out_specs=(P("grp", "patch", None, None, None), P()),
        check_vma=False,
    )
```

```python
import jax
import jax.numpy as jnp
from jax import lax
from jax.experimental import pallas as pl
from jax.experimental.pallas import tpu as pltpu
from jax.sharding import PartitionSpec as P

SRC_ROWS = 4
STEPS = 4
FAULTS = 2048
WIDTH = 8
HALF = WIDTH // 2
FIELDS = 4
KINDS = 4
SOUTH_TILE = 6
COEF_TILE = SOUTH_TILE + FIELDS
PACK_ROWS = (COEF_TILE + 1) * WIDTH
HIGH = lax.Precision.HIGHEST


def half_coef_rows(level, shape):
    levels = jnp.full(shape, level, jnp.int32)
    upper = (levels >= 1).astype(jnp.float32) + 2.0 * (levels >= 2).astype(jnp.float32)
    return 0.5 * (0.1 * (1.0 + upper))


def pack_kernel(level_ref, state_ref, depth_ref, wet_ref, out_ref):
    local, _, n, _ = state_ref.shape
    for k in range(local):
        wet = wet_ref[k].astype(jnp.float32)
        fields = (state_ref[k, 0], state_ref[k, 1], state_ref[k, 2], wet * depth_ref[k])
        for f, x in enumerate(fields):
            x_t = x.T
            pair, half = divmod(f, 2)
            for tile, strip in ((pair, x_t[0:HALF]), (2 + pair, x_t[n - HALF:n]), (4 + pair, x[n - HALF:n])):
                at = tile * WIDTH + half * HALF
                out_ref[k, at:at + HALF, :] = strip
            at = (SOUTH_TILE + f) * WIDTH
            out_ref[k, at:at + WIDTH, :] = x[0:WIDTH]
        at = COEF_TILE * WIDTH
        out_ref[k, at:at + WIDTH, :] = half_coef_rows(level_ref[k], (WIDTH, n))


def replay_kernel(base_ref, readers_ref, every_ref, green_ref, ids_ref, mine_ref, grad_ref,
                  q_ref, ghost_ref, south_ref):
    group, _, n = every_ref.shape
    local = mine_ref.shape[1]
    rows = group * WIDTH
    base = base_ref[0]

    def tile(index):
        return every_ref[:, index * WIDTH:(index + 1) * WIDTH, :]

    def load(kind, f):
        pair, half = divmod(f, 2)
        if kind == 2:
            block = tile(SOUTH_TILE + f)
        else:
            block = tile((0, 2, None, 4)[kind] + pair)
            if half != (0 if kind == 0 else 1):
                block = pltpu.roll(block, HALF, 1)
        return block.reshape(rows, n)

    strips = [[load(kind, f) for f in range(FIELDS)] for kind in range(KINDS)]
    half_all = tile(COEF_TILE).reshape(rows, n)

    lane = lax.broadcasted_iota(jnp.int32, (1, rows), 1)

    def spread(j, lanes):
        return tuple(
            jnp.where(lane == j * WIDTH + (0 if s in (0, 2) else WIDTH - 1), readers_ref[j, s], lanes[s])
            for s in range(4)
        )

    empty = jnp.full((1, rows), -1, jnp.int32)
    lanes = lax.fori_loop(0, group, spread, (empty,) * 4)
    owner = lax.broadcasted_iota(jnp.int32, (rows, rows), 0) // WIDTH
    for t in range(4):
        q_ref[t] = (lanes[t ^ 1] == owner).astype(jnp.float32)

    srow = lax.broadcasted_iota(jnp.int32, (rows, n), 0) & (WIDTH - 1)
    slane = lax.broadcasted_iota(jnp.int32, (rows, n), 1)

    def across_low(f, ghost):
        return pltpu.roll(f, rows - 1, 0) - jnp.where(srow == 0, ghost, pltpu.roll(f, 1, 0))

    def across_high(f, ghost):
        return jnp.where(srow == WIDTH - 1, ghost, pltpu.roll(f, rows - 1, 0)) - pltpu.roll(f, 1, 0)

    def pick(ghost, offset):
        return jnp.sum(jnp.where(slane == srow + offset, ghost, 0.0), axis=1, keepdims=True)

    def along(f, low, high):
        right = jnp.where(slane == n - 1, high, pltpu.roll(f, n - 1, 1))
        left = jnp.where(slane == 0, low, pltpu.roll(f, 1, 1))
        return right - left

    for sweep in range(STEPS):
        face_data = []
        for kind in range(KINDS):
            h, e, nf, dw = strips[kind]
            flux = dw * (e if kind < 2 else nf)
            face_data.append((flux, h))
        for t in range(4):
            source = t ^ 1
            for c in range(2):
                ghost_ref[t, c] = jnp.dot(
                    q_ref[t], face_data[source][c], precision=HIGH,
                    preferred_element_type=jnp.float32,
                )
        for k in range(local):
            at = (base + k) * WIDTH
            for t in range(4):
                for c in range(2):
                    mine_ref[sweep, k, 2 * t + c:2 * t + c + 1, :] = ghost_ref[t, c, pl.ds(at, 1), :]

        gw = [ghost_ref[0, c] for c in range(2)]
        ge = [ghost_ref[1, c] for c in range(2)]
        gs = [ghost_ref[2, c] for c in range(2)]
        gn = [ghost_ref[3, c] for c in range(2)]
        advanced = []
        for kind in range(KINDS):
            h, e, nf, dw = strips[kind]
            if sweep == STEPS - 1 and kind != 2:
                advanced.append(strips[kind])
                continue
            wet = jnp.where(dw > 0.0, 1.0, 0.0)
            fx = dw * e
            fy = dw * nf
            if kind < 2:
                offset = 0 if kind == 0 else n - WIDTH
                across = across_low if kind == 0 else across_high
                ghost = gw if kind == 0 else ge
                d_fx = across(fx, ghost[0])
                d_hx = across(h, ghost[1])
                d_fy = along(fy, pick(gs[0], offset), pick(gn[0], offset))
                d_hy = along(h, pick(gs[1], offset), pick(gn[1], offset))
            else:
                offset = 0 if kind == 2 else n - WIDTH
                across = across_low if kind == 2 else across_high
                ghost = gs if kind == 2 else gn
                d_fy = across(fy, ghost[0])
                d_hy = across(h, ghost[1])
                d_fx = along(fx, pick(gw[0], offset), pick(ge[0], offset))
                d_hx = along(h, pick(gw[1], offset), pick(ge[1], offset))
            new_h = h + half_all * (d_fx + d_fy)
            new_e = wet * (e + half_all * d_hx)
            new_n = wet * (nf + half_all * d_hy)
            advanced.append((new_h, new_e, new_n, dw))
        strips = advanced

    south_ref[...] = strips[2][0]

    subfaults = green_ref.shape[0]

    def project(r, acc):
        j, i = r // SRC_ROWS, r % SRC_ROWS
        block = green_ref[:, pl.ds(pl.multiple_of(r * n, n), n)].astype(jnp.float32)
        shown = south_ref[pl.ds(j * WIDTH + i, 1), :].astype(jnp.bfloat16).astype(jnp.float32)
        return acc + block * shown

    acc = lax.fori_loop(0, group * SRC_ROWS, project, jnp.zeros((subfaults, n), jnp.float32))
    slip = jnp.sum(acc, axis=1, keepdims=True)
    ghost_ref[0, 0] = jnp.zeros((rows, n), jnp.float32)
    ghost_ref[0, 0, 0:1, 0:subfaults] = ids_ref[...].astype(jnp.float32)
    ids = ghost_ref[0, 0, 0:n, :].T[0:subfaults, 0:1]
    faults = grad_ref.shape[1]
    which = lax.broadcasted_iota(jnp.int32, (subfaults, faults), 1).astype(jnp.float32)
    grad_ref[...] = jnp.sum(jnp.where(which == ids, slip, 0.0), axis=0, keepdims=True)


def update_kernel(level_ref, mine_ref, state_ref, depth_ref, wet_ref, out_ref, turn_ref):
    local, _, n, _ = state_ref.shape
    col = lax.broadcasted_iota(jnp.int32, (n, n), 1)
    row = lax.broadcasted_iota(jnp.int32, (n, n), 0)

    def diff_cols(f, west, east):
        right = jnp.where(col == n - 1, east, pltpu.roll(f, n - 1, 1))
        left = jnp.where(col == 0, west, pltpu.roll(f, 1, 1))
        return right - left

    def diff_rows(f, south, north):
        upper = jnp.where(row == n - 1, north, pltpu.roll(f, n - 1, 0))
        lower = jnp.where(row == 0, south, pltpu.roll(f, 1, 0))
        return upper - lower

    turn_ref[...] = jnp.zeros_like(turn_ref)
    for k in range(local):
        half_coef = half_coef_rows(level_ref[k], (1, n))
        wet = wet_ref[k].astype(jnp.float32)
        depth_wet = wet * depth_ref[k]
        height = state_ref[k, 0]
        east_flow = state_ref[k, 1]
        north_flow = state_ref[k, 2]
        for sweep in range(STEPS):
            g = mine_ref[sweep, k]
            turn_ref[0:WIDTH, :] = g
            sides = turn_ref[...].T
            west_fx, west_h = sides[:, 0:1], sides[:, 1:2]
            east_fx, east_h = sides[:, 2:3], sides[:, 3:4]
            flux_x = depth_wet * east_flow
            flux_y = depth_wet * north_flow
            new_height = height + half_coef * (
                diff_cols(flux_x, west_fx, east_fx) + diff_rows(flux_y, g[4:5], g[6:7])
            )
            new_east = wet * (east_flow + half_coef * diff_cols(height, west_h, east_h))
            new_north = wet * (north_flow + half_coef * diff_rows(height, g[5:6], g[7:8]))
            height, east_flow, north_flow = new_height, new_east, new_north
        out_ref[k, 0] = height
        out_ref[k, 1] = east_flow
        out_ref[k, 2] = north_flow


def _vmem():
    return pl.BlockSpec(memory_space=pltpu.VMEM)


def _smem():
    return pl.BlockSpec(memory_space=pltpu.SMEM)


def pack(levels, state, depth, wet_mask):
    local, _, n, _ = state.shape
    return pl.pallas_call(
        pack_kernel,
        out_shape=jax.ShapeDtypeStruct((local, PACK_ROWS, n), jnp.float32),
        in_specs=[_smem()] + [_vmem()] * 3,
        out_specs=_vmem(),
    )(levels, state, depth, wet_mask)


def replay(base, readers, every, green, ids, local):
    group, _, n = every.shape
    rows = group * WIDTH
    return pl.pallas_call(
        replay_kernel,
        out_shape=(
            jax.ShapeDtypeStruct((STEPS, local, WIDTH, n), jnp.float32),
            jax.ShapeDtypeStruct((1, FAULTS), jnp.float32),
        ),
        in_specs=[_smem(), _smem()] + [_vmem()] * 3,
        out_specs=(_vmem(), _vmem()),
        scratch_shapes=[
            pltpu.VMEM((4, rows, rows), jnp.float32),
            pltpu.VMEM((4, 2, rows, n), jnp.float32),
            pltpu.VMEM((rows, n), jnp.float32),
        ],
    )(base, readers, every, green, ids)


def update(levels, mine, state, depth, wet_mask):
    local, _, n, _ = state.shape
    cells = local * n * n
    return pl.pallas_call(
        update_kernel,
        out_shape=jax.ShapeDtypeStruct(state.shape, jnp.float32),
        in_specs=[_smem()] + [_vmem()] * 4,
        out_specs=_vmem(),
        scratch_shapes=[pltpu.VMEM((n, n), jnp.float32)],
        cost_estimate=pl.CostEstimate(
            flops=40 * STEPS * cells, transcendentals=0, bytes_accessed=4 * 8 * cells
        ),
    )(levels, mine, state, depth, wet_mask)


def all_sum(x, axis):
    size = lax.axis_size(axis)
    total = x
    for shift in range(1, size):
        pairs = [(i, (i + shift) % size) for i in range(size)]
        total = total + lax.ppermute(x, axis, pairs)
    return total


def shards(adjoint_init, depth, wet_mask, levels, readers, green, fault_ids):
    state = adjoint_init[0]
    local, _, n, _ = state.shape
    base = (lax.axis_index("patch") * local).astype(jnp.int32).reshape(1)
    packed = pack(levels[0], state, depth[0], wet_mask[0])
    every = lax.all_gather(packed, "patch", axis=0, tiled=True)
    mine, partial_grad = replay(base, readers[0], every, green[0], fault_ids[0].reshape(1, -1), local)
    partial_grad = partial_grad.reshape(-1)
    group_grad = lax.all_gather(partial_grad, "patch", axis=0).sum(axis=0)
    fault_grad = all_sum(group_grad, "grp")
    state = update(levels[0], mine, state, depth[0], wet_mask[0])
    return (state[None], fault_grad)


def solution(mesh):
    placed = (
        P("grp", "patch", None, None, None),
        P("grp", "patch", None, None),
        P("grp", "patch", None, None),
        P("grp", "patch"),
        P("grp", None, None),
        P("grp", "patch", None),
        P("grp", "patch"),
    )
    return jax.shard_map(
        shards,
        mesh=mesh,
        in_specs=placed,
        out_specs=(P("grp", "patch", None, None, None), P()),
        check_vma=False,
    )
```

```python
import jax
import jax.numpy as jnp
from jax import lax
from jax.experimental import pallas as pl
from jax.experimental.pallas import tpu as pltpu
from jax.sharding import PartitionSpec as P

SRC_ROWS = 4
STEPS = 4
FAULTS = 2048
WIDTH = 8
HALF = WIDTH // 2
FIELDS = 4
KINDS = 3
NORTH_TILE = FIELDS
SOUTH_TILE = NORTH_TILE + 2
COEF_TILE = SOUTH_TILE + FIELDS
PACK_ROWS = (COEF_TILE + 1) * WIDTH
HIGH = lax.Precision.HIGHEST


def half_coef_rows(level, shape):
    levels = jnp.full(shape, level, jnp.int32)
    upper = (levels >= 1).astype(jnp.float32) + 2.0 * (levels >= 2).astype(jnp.float32)
    return 0.5 * (0.1 * (1.0 + upper))


def pack_kernel(level_ref, state_ref, depth_ref, wet_ref, out_ref):
    local, _, n, _ = state_ref.shape
    for k in range(local):
        wet = wet_ref[k].astype(jnp.float32)
        fields = (state_ref[k, 0], state_ref[k, 1], state_ref[k, 2], wet * depth_ref[k])
        for f, x in enumerate(fields):
            x_t = x.T
            pair, half = divmod(f, 2)
            at = f * WIDTH
            out_ref[k, at:at + HALF, :] = x_t[0:HALF]
            out_ref[k, at + HALF:at + WIDTH, :] = x_t[n - HALF:n]
            at = (NORTH_TILE + pair) * WIDTH + half * HALF
            out_ref[k, at:at + HALF, :] = x[n - HALF:n]
            at = (SOUTH_TILE + f) * WIDTH
            out_ref[k, at:at + WIDTH, :] = x[0:WIDTH]
        at = COEF_TILE * WIDTH
        out_ref[k, at:at + WIDTH, :] = half_coef_rows(level_ref[k], (WIDTH, n))


def replay_kernel(base_ref, readers_ref, every_ref, green_ref, ids_ref, mine_ref, grad_ref,
                  q_ref, ghost_ref, south_ref):
    group, _, n = every_ref.shape
    local = mine_ref.shape[1]
    rows = group * WIDTH
    base = base_ref[0]

    def tile(index):
        return every_ref[:, index * WIDTH:(index + 1) * WIDTH, :]

    def load(kind, f):
        pair, half = divmod(f, 2)
        if kind == 0:
            block = tile(f)
        elif kind == 1:
            block = tile(SOUTH_TILE + f)
        else:
            block = tile(NORTH_TILE + pair)
            if half == 0:
                block = pltpu.roll(block, HALF, 1)
        return block.reshape(rows, n)

    strips = [[load(kind, f) for f in range(FIELDS)] for kind in range(KINDS)]
    half_all = tile(COEF_TILE).reshape(rows, n)

    lane = lax.broadcasted_iota(jnp.int32, (1, rows), 1)

    def spread(j, lanes):
        return tuple(
            jnp.where(lane == j * WIDTH + (0 if s in (0, 2) else WIDTH - 1), readers_ref[j, s], lanes[s])
            for s in range(4)
        )

    empty = jnp.full((1, rows), -1, jnp.int32)
    lanes = lax.fori_loop(0, group, spread, (empty,) * 4)
    owner = lax.broadcasted_iota(jnp.int32, (rows, rows), 0) // WIDTH
    for t in range(4):
        q_ref[t] = (lanes[t ^ 1] == owner).astype(jnp.float32)

    srow = lax.broadcasted_iota(jnp.int32, (rows, n), 0) & (WIDTH - 1)
    slane = lax.broadcasted_iota(jnp.int32, (rows, n), 1)

    def across_low(f, ghost):
        return pltpu.roll(f, rows - 1, 0) - jnp.where(srow == 0, ghost, pltpu.roll(f, 1, 0))

    def across_high(f, ghost):
        return jnp.where(srow == WIDTH - 1, ghost, pltpu.roll(f, rows - 1, 0)) - pltpu.roll(f, 1, 0)

    def pick(ghost, offset):
        return jnp.sum(jnp.where(slane == srow + offset, ghost, 0.0), axis=1, keepdims=True)

    def along(f, low, high):
        right = jnp.where(slane == n - 1, high, pltpu.roll(f, n - 1, 1))
        left = jnp.where(slane == 0, low, pltpu.roll(f, 1, 1))
        return right - left

    far = jnp.where(srow >= HALF, n - WIDTH, 0)
    for sweep in range(STEPS):
        face_data = []
        for kind in range(KINDS):
            h, e, nf, dw = strips[kind]
            flux = dw * (e if kind == 0 else nf)
            face_data.append((flux, h))
        for t in range(4):
            source = t ^ 1
            for c in range(2):
                ghost_ref[t, c] = jnp.dot(
                    q_ref[t], face_data[(0, 0, 1, 2)[source]][c], precision=HIGH,
                    preferred_element_type=jnp.float32,
                )
        for k in range(local):
            at = (base + k) * WIDTH
            for t in range(4):
                for c in range(2):
                    mine_ref[sweep, k, 2 * t + c:2 * t + c + 1, :] = ghost_ref[t, c, pl.ds(at, 1), :]

        gw = [ghost_ref[0, c] for c in range(2)]
        ge = [ghost_ref[1, c] for c in range(2)]
        gs = [ghost_ref[2, c] for c in range(2)]
        gn = [ghost_ref[3, c] for c in range(2)]
        advanced = []
        for kind in range(KINDS):
            h, e, nf, dw = strips[kind]
            if sweep == STEPS - 1 and kind != 1:
                advanced.append(strips[kind])
                continue
            wet = jnp.where(dw > 0.0, 1.0, 0.0)
            fx = dw * e
            fy = dw * nf
            if kind == 0:
                def across(f, west, east):
                    upper = jnp.where(srow == WIDTH - 1, east, pltpu.roll(f, rows - 1, 0))
                    lower = jnp.where(srow == 0, west, pltpu.roll(f, 1, 0))
                    return upper - lower
                d_fx = across(fx, gw[0], ge[0])
                d_hx = across(h, gw[1], ge[1])
                d_fy = along(fy, pick(gs[0], far), pick(gn[0], far))
                d_hy = along(h, pick(gs[1], far), pick(gn[1], far))
            else:
                offset = 0 if kind == 1 else n - WIDTH
                across = across_low if kind == 1 else across_high
                ghost = gs if kind == 1 else gn
                d_fy = across(fy, ghost[0])
                d_hy = across(h, ghost[1])
                d_fx = along(fx, pick(gw[0], offset), pick(ge[0], offset))
                d_hx = along(h, pick(gw[1], offset), pick(ge[1], offset))
            new_h = h + half_all * (d_fx + d_fy)
            new_e = wet * (e + half_all * d_hx)
            new_n = wet * (nf + half_all * d_hy)
            advanced.append((new_h, new_e, new_n, dw))
        strips = advanced

    south_ref[...] = strips[1][0]

    subfaults = green_ref.shape[0]

    def project(r, acc):
        j, i = r // SRC_ROWS, r % SRC_ROWS
        block = green_ref[:, pl.ds(pl.multiple_of(r * n, n), n)].astype(jnp.float32)
        shown = south_ref[pl.ds(j * WIDTH + i, 1), :].astype(jnp.bfloat16).astype(jnp.float32)
        return acc + block * shown

    acc = lax.fori_loop(0, group * SRC_ROWS, project, jnp.zeros((subfaults, n), jnp.float32), unroll=8)
    slip = jnp.sum(acc, axis=1, keepdims=True)
    ghost_ref[0, 0] = jnp.zeros((rows, n), jnp.float32)
    ghost_ref[0, 0, 0:1, 0:subfaults] = ids_ref[...].astype(jnp.float32)
    ids = ghost_ref[0, 0, 0:n, :].T[0:subfaults, 0:1]
    faults = grad_ref.shape[1]
    which = lax.broadcasted_iota(jnp.int32, (subfaults, faults), 1).astype(jnp.float32)
    grad_ref[...] = jnp.sum(jnp.where(which == ids, slip, 0.0), axis=0, keepdims=True)


def update_kernel(level_ref, mine_ref, state_ref, depth_ref, wet_ref, out_ref, turn_ref):
    local, _, n, _ = state_ref.shape
    col = lax.broadcasted_iota(jnp.int32, (n, n), 1)
    row = lax.broadcasted_iota(jnp.int32, (n, n), 0)

    def diff_cols(f, west, east):
        right = jnp.where(col == n - 1, east, pltpu.roll(f, n - 1, 1))
        left = jnp.where(col == 0, west, pltpu.roll(f, 1, 1))
        return right - left

    def diff_rows(f, south, north):
        upper = jnp.where(row == n - 1, north, pltpu.roll(f, n - 1, 0))
        lower = jnp.where(row == 0, south, pltpu.roll(f, 1, 0))
        return upper - lower

    turn_ref[...] = jnp.zeros_like(turn_ref)
    for k in range(local):
        half_coef = half_coef_rows(level_ref[k], (1, n))
        wet = wet_ref[k].astype(jnp.float32)
        depth_wet = wet * depth_ref[k]
        height = state_ref[k, 0]
        east_flow = state_ref[k, 1]
        north_flow = state_ref[k, 2]
        for sweep in range(STEPS):
            g = mine_ref[sweep, k]
            turn_ref[0:WIDTH, :] = g
            sides = turn_ref[...].T
            west_fx, west_h = sides[:, 0:1], sides[:, 1:2]
            east_fx, east_h = sides[:, 2:3], sides[:, 3:4]
            flux_x = depth_wet * east_flow
            flux_y = depth_wet * north_flow
            new_height = height + half_coef * (
                diff_cols(flux_x, west_fx, east_fx) + diff_rows(flux_y, g[4:5], g[6:7])
            )
            new_east = wet * (east_flow + half_coef * diff_cols(height, west_h, east_h))
            new_north = wet * (north_flow + half_coef * diff_rows(height, g[5:6], g[7:8]))
            height, east_flow, north_flow = new_height, new_east, new_north
        out_ref[k, 0] = height
        out_ref[k, 1] = east_flow
        out_ref[k, 2] = north_flow


def _vmem():
    return pl.BlockSpec(memory_space=pltpu.VMEM)


def _smem():
    return pl.BlockSpec(memory_space=pltpu.SMEM)


def pack(levels, state, depth, wet_mask):
    local, _, n, _ = state.shape
    return pl.pallas_call(
        pack_kernel,
        out_shape=jax.ShapeDtypeStruct((local, PACK_ROWS, n), jnp.float32),
        in_specs=[_smem()] + [_vmem()] * 3,
        out_specs=_vmem(),
    )(levels, state, depth, wet_mask)


def replay(base, readers, every, green, ids, local):
    group, _, n = every.shape
    rows = group * WIDTH
    return pl.pallas_call(
        replay_kernel,
        out_shape=(
            jax.ShapeDtypeStruct((STEPS, local, WIDTH, n), jnp.float32),
            jax.ShapeDtypeStruct((1, FAULTS), jnp.float32),
        ),
        in_specs=[_smem(), _smem()] + [_vmem()] * 3,
        out_specs=(_vmem(), _vmem()),
        scratch_shapes=[
            pltpu.VMEM((4, rows, rows), jnp.float32),
            pltpu.VMEM((4, 2, rows, n), jnp.float32),
            pltpu.VMEM((rows, n), jnp.float32),
        ],
    )(base, readers, every, green, ids)


def update(levels, mine, state, depth, wet_mask):
    local, _, n, _ = state.shape
    cells = local * n * n
    return pl.pallas_call(
        update_kernel,
        out_shape=jax.ShapeDtypeStruct(state.shape, jnp.float32),
        in_specs=[_smem()] + [_vmem()] * 4,
        out_specs=_vmem(),
        scratch_shapes=[pltpu.VMEM((n, n), jnp.float32)],
        cost_estimate=pl.CostEstimate(
            flops=40 * STEPS * cells, transcendentals=0, bytes_accessed=4 * 8 * cells
        ),
    )(levels, mine, state, depth, wet_mask)


def all_sum(x, axis):
    size = lax.axis_size(axis)
    total = x
    for shift in range(1, size):
        pairs = [(i, (i + shift) % size) for i in range(size)]
        total = total + lax.ppermute(x, axis, pairs)
    return total


def shards(adjoint_init, depth, wet_mask, levels, readers, green, fault_ids):
    state = adjoint_init[0]
    local, _, n, _ = state.shape
    base = (lax.axis_index("patch") * local).astype(jnp.int32).reshape(1)
    packed = pack(levels[0], state, depth[0], wet_mask[0])
    every = lax.all_gather(packed, "patch", axis=0, tiled=True)
    mine, partial_grad = replay(base, readers[0], every, green[0], fault_ids[0].reshape(1, -1), local)
    partial_grad = partial_grad.reshape(-1)
    group_grad = lax.all_gather(partial_grad, "patch", axis=0).sum(axis=0)
    fault_grad = all_sum(group_grad, "grp")
    state = update(levels[0], mine, state, depth[0], wet_mask[0])
    return (state[None], fault_grad)


def solution(mesh):
    placed = (
        P("grp", "patch", None, None, None),
        P("grp", "patch", None, None),
        P("grp", "patch", None, None),
        P("grp", "patch"),
        P("grp", None, None),
        P("grp", "patch", None),
        P("grp", "patch"),
    )
    return jax.shard_map(
        shards,
        mesh=mesh,
        in_specs=placed,
        out_specs=(P("grp", "patch", None, None, None), P()),
        check_vma=False,
    )
```

```python
import jax
import jax.numpy as jnp
from jax import lax
from jax.experimental import pallas as pl
from jax.experimental.pallas import tpu as pltpu
from jax.sharding import PartitionSpec as P

SRC_ROWS = 4
STEPS = 4
FAULTS = 2048
WIDTH = 8
HALF = WIDTH // 2
FIELDS = 4
KINDS = 3
NORTH_TILE = FIELDS
SOUTH_TILE = NORTH_TILE + 2
COEF_TILE = SOUTH_TILE + FIELDS
PACK_ROWS = (COEF_TILE + 1) * WIDTH
HIGH = lax.Precision.HIGHEST


def half_coef_rows(level, shape):
    levels = jnp.full(shape, level, jnp.int32)
    upper = (levels >= 1).astype(jnp.float32) + 2.0 * (levels >= 2).astype(jnp.float32)
    return 0.5 * (0.1 * (1.0 + upper))


def pack_kernel(level_ref, state_ref, depth_ref, wet_ref, out_ref):
    local, _, n, _ = state_ref.shape
    lane = lax.broadcasted_iota(jnp.int32, (n, n), 1)
    for k in range(local):
        wet = wet_ref[k].astype(jnp.float32)
        fields = (state_ref[k, 0], state_ref[k, 1], state_ref[k, 2], wet * depth_ref[k])
        columns = jnp.zeros((n, n), jnp.float32)
        for f, x in enumerate(fields):
            at = f * WIDTH
            near = pltpu.roll(x, at, 1)
            far = pltpu.roll(x, (at + WIDTH - n) % n, 1)
            columns = jnp.where((lane >= at) & (lane < at + HALF), near, columns)
            columns = jnp.where((lane >= at + HALF) & (lane < at + WIDTH), far, columns)
            pair, half = divmod(f, 2)
            at = (NORTH_TILE + pair) * WIDTH + half * HALF
            out_ref[k, at:at + HALF, :] = x[n - HALF:n]
            at = (SOUTH_TILE + f) * WIDTH
            out_ref[k, at:at + WIDTH, :] = x[0:WIDTH]
        out_ref[k, 0:FIELDS * WIDTH, :] = columns.T[0:FIELDS * WIDTH]
        at = COEF_TILE * WIDTH
        out_ref[k, at:at + WIDTH, :] = half_coef_rows(level_ref[k], (WIDTH, n))


def replay_kernel(base_ref, readers_ref, every_ref, green_ref, ids_ref, mine_ref, grad_ref,
                  q_ref, ghost_ref, south_ref):
    group, _, n = every_ref.shape
    local = mine_ref.shape[1]
    rows = group * WIDTH
    base = base_ref[0]

    def tile(index):
        return every_ref[:, index * WIDTH:(index + 1) * WIDTH, :]

    def load(kind, f):
        pair, half = divmod(f, 2)
        if kind == 0:
            block = tile(f)
        elif kind == 1:
            block = tile(SOUTH_TILE + f)
        else:
            block = tile(NORTH_TILE + pair)
            if half == 0:
                block = pltpu.roll(block, HALF, 1)
        return block.reshape(rows, n)

    strips = [[load(kind, f) for f in range(FIELDS)] for kind in range(KINDS)]
    half_all = tile(COEF_TILE).reshape(rows, n)

    lane = lax.broadcasted_iota(jnp.int32, (1, rows), 1)

    def spread(j, lanes):
        return tuple(
            jnp.where(lane == j * WIDTH + (0 if s in (0, 2) else WIDTH - 1), readers_ref[j, s], lanes[s])
            for s in range(4)
        )

    empty = jnp.full((1, rows), -1, jnp.int32)
    lanes = lax.fori_loop(0, group, spread, (empty,) * 4)
    owner = lax.broadcasted_iota(jnp.int32, (rows, rows), 0) // WIDTH
    for t in range(4):
        q_ref[t] = (lanes[t ^ 1] == owner).astype(jnp.bfloat16)

    srow = lax.broadcasted_iota(jnp.int32, (rows, n), 0) & (WIDTH - 1)
    slane = lax.broadcasted_iota(jnp.int32, (rows, n), 1)

    def across_low(f, ghost):
        return pltpu.roll(f, rows - 1, 0) - jnp.where(srow == 0, ghost, pltpu.roll(f, 1, 0))

    def across_high(f, ghost):
        return jnp.where(srow == WIDTH - 1, ghost, pltpu.roll(f, rows - 1, 0)) - pltpu.roll(f, 1, 0)

    def pick(ghost, offset):
        return jnp.sum(jnp.where(slane == srow + offset, ghost, 0.0), axis=1, keepdims=True)

    def along(f, low, high):
        right = jnp.where(slane == n - 1, high, pltpu.roll(f, n - 1, 1))
        left = jnp.where(slane == 0, low, pltpu.roll(f, 1, 1))
        return right - left

    far = jnp.where(srow >= HALF, n - WIDTH, 0)
    for sweep in range(STEPS):
        face_data = []
        for kind in range(KINDS):
            h, e, nf, dw = strips[kind]
            flux = dw * (e if kind == 0 else nf)
            face_data.append((flux, h))
        pieces = []
        for flux, h in face_data:
            rest = jnp.concatenate([flux, h], axis=1)
            parts = []
            for _ in range(3):
                part = rest.astype(jnp.bfloat16)
                rest = rest - part.astype(jnp.float32)
                parts.append(part)
            pieces.append(parts)
        for t in range(4):
            parts = pieces[(0, 0, 1, 2)[t ^ 1]]
            total = None
            for part in parts:
                term = jnp.dot(q_ref[t], part, preferred_element_type=jnp.float32)
                total = term if total is None else total + term
            ghost_ref[t, 0] = total[:, 0:n]
            ghost_ref[t, 1] = total[:, n:2 * n]
        for k in range(local):
            at = (base + k) * WIDTH
            for t in range(4):
                for c in range(2):
                    mine_ref[sweep, k, 2 * t + c:2 * t + c + 1, :] = ghost_ref[t, c, pl.ds(at, 1), :]

        gw = [ghost_ref[0, c] for c in range(2)]
        ge = [ghost_ref[1, c] for c in range(2)]
        gs = [ghost_ref[2, c] for c in range(2)]
        gn = [ghost_ref[3, c] for c in range(2)]
        advanced = []
        for kind in range(KINDS):
            h, e, nf, dw = strips[kind]
            if sweep == STEPS - 1 and kind != 1:
                advanced.append(strips[kind])
                continue
            wet = jnp.where(dw > 0.0, 1.0, 0.0)
            fx = dw * e
            fy = dw * nf
            if kind == 0:
                def across(f, west, east):
                    upper = jnp.where(srow == WIDTH - 1, east, pltpu.roll(f, rows - 1, 0))
                    lower = jnp.where(srow == 0, west, pltpu.roll(f, 1, 0))
                    return upper - lower
                d_fx = across(fx, gw[0], ge[0])
                d_hx = across(h, gw[1], ge[1])
                d_fy = along(fy, pick(gs[0], far), pick(gn[0], far))
                d_hy = along(h, pick(gs[1], far), pick(gn[1], far))
            else:
                offset = 0 if kind == 1 else n - WIDTH
                across = across_low if kind == 1 else across_high
                ghost = gs if kind == 1 else gn
                d_fy = across(fy, ghost[0])
                d_hy = across(h, ghost[1])
                d_fx = along(fx, pick(gw[0], offset), pick(ge[0], offset))
                d_hx = along(h, pick(gw[1], offset), pick(ge[1], offset))
            new_h = h + half_all * (d_fx + d_fy)
            new_e = wet * (e + half_all * d_hx)
            new_n = wet * (nf + half_all * d_hy)
            advanced.append((new_h, new_e, new_n, dw))
        strips = advanced

    south_ref[...] = strips[1][0]

    subfaults = green_ref.shape[0]

    def project(r, acc):
        j, i = r // SRC_ROWS, r % SRC_ROWS
        block = green_ref[:, pl.ds(pl.multiple_of(r * n, n), n)].astype(jnp.float32)
        shown = south_ref[pl.ds(j * WIDTH + i, 1), :].astype(jnp.bfloat16).astype(jnp.float32)
        return acc + block * shown

    acc = lax.fori_loop(0, group * SRC_ROWS, project, jnp.zeros((subfaults, n), jnp.float32), unroll=8)
    slip = jnp.sum(acc, axis=1, keepdims=True)
    ghost_ref[0, 0] = jnp.zeros((rows, n), jnp.float32)
    ghost_ref[0, 0, 0:1, 0:subfaults] = ids_ref[...].astype(jnp.float32)
    ids = ghost_ref[0, 0, 0:n, :].T[0:subfaults, 0:1]
    faults = grad_ref.shape[1]
    which = lax.broadcasted_iota(jnp.int32, (subfaults, faults), 1).astype(jnp.float32)
    grad_ref[...] = jnp.sum(jnp.where(which == ids, slip, 0.0), axis=0, keepdims=True)


def update_kernel(level_ref, mine_ref, state_ref, depth_ref, wet_ref, out_ref, turn_ref):
    local, _, n, _ = state_ref.shape
    col = lax.broadcasted_iota(jnp.int32, (n, n), 1)
    row = lax.broadcasted_iota(jnp.int32, (n, n), 0)

    def diff_cols(f, west, east):
        right = jnp.where(col == n - 1, east, pltpu.roll(f, n - 1, 1))
        left = jnp.where(col == 0, west, pltpu.roll(f, 1, 1))
        return right - left

    def diff_rows(f, south, north):
        upper = jnp.where(row == n - 1, north, pltpu.roll(f, n - 1, 0))
        lower = jnp.where(row == 0, south, pltpu.roll(f, 1, 0))
        return upper - lower

    turn_ref[...] = jnp.zeros_like(turn_ref)
    for k in range(local):
        half_coef = half_coef_rows(level_ref[k], (1, n))
        wet = wet_ref[k].astype(jnp.float32)
        depth_wet = wet * depth_ref[k]
        height = state_ref[k, 0]
        east_flow = state_ref[k, 1]
        north_flow = state_ref[k, 2]
        for sweep in range(STEPS):
            g = mine_ref[sweep, k]
            turn_ref[0:WIDTH, :] = g
            sides = turn_ref[...].T
            west_fx, west_h = sides[:, 0:1], sides[:, 1:2]
            east_fx, east_h = sides[:, 2:3], sides[:, 3:4]
            flux_x = depth_wet * east_flow
            flux_y = depth_wet * north_flow
            new_height = height + half_coef * (
                diff_cols(flux_x, west_fx, east_fx) + diff_rows(flux_y, g[4:5], g[6:7])
            )
            new_east = wet * (east_flow + half_coef * diff_cols(height, west_h, east_h))
            new_north = wet * (north_flow + half_coef * diff_rows(height, g[5:6], g[7:8]))
            height, east_flow, north_flow = new_height, new_east, new_north
        out_ref[k, 0] = height
        out_ref[k, 1] = east_flow
        out_ref[k, 2] = north_flow


def _vmem():
    return pl.BlockSpec(memory_space=pltpu.VMEM)


def _smem():
    return pl.BlockSpec(memory_space=pltpu.SMEM)


def pack(levels, state, depth, wet_mask):
    local, _, n, _ = state.shape
    return pl.pallas_call(
        pack_kernel,
        out_shape=jax.ShapeDtypeStruct((local, PACK_ROWS, n), jnp.float32),
        in_specs=[_smem()] + [_vmem()] * 3,
        out_specs=_vmem(),
    )(levels, state, depth, wet_mask)


def replay(base, readers, every, green, ids, local):
    group, _, n = every.shape
    rows = group * WIDTH
    return pl.pallas_call(
        replay_kernel,
        out_shape=(
            jax.ShapeDtypeStruct((STEPS, local, WIDTH, n), jnp.float32),
            jax.ShapeDtypeStruct((1, FAULTS), jnp.float32),
        ),
        in_specs=[_smem(), _smem()] + [_vmem()] * 3,
        out_specs=(_vmem(), _vmem()),
        scratch_shapes=[
            pltpu.VMEM((4, rows, rows), jnp.bfloat16),
            pltpu.VMEM((4, 2, rows, n), jnp.float32),
            pltpu.VMEM((rows, n), jnp.float32),
        ],
    )(base, readers, every, green, ids)


def update(levels, mine, state, depth, wet_mask):
    local, _, n, _ = state.shape
    cells = local * n * n
    return pl.pallas_call(
        update_kernel,
        out_shape=jax.ShapeDtypeStruct(state.shape, jnp.float32),
        in_specs=[_smem()] + [_vmem()] * 4,
        out_specs=_vmem(),
        scratch_shapes=[pltpu.VMEM((n, n), jnp.float32)],
        cost_estimate=pl.CostEstimate(
            flops=40 * STEPS * cells, transcendentals=0, bytes_accessed=4 * 8 * cells
        ),
    )(levels, mine, state, depth, wet_mask)


def all_sum(x, axis):
    size = lax.axis_size(axis)
    total = x
    for shift in range(1, size):
        pairs = [(i, (i + shift) % size) for i in range(size)]
        total = total + lax.ppermute(x, axis, pairs)
    return total


def shards(adjoint_init, depth, wet_mask, levels, readers, green, fault_ids):
    state = adjoint_init[0]
    local, _, n, _ = state.shape
    base = (lax.axis_index("patch") * local).astype(jnp.int32).reshape(1)
    packed = pack(levels[0], state, depth[0], wet_mask[0])
    every = lax.all_gather(packed, "patch", axis=0, tiled=True)
    mine, partial_grad = replay(base, readers[0], every, green[0], fault_ids[0].reshape(1, -1), local)
    partial_grad = partial_grad.reshape(-1)
    group_grad = lax.all_gather(partial_grad, "patch", axis=0).sum(axis=0)
    fault_grad = all_sum(group_grad, "grp")
    state = update(levels[0], mine, state, depth[0], wet_mask[0])
    return (state[None], fault_grad)


def solution(mesh):
    placed = (
        P("grp", "patch", None, None, None),
        P("grp", "patch", None, None),
        P("grp", "patch", None, None),
        P("grp", "patch"),
        P("grp", None, None),
        P("grp", "patch", None),
        P("grp", "patch"),
    )
    return jax.shard_map(
        shards,
        mesh=mesh,
        in_specs=placed,
        out_specs=(P("grp", "patch", None, None, None), P()),
        check_vma=False,
    )
```

```python
import jax
import jax.numpy as jnp
from jax import lax
from jax.experimental import pallas as pl
from jax.experimental.pallas import tpu as pltpu
from jax.sharding import PartitionSpec as P

SRC_ROWS = 4
STEPS = 4
FAULTS = 2048
WIDTH = 8
HALF = WIDTH // 2
FIELDS = 4
KINDS = 3
NORTH_TILE = FIELDS
SOUTH_TILE = NORTH_TILE + 2
COEF_TILE = SOUTH_TILE + FIELDS
PACK_ROWS = (COEF_TILE + 1) * WIDTH
HIGH = lax.Precision.HIGHEST


def half_coef_rows(level, shape):
    levels = jnp.full(shape, level, jnp.int32)
    upper = (levels >= 1).astype(jnp.float32) + 2.0 * (levels >= 2).astype(jnp.float32)
    return 0.5 * (0.1 * (1.0 + upper))


def pack_kernel(level_ref, state_ref, depth_ref, wet_ref, out_ref):
    local, _, n, _ = state_ref.shape
    for k in range(local):
        wet = wet_ref[k].astype(jnp.float32)
        fields = (state_ref[k, 0], state_ref[k, 1], state_ref[k, 2], wet * depth_ref[k])
        for f, x in enumerate(fields):
            x_t = x.T
            pair, half = divmod(f, 2)
            at = f * WIDTH
            out_ref[k, at:at + HALF, :] = x_t[0:HALF]
            out_ref[k, at + HALF:at + WIDTH, :] = x_t[n - HALF:n]
            at = (NORTH_TILE + pair) * WIDTH + half * HALF
            out_ref[k, at:at + HALF, :] = x[n - HALF:n]
            at = (SOUTH_TILE + f) * WIDTH
            out_ref[k, at:at + WIDTH, :] = x[0:WIDTH]
        at = COEF_TILE * WIDTH
        out_ref[k, at:at + WIDTH, :] = half_coef_rows(level_ref[k], (WIDTH, n))


def replay_kernel(base_ref, readers_ref, every_ref, green_ref, ids_ref, mine_ref, grad_ref,
                  q_ref, ghost_ref, south_ref):
    group, _, n = every_ref.shape
    local = mine_ref.shape[1]
    rows = group * WIDTH
    base = base_ref[0]

    def tile(index):
        return every_ref[:, index * WIDTH:(index + 1) * WIDTH, :]

    def load(kind, f):
        pair, half = divmod(f, 2)
        if kind == 0:
            block = tile(f)
        elif kind == 1:
            block = tile(SOUTH_TILE + f)
        else:
            block = tile(NORTH_TILE + pair)
            if half == 0:
                block = pltpu.roll(block, HALF, 1)
        return block.reshape(rows, n)

    strips = [[load(kind, f) for f in range(FIELDS)] for kind in range(KINDS)]
    half_all = tile(COEF_TILE).reshape(rows, n)

    lane = lax.broadcasted_iota(jnp.int32, (1, rows), 1)

    def spread(j, lanes):
        return tuple(
            jnp.where(lane == j * WIDTH + (0 if s in (0, 2) else WIDTH - 1), readers_ref[j, s], lanes[s])
            for s in range(4)
        )

    empty = jnp.full((1, rows), -1, jnp.int32)
    lanes = lax.fori_loop(0, group, spread, (empty,) * 4)
    owner = lax.broadcasted_iota(jnp.int32, (rows, rows), 0) // WIDTH
    for t in range(4):
        q_ref[t] = (lanes[t ^ 1] == owner).astype(jnp.bfloat16)

    srow = lax.broadcasted_iota(jnp.int32, (rows, n), 0) & (WIDTH - 1)
    slane = lax.broadcasted_iota(jnp.int32, (rows, n), 1)

    def across_low(f, ghost):
        return pltpu.roll(f, rows - 1, 0) - jnp.where(srow == 0, ghost, pltpu.roll(f, 1, 0))

    def across_high(f, ghost):
        return jnp.where(srow == WIDTH - 1, ghost, pltpu.roll(f, rows - 1, 0)) - pltpu.roll(f, 1, 0)

    def pick(ghost, offset):
        return jnp.sum(jnp.where(slane == srow + offset, ghost, 0.0), axis=1, keepdims=True)

    def along(f, low, high):
        right = jnp.where(slane == n - 1, high, pltpu.roll(f, n - 1, 1))
        left = jnp.where(slane == 0, low, pltpu.roll(f, 1, 1))
        return right - left

    far = jnp.where(srow >= HALF, n - WIDTH, 0)
    for sweep in range(STEPS):
        face_data = []
        for kind in range(KINDS):
            h, e, nf, dw = strips[kind]
            flux = dw * (e if kind == 0 else nf)
            face_data.append((flux, h))
        pieces = []
        for flux, h in face_data:
            rest = jnp.concatenate([flux, h], axis=1)
            parts = []
            for _ in range(3):
                part = rest.astype(jnp.bfloat16)
                rest = rest - part.astype(jnp.float32)
                parts.append(part)
            pieces.append(parts)
        for t in range(4):
            parts = pieces[(0, 0, 1, 2)[t ^ 1]]
            total = None
            for part in parts:
                term = jnp.dot(q_ref[t], part, preferred_element_type=jnp.float32)
                total = term if total is None else total + term
            ghost_ref[t, 0] = total[:, 0:n]
            ghost_ref[t, 1] = total[:, n:2 * n]
        for k in range(local):
            at = (base + k) * WIDTH
            for t in range(4):
                for c in range(2):
                    mine_ref[sweep, k, 2 * t + c:2 * t + c + 1, :] = ghost_ref[t, c, pl.ds(at, 1), :]

        gw = [ghost_ref[0, c] for c in range(2)]
        ge = [ghost_ref[1, c] for c in range(2)]
        gs = [ghost_ref[2, c] for c in range(2)]
        gn = [ghost_ref[3, c] for c in range(2)]
        advanced = []
        for kind in range(KINDS):
            h, e, nf, dw = strips[kind]
            if sweep == STEPS - 1 and kind != 1:
                advanced.append(strips[kind])
                continue
            wet = jnp.where(dw > 0.0, 1.0, 0.0)
            fx = dw * e
            fy = dw * nf
            if kind == 0:
                def across(f, west, east):
                    upper = jnp.where(srow == WIDTH - 1, east, pltpu.roll(f, rows - 1, 0))
                    lower = jnp.where(srow == 0, west, pltpu.roll(f, 1, 0))
                    return upper - lower
                d_fx = across(fx, gw[0], ge[0])
                d_hx = across(h, gw[1], ge[1])
                d_fy = along(fy, pick(gs[0], far), pick(gn[0], far))
                d_hy = along(h, pick(gs[1], far), pick(gn[1], far))
            else:
                offset = 0 if kind == 1 else n - WIDTH
                across = across_low if kind == 1 else across_high
                ghost = gs if kind == 1 else gn
                d_fy = across(fy, ghost[0])
                d_hy = across(h, ghost[1])
                d_fx = along(fx, pick(gw[0], offset), pick(ge[0], offset))
                d_hx = along(h, pick(gw[1], offset), pick(ge[1], offset))
            new_h = h + half_all * (d_fx + d_fy)
            new_e = wet * (e + half_all * d_hx)
            new_n = wet * (nf + half_all * d_hy)
            advanced.append((new_h, new_e, new_n, dw))
        strips = advanced

    south_ref[...] = strips[1][0]

    subfaults = green_ref.shape[0]

    def project(r, acc):
        j, i = r // SRC_ROWS, r % SRC_ROWS
        block = green_ref[:, pl.ds(pl.multiple_of(r * n, n), n)].astype(jnp.float32)
        shown = south_ref[pl.ds(j * WIDTH + i, 1), :].astype(jnp.bfloat16).astype(jnp.float32)
        return acc + block * shown

    acc = lax.fori_loop(0, group * SRC_ROWS, project, jnp.zeros((subfaults, n), jnp.float32), unroll=8)
    slip = jnp.sum(acc, axis=1, keepdims=True)
    ghost_ref[0, 0] = jnp.zeros((rows, n), jnp.float32)
    ghost_ref[0, 0, 0:1, 0:subfaults] = ids_ref[...].astype(jnp.float32)
    ids = ghost_ref[0, 0, 0:n, :].T[0:subfaults, 0:1]
    faults = grad_ref.shape[1]
    which = lax.broadcasted_iota(jnp.int32, (subfaults, faults), 1).astype(jnp.float32)
    grad_ref[...] = jnp.sum(jnp.where(which == ids, slip, 0.0), axis=0, keepdims=True)


def update_kernel(level_ref, mine_ref, state_ref, depth_ref, wet_ref, out_ref, turn_ref):
    local, _, n, _ = state_ref.shape
    col = lax.broadcasted_iota(jnp.int32, (n, n), 1)
    row = lax.broadcasted_iota(jnp.int32, (n, n), 0)

    def diff_cols(f, west, east):
        right = jnp.where(col == n - 1, east, pltpu.roll(f, n - 1, 1))
        left = jnp.where(col == 0, west, pltpu.roll(f, 1, 1))
        return right - left

    def diff_rows(f, south, north):
        upper = jnp.where(row == n - 1, north, pltpu.roll(f, n - 1, 0))
        lower = jnp.where(row == 0, south, pltpu.roll(f, 1, 0))
        return upper - lower

    turn_ref[...] = jnp.zeros_like(turn_ref)
    for k in range(local):
        half_coef = half_coef_rows(level_ref[k], (1, n))
        wet = wet_ref[k].astype(jnp.float32)
        depth_wet = wet * depth_ref[k]
        height = state_ref[k, 0]
        east_flow = state_ref[k, 1]
        north_flow = state_ref[k, 2]
        for sweep in range(STEPS):
            g = mine_ref[sweep, k]
            turn_ref[0:WIDTH, :] = g
            sides = turn_ref[...].T
            west_fx, west_h = sides[:, 0:1], sides[:, 1:2]
            east_fx, east_h = sides[:, 2:3], sides[:, 3:4]
            flux_x = depth_wet * east_flow
            flux_y = depth_wet * north_flow
            new_height = height + half_coef * (
                diff_cols(flux_x, west_fx, east_fx) + diff_rows(flux_y, g[4:5], g[6:7])
            )
            new_east = wet * (east_flow + half_coef * diff_cols(height, west_h, east_h))
            new_north = wet * (north_flow + half_coef * diff_rows(height, g[5:6], g[7:8]))
            height, east_flow, north_flow = new_height, new_east, new_north
        out_ref[k, 0] = height
        out_ref[k, 1] = east_flow
        out_ref[k, 2] = north_flow


def _vmem():
    return pl.BlockSpec(memory_space=pltpu.VMEM)


def _smem():
    return pl.BlockSpec(memory_space=pltpu.SMEM)


def pack(levels, state, depth, wet_mask):
    local, _, n, _ = state.shape
    return pl.pallas_call(
        pack_kernel,
        out_shape=jax.ShapeDtypeStruct((local, PACK_ROWS, n), jnp.float32),
        in_specs=[_smem()] + [_vmem()] * 3,
        out_specs=_vmem(),
    )(levels, state, depth, wet_mask)


def replay(base, readers, every, green, ids, local):
    group, _, n = every.shape
    rows = group * WIDTH
    return pl.pallas_call(
        replay_kernel,
        out_shape=(
            jax.ShapeDtypeStruct((STEPS, local, WIDTH, n), jnp.float32),
            jax.ShapeDtypeStruct((1, FAULTS), jnp.float32),
        ),
        in_specs=[_smem(), _smem()] + [_vmem()] * 3,
        out_specs=(_vmem(), _vmem()),
        scratch_shapes=[
            pltpu.VMEM((4, rows, rows), jnp.bfloat16),
            pltpu.VMEM((4, 2, rows, n), jnp.float32),
            pltpu.VMEM((rows, n), jnp.float32),
        ],
    )(base, readers, every, green, ids)


def update(levels, mine, state, depth, wet_mask):
    local, _, n, _ = state.shape
    cells = local * n * n
    return pl.pallas_call(
        update_kernel,
        out_shape=jax.ShapeDtypeStruct(state.shape, jnp.float32),
        in_specs=[_smem()] + [_vmem()] * 4,
        out_specs=_vmem(),
        scratch_shapes=[pltpu.VMEM((n, n), jnp.float32)],
        cost_estimate=pl.CostEstimate(
            flops=40 * STEPS * cells, transcendentals=0, bytes_accessed=4 * 8 * cells
        ),
    )(levels, mine, state, depth, wet_mask)


def all_sum(x, axis):
    size = lax.axis_size(axis)
    total = x
    for shift in range(1, size):
        if size & (size - 1) == 0:
            pairs = [(i, i ^ shift) for i in range(size)]
        else:
            pairs = [(i, (i + shift) % size) for i in range(size)]
        total = total + lax.ppermute(x, axis, pairs)
    return total


def shards(adjoint_init, depth, wet_mask, levels, readers, green, fault_ids):
    state = adjoint_init[0]
    local, _, n, _ = state.shape
    base = (lax.axis_index("patch") * local).astype(jnp.int32).reshape(1)
    packed = pack(levels[0], state, depth[0], wet_mask[0])
    every = lax.all_gather(packed, "patch", axis=0, tiled=True)
    mine, partial_grad = replay(base, readers[0], every, green[0], fault_ids[0].reshape(1, -1), local)
    partial_grad = partial_grad.reshape(-1)
    group_grad = lax.all_gather(partial_grad, "patch", axis=0).sum(axis=0)
    fault_grad = all_sum(group_grad, "grp")
    state = update(levels[0], mine, state, depth[0], wet_mask[0])
    return (state[None], fault_grad)


def solution(mesh):
    placed = (
        P("grp", "patch", None, None, None),
        P("grp", "patch", None, None),
        P("grp", "patch", None, None),
        P("grp", "patch"),
        P("grp", None, None),
        P("grp", "patch", None),
        P("grp", "patch"),
    )
    return jax.shard_map(
        shards,
        mesh=mesh,
        in_specs=placed,
        out_specs=(P("grp", "patch", None, None, None), P()),
        check_vma=False,
    )
```

```python
import jax
import jax.numpy as jnp
from jax import lax
from jax.experimental import pallas as pl
from jax.experimental.pallas import tpu as pltpu
from jax.sharding import PartitionSpec as P

SRC_ROWS = 4
STEPS = 4
FAULTS = 2048
WIDTH = 8
HALF = WIDTH // 2
FIELDS = 4
KINDS = 3
NORTH_TILE = FIELDS
SOUTH_TILE = NORTH_TILE + 2
COEF_TILE = SOUTH_TILE + FIELDS
PACK_ROWS = (COEF_TILE + 1) * WIDTH
HIGH = lax.Precision.HIGHEST


def half_coef_rows(level, shape):
    levels = jnp.full(shape, level, jnp.int32)
    upper = (levels >= 1).astype(jnp.float32) + 2.0 * (levels >= 2).astype(jnp.float32)
    return 0.5 * (0.1 * (1.0 + upper))


def pack_kernel(level_ref, state_ref, depth_ref, wet_ref, out_ref):
    local, _, n, _ = state_ref.shape
    for k in range(local):
        wet = wet_ref[k].astype(jnp.float32)
        fields = (state_ref[k, 0], state_ref[k, 1], state_ref[k, 2], wet * depth_ref[k])
        for f, x in enumerate(fields):
            x_t = x.T
            pair, half = divmod(f, 2)
            at = f * WIDTH
            out_ref[k, at:at + HALF, :] = x_t[0:HALF]
            out_ref[k, at + HALF:at + WIDTH, :] = x_t[n - HALF:n]
            at = (NORTH_TILE + pair) * WIDTH + half * HALF
            out_ref[k, at:at + HALF, :] = x[n - HALF:n]
            at = (SOUTH_TILE + f) * WIDTH
            out_ref[k, at:at + WIDTH, :] = x[0:WIDTH]
        at = COEF_TILE * WIDTH
        out_ref[k, at:at + WIDTH, :] = half_coef_rows(level_ref[k], (WIDTH, n))


def replay_kernel(base_ref, readers_ref, every_ref, green_ref, ids_ref, mine_ref, grad_ref,
                  q_ref, ghost_ref, south_ref, flat_ref):
    group, _, n = every_ref.shape
    local = mine_ref.shape[1]
    rows = group * WIDTH
    base = base_ref[0]

    def tile(index):
        return every_ref[:, index * WIDTH:(index + 1) * WIDTH, :]

    def load(kind, f):
        pair, half = divmod(f, 2)
        if kind == 0:
            block = tile(f)
        elif kind == 1:
            block = tile(SOUTH_TILE + f)
        else:
            block = tile(NORTH_TILE + pair)
            if half == 0:
                block = pltpu.roll(block, HALF, 1)
        return block.reshape(rows, n)

    strips = [[load(kind, f) for f in range(FIELDS)] for kind in range(KINDS)]
    half_all = tile(COEF_TILE).reshape(rows, n)

    lane = lax.broadcasted_iota(jnp.int32, (1, rows), 1)

    def spread(j, lanes):
        return tuple(
            jnp.where(lane == j * WIDTH + (0 if s in (0, 2) else WIDTH - 1), readers_ref[j, s], lanes[s])
            for s in range(4)
        )

    empty = jnp.full((1, rows), -1, jnp.int32)
    lanes = lax.fori_loop(0, group, spread, (empty,) * 4)
    owner = lax.broadcasted_iota(jnp.int32, (rows, rows), 0) // WIDTH
    for t in range(4):
        q_ref[t] = (lanes[t ^ 1] == owner).astype(jnp.bfloat16)

    srow = lax.broadcasted_iota(jnp.int32, (rows, n), 0) & (WIDTH - 1)
    slane = lax.broadcasted_iota(jnp.int32, (rows, n), 1)

    def across_low(f, ghost):
        return pltpu.roll(f, rows - 1, 0) - jnp.where(srow == 0, ghost, pltpu.roll(f, 1, 0))

    def across_high(f, ghost):
        return jnp.where(srow == WIDTH - 1, ghost, pltpu.roll(f, rows - 1, 0)) - pltpu.roll(f, 1, 0)

    def pick(ghost, offset):
        return jnp.sum(jnp.where(slane == srow + offset, ghost, 0.0), axis=1, keepdims=True)

    def along(f, low, high):
        right = jnp.where(slane == n - 1, high, pltpu.roll(f, n - 1, 1))
        left = jnp.where(slane == 0, low, pltpu.roll(f, 1, 1))
        return right - left

    far = jnp.where(srow >= HALF, n - WIDTH, 0)
    for sweep in range(STEPS):
        face_data = []
        for kind in range(KINDS):
            h, e, nf, dw = strips[kind]
            flux = dw * (e if kind == 0 else nf)
            face_data.append((flux, h))
        pieces = []
        for flux, h in face_data:
            rest = jnp.concatenate([flux, h], axis=1)
            parts = []
            for _ in range(3):
                part = rest.astype(jnp.bfloat16)
                rest = rest - part.astype(jnp.float32)
                parts.append(part)
            pieces.append(parts)
        for t in range(4):
            parts = pieces[(0, 0, 1, 2)[t ^ 1]]
            total = None
            for part in parts:
                term = jnp.dot(q_ref[t], part, preferred_element_type=jnp.float32)
                total = term if total is None else total + term
            ghost_ref[t, 0] = total[:, 0:n]
            ghost_ref[t, 1] = total[:, n:2 * n]
        for k in range(local):
            at = (base + k) * WIDTH
            for t in range(4):
                for c in range(2):
                    mine_ref[sweep, k, 2 * t + c:2 * t + c + 1, :] = ghost_ref[t, c, pl.ds(at, 1), :]

        gw = [ghost_ref[0, c] for c in range(2)]
        ge = [ghost_ref[1, c] for c in range(2)]
        gs = [ghost_ref[2, c] for c in range(2)]
        gn = [ghost_ref[3, c] for c in range(2)]
        advanced = []
        for kind in range(KINDS):
            h, e, nf, dw = strips[kind]
            if sweep == STEPS - 1 and kind != 1:
                advanced.append(strips[kind])
                continue
            wet = jnp.where(dw > 0.0, 1.0, 0.0)
            fx = dw * e
            fy = dw * nf
            if kind == 0:
                def across(f, west, east):
                    upper = jnp.where(srow == WIDTH - 1, east, pltpu.roll(f, rows - 1, 0))
                    lower = jnp.where(srow == 0, west, pltpu.roll(f, 1, 0))
                    return upper - lower
                d_fx = across(fx, gw[0], ge[0])
                d_hx = across(h, gw[1], ge[1])
                d_fy = along(fy, pick(gs[0], far), pick(gn[0], far))
                d_hy = along(h, pick(gs[1], far), pick(gn[1], far))
            else:
                offset = 0 if kind == 1 else n - WIDTH
                across = across_low if kind == 1 else across_high
                ghost = gs if kind == 1 else gn
                d_fy = across(fy, ghost[0])
                d_hy = across(h, ghost[1])
                d_fx = along(fx, pick(gw[0], offset), pick(ge[0], offset))
                d_hx = along(h, pick(gw[1], offset), pick(ge[1], offset))
            new_h = h + half_all * (d_fx + d_fy)
            new_e = wet * (e + half_all * d_hx)
            new_n = wet * (nf + half_all * d_hy)
            advanced.append((new_h, new_e, new_n, dw))
        strips = advanced

    south_ref[...] = strips[1][0]

    subfaults = green_ref.shape[0]
    flat_ref[...] = jnp.zeros_like(flat_ref)

    def flatten(r, carry):
        j, i = r // SRC_ROWS, r % SRC_ROWS
        flat_ref[0:1, pl.ds(pl.multiple_of(r * n, n), n)] = south_ref[pl.ds(j * WIDTH + i, 1), :]
        return carry

    lax.fori_loop(0, group * SRC_ROWS, flatten, 0)
    contract_last = (((1,), (1,)), ((), ()))
    slip = lax.dot_general(
        flat_ref[...].astype(jnp.bfloat16), green_ref[...], contract_last,
        preferred_element_type=jnp.float32,
    )
    faults = grad_ref.shape[1]
    which = lax.broadcasted_iota(jnp.int32, (faults, subfaults), 0)
    chosen = (which == ids_ref[...]).astype(jnp.bfloat16)
    rest = slip
    total = None
    for _ in range(3):
        part = rest.astype(jnp.bfloat16)
        rest = rest - part.astype(jnp.float32)
        term = lax.dot_general(part, chosen, contract_last, preferred_element_type=jnp.float32)
        total = term if total is None else total + term
    grad_ref[...] = total[0:1, :]


def update_kernel(level_ref, mine_ref, state_ref, depth_ref, wet_ref, out_ref, turn_ref):
    local, _, n, _ = state_ref.shape
    col = lax.broadcasted_iota(jnp.int32, (n, n), 1)
    row = lax.broadcasted_iota(jnp.int32, (n, n), 0)

    def diff_cols(f, west, east):
        right = jnp.where(col == n - 1, east, pltpu.roll(f, n - 1, 1))
        left = jnp.where(col == 0, west, pltpu.roll(f, 1, 1))
        return right - left

    def diff_rows(f, south, north):
        upper = jnp.where(row == n - 1, north, pltpu.roll(f, n - 1, 0))
        lower = jnp.where(row == 0, south, pltpu.roll(f, 1, 0))
        return upper - lower

    turn_ref[...] = jnp.zeros_like(turn_ref)
    for k in range(local):
        half_coef = half_coef_rows(level_ref[k], (1, n))
        wet = wet_ref[k].astype(jnp.float32)
        depth_wet = wet * depth_ref[k]
        height = state_ref[k, 0]
        east_flow = state_ref[k, 1]
        north_flow = state_ref[k, 2]
        for sweep in range(STEPS):
            g = mine_ref[sweep, k]
            turn_ref[0:WIDTH, :] = g
            sides = turn_ref[...].T
            west_fx, west_h = sides[:, 0:1], sides[:, 1:2]
            east_fx, east_h = sides[:, 2:3], sides[:, 3:4]
            flux_x = depth_wet * east_flow
            flux_y = depth_wet * north_flow
            new_height = height + half_coef * (
                diff_cols(flux_x, west_fx, east_fx) + diff_rows(flux_y, g[4:5], g[6:7])
            )
            new_east = wet * (east_flow + half_coef * diff_cols(height, west_h, east_h))
            new_north = wet * (north_flow + half_coef * diff_rows(height, g[5:6], g[7:8]))
            height, east_flow, north_flow = new_height, new_east, new_north
        out_ref[k, 0] = height
        out_ref[k, 1] = east_flow
        out_ref[k, 2] = north_flow


def _vmem():
    return pl.BlockSpec(memory_space=pltpu.VMEM)


def _smem():
    return pl.BlockSpec(memory_space=pltpu.SMEM)


def pack(levels, state, depth, wet_mask):
    local, _, n, _ = state.shape
    return pl.pallas_call(
        pack_kernel,
        out_shape=jax.ShapeDtypeStruct((local, PACK_ROWS, n), jnp.float32),
        in_specs=[_smem()] + [_vmem()] * 3,
        out_specs=_vmem(),
    )(levels, state, depth, wet_mask)


def replay(base, readers, every, green, ids, local):
    group, _, n = every.shape
    rows = group * WIDTH
    return pl.pallas_call(
        replay_kernel,
        out_shape=(
            jax.ShapeDtypeStruct((STEPS, local, WIDTH, n), jnp.float32),
            jax.ShapeDtypeStruct((1, FAULTS), jnp.float32),
        ),
        in_specs=[_smem(), _smem()] + [_vmem()] * 3,
        out_specs=(_vmem(), _vmem()),
        scratch_shapes=[
            pltpu.VMEM((4, rows, rows), jnp.bfloat16),
            pltpu.VMEM((4, 2, rows, n), jnp.float32),
            pltpu.VMEM((rows, n), jnp.float32),
            pltpu.VMEM((WIDTH, green.shape[1]), jnp.float32),
        ],
    )(base, readers, every, green, ids)


def update(levels, mine, state, depth, wet_mask):
    local, _, n, _ = state.shape
    cells = local * n * n
    return pl.pallas_call(
        update_kernel,
        out_shape=jax.ShapeDtypeStruct(state.shape, jnp.float32),
        in_specs=[_smem()] + [_vmem()] * 4,
        out_specs=_vmem(),
        scratch_shapes=[pltpu.VMEM((n, n), jnp.float32)],
        cost_estimate=pl.CostEstimate(
            flops=40 * STEPS * cells, transcendentals=0, bytes_accessed=4 * 8 * cells
        ),
    )(levels, mine, state, depth, wet_mask)


def all_sum(x, axis):
    size = lax.axis_size(axis)
    total = x
    for shift in range(1, size):
        if size & (size - 1) == 0:
            pairs = [(i, i ^ shift) for i in range(size)]
        else:
            pairs = [(i, (i + shift) % size) for i in range(size)]
        total = total + lax.ppermute(x, axis, pairs)
    return total


def shards(adjoint_init, depth, wet_mask, levels, readers, green, fault_ids):
    state = adjoint_init[0]
    local, _, n, _ = state.shape
    base = (lax.axis_index("patch") * local).astype(jnp.int32).reshape(1)
    packed = pack(levels[0], state, depth[0], wet_mask[0])
    every = lax.all_gather(packed, "patch", axis=0, tiled=True)
    mine, partial_grad = replay(base, readers[0], every, green[0], fault_ids[0].reshape(1, -1), local)
    partial_grad = partial_grad.reshape(-1)
    group_grad = lax.all_gather(partial_grad, "patch", axis=0).sum(axis=0)
    fault_grad = all_sum(group_grad, "grp")
    state = update(levels[0], mine, state, depth[0], wet_mask[0])
    return (state[None], fault_grad)


def solution(mesh):
    placed = (
        P("grp", "patch", None, None, None),
        P("grp", "patch", None, None),
        P("grp", "patch", None, None),
        P("grp", "patch"),
        P("grp", None, None),
        P("grp", "patch", None),
        P("grp", "patch"),
    )
    return jax.shard_map(
        shards,
        mesh=mesh,
        in_specs=placed,
        out_specs=(P("grp", "patch", None, None, None), P()),
        check_vma=False,
    )
```

```python
import jax
import jax.numpy as jnp
from jax import lax
from jax.experimental import pallas as pl
from jax.experimental.pallas import tpu as pltpu
from jax.sharding import PartitionSpec as P

SRC_ROWS = 4
STEPS = 4
FAULTS = 2048
WIDTH = 8
HALF = WIDTH // 2
FIELDS = 4
KINDS = 3
NORTH_TILE = FIELDS
SOUTH_TILE = NORTH_TILE + 2
COEF_TILE = SOUTH_TILE + FIELDS
PACK_ROWS = COEF_TILE * WIDTH
HIGH = lax.Precision.HIGHEST


def half_coef_rows(level, shape):
    levels = jnp.full(shape, level, jnp.int32)
    upper = (levels >= 1).astype(jnp.float32) + 2.0 * (levels >= 2).astype(jnp.float32)
    return 0.5 * (0.1 * (1.0 + upper))


def pack_kernel(level_ref, state_ref, depth_ref, wet_ref, out_ref):
    local, _, n, _ = state_ref.shape
    for k in range(local):
        wet = wet_ref[k].astype(jnp.float32)
        fields = (state_ref[k, 0], state_ref[k, 1], state_ref[k, 2], wet * depth_ref[k])
        for f, x in enumerate(fields):
            x_t = x.T
            pair, half = divmod(f, 2)
            at = f * WIDTH
            out_ref[k, at:at + HALF, :] = x_t[0:HALF]
            out_ref[k, at + HALF:at + WIDTH, :] = x_t[n - HALF:n]
            at = (NORTH_TILE + pair) * WIDTH + half * HALF
            out_ref[k, at:at + HALF, :] = x[n - HALF:n]
            at = (SOUTH_TILE + f) * WIDTH
            out_ref[k, at:at + WIDTH, :] = x[0:WIDTH]
        at = COEF_TILE * WIDTH
        out_ref[k, at - 1:at, :] = half_coef_rows(level_ref[k], (1, n))


def replay_kernel(base_ref, readers_ref, every_ref, green_ref, ids_ref, mine_ref, grad_ref,
                  q_ref, ghost_ref, south_ref):
    group, _, n = every_ref.shape
    local = mine_ref.shape[1]
    rows = group * WIDTH
    base = base_ref[0]

    def tile(index):
        return every_ref[:, index * WIDTH:(index + 1) * WIDTH, :]

    def load(kind, f):
        pair, half = divmod(f, 2)
        if kind == 0:
            block = tile(f)
        elif kind == 1:
            block = tile(SOUTH_TILE + f)
        else:
            block = tile(NORTH_TILE + pair)
            if half == 0:
                block = pltpu.roll(block, HALF, 1)
        return block.reshape(rows, n)

    strips = [[load(kind, f) for f in range(FIELDS)] for kind in range(KINDS)]
    coef_row = every_ref[:, COEF_TILE * WIDTH - 1:COEF_TILE * WIDTH, :]
    half_all = jnp.broadcast_to(coef_row, (group, WIDTH, n)).reshape(rows, n)

    lane = lax.broadcasted_iota(jnp.int32, (1, rows), 1)

    def spread(j, lanes):
        return tuple(
            jnp.where(lane == j * WIDTH + (0 if s in (0, 2) else WIDTH - 1), readers_ref[j, s], lanes[s])
            for s in range(4)
        )

    empty = jnp.full((1, rows), -1, jnp.int32)
    lanes = lax.fori_loop(0, group, spread, (empty,) * 4)
    owner = lax.broadcasted_iota(jnp.int32, (rows, rows), 0) // WIDTH
    for t in range(4):
        q_ref[t] = (lanes[t ^ 1] == owner).astype(jnp.bfloat16)

    srow = lax.broadcasted_iota(jnp.int32, (rows, n), 0) & (WIDTH - 1)
    slane = lax.broadcasted_iota(jnp.int32, (rows, n), 1)

    def across_low(f, ghost):
        return pltpu.roll(f, rows - 1, 0) - jnp.where(srow == 0, ghost, pltpu.roll(f, 1, 0))

    def across_high(f, ghost):
        return jnp.where(srow == WIDTH - 1, ghost, pltpu.roll(f, rows - 1, 0)) - pltpu.roll(f, 1, 0)

    def pick(ghost, offset):
        return jnp.sum(jnp.where(slane == srow + offset, ghost, 0.0), axis=1, keepdims=True)

    def along(f, low, high):
        right = jnp.where(slane == n - 1, high, pltpu.roll(f, n - 1, 1))
        left = jnp.where(slane == 0, low, pltpu.roll(f, 1, 1))
        return right - left

    far = jnp.where(srow >= HALF, n - WIDTH, 0)
    for sweep in range(STEPS):
        face_data = []
        for kind in range(KINDS):
            h, e, nf, dw = strips[kind]
            flux = dw * (e if kind == 0 else nf)
            face_data.append((flux, h))
        pieces = []
        for flux, h in face_data:
            rest = jnp.concatenate([flux, h], axis=1)
            parts = []
            for _ in range(3):
                part = rest.astype(jnp.bfloat16)
                rest = rest - part.astype(jnp.float32)
                parts.append(part)
            pieces.append(parts)
        for t in range(4):
            parts = pieces[(0, 0, 1, 2)[t ^ 1]]
            total = None
            for part in parts:
                term = jnp.dot(q_ref[t], part, preferred_element_type=jnp.float32)
                total = term if total is None else total + term
            ghost_ref[t, 0] = total[:, 0:n]
            ghost_ref[t, 1] = total[:, n:2 * n]
        for k in range(local):
            at = (base + k) * WIDTH
            for t in range(4):
                for c in range(2):
                    mine_ref[sweep, k, 2 * t + c:2 * t + c + 1, :] = ghost_ref[t, c, pl.ds(at, 1), :]

        gw = [ghost_ref[0, c] for c in range(2)]
        ge = [ghost_ref[1, c] for c in range(2)]
        gs = [ghost_ref[2, c] for c in range(2)]
        gn = [ghost_ref[3, c] for c in range(2)]
        advanced = []
        for kind in range(KINDS):
            h, e, nf, dw = strips[kind]
            if sweep == STEPS - 1 and kind != 1:
                advanced.append(strips[kind])
                continue
            wet = jnp.where(dw > 0.0, 1.0, 0.0)
            fx = dw * e
            fy = dw * nf
            if kind == 0:
                def across(f, west, east):
                    upper = jnp.where(srow == WIDTH - 1, east, pltpu.roll(f, rows - 1, 0))
                    lower = jnp.where(srow == 0, west, pltpu.roll(f, 1, 0))
                    return upper - lower
                d_fx = across(fx, gw[0], ge[0])
                d_hx = across(h, gw[1], ge[1])
                d_fy = along(fy, pick(gs[0], far), pick(gn[0], far))
                d_hy = along(h, pick(gs[1], far), pick(gn[1], far))
            else:
                offset = 0 if kind == 1 else n - WIDTH
                across = across_low if kind == 1 else across_high
                ghost = gs if kind == 1 else gn
                d_fy = across(fy, ghost[0])
                d_hy = across(h, ghost[1])
                d_fx = along(fx, pick(gw[0], offset), pick(ge[0], offset))
                d_hx = along(h, pick(gw[1], offset), pick(ge[1], offset))
            new_h = h + half_all * (d_fx + d_fy)
            new_e = wet * (e + half_all * d_hx)
            new_n = wet * (nf + half_all * d_hy)
            advanced.append((new_h, new_e, new_n, dw))
        strips = advanced

    south_ref[...] = strips[1][0]

    subfaults = green_ref.shape[0]

    def project(r, acc):
        j, i = r // SRC_ROWS, r % SRC_ROWS
        block = green_ref[:, pl.ds(pl.multiple_of(r * n, n), n)].astype(jnp.float32)
        shown = south_ref[pl.ds(j * WIDTH + i, 1), :].astype(jnp.bfloat16).astype(jnp.float32)
        return acc + block * shown

    acc = lax.fori_loop(0, group * SRC_ROWS, project, jnp.zeros((subfaults, n), jnp.float32), unroll=8)
    slip = jnp.sum(acc, axis=1, keepdims=True)
    ghost_ref[0, 0] = jnp.zeros((rows, n), jnp.float32)
    ghost_ref[0, 0, 0:1, 0:subfaults] = ids_ref[...].astype(jnp.float32)
    ids = ghost_ref[0, 0, 0:n, :].T[0:subfaults, 0:1]
    faults = grad_ref.shape[1]
    which = lax.broadcasted_iota(jnp.int32, (subfaults, faults), 1).astype(jnp.float32)
    grad_ref[...] = jnp.sum(jnp.where(which == ids, slip, 0.0), axis=0, keepdims=True)


def update_kernel(level_ref, mine_ref, state_ref, depth_ref, wet_ref, out_ref, turn_ref):
    local, _, n, _ = state_ref.shape
    col = lax.broadcasted_iota(jnp.int32, (n, n), 1)
    row = lax.broadcasted_iota(jnp.int32, (n, n), 0)

    def diff_cols(f, west, east):
        right = jnp.where(col == n - 1, east, pltpu.roll(f, n - 1, 1))
        left = jnp.where(col == 0, west, pltpu.roll(f, 1, 1))
        return right - left

    def diff_rows(f, south, north):
        upper = jnp.where(row == n - 1, north, pltpu.roll(f, n - 1, 0))
        lower = jnp.where(row == 0, south, pltpu.roll(f, 1, 0))
        return upper - lower

    turn_ref[...] = jnp.zeros_like(turn_ref)
    for k in range(local):
        half_coef = half_coef_rows(level_ref[k], (1, n))
        wet = wet_ref[k].astype(jnp.float32)
        depth_wet = wet * depth_ref[k]
        height = state_ref[k, 0]
        east_flow = state_ref[k, 1]
        north_flow = state_ref[k, 2]
        for sweep in range(STEPS):
            g = mine_ref[sweep, k]
            turn_ref[0:WIDTH, :] = g
            sides = turn_ref[...].T
            west_fx, west_h = sides[:, 0:1], sides[:, 1:2]
            east_fx, east_h = sides[:, 2:3], sides[:, 3:4]
            flux_x = depth_wet * east_flow
            flux_y = depth_wet * north_flow
            new_height = height + half_coef * (
                diff_cols(flux_x, west_fx, east_fx) + diff_rows(flux_y, g[4:5], g[6:7])
            )
            new_east = wet * (east_flow + half_coef * diff_cols(height, west_h, east_h))
            new_north = wet * (north_flow + half_coef * diff_rows(height, g[5:6], g[7:8]))
            height, east_flow, north_flow = new_height, new_east, new_north
        out_ref[k, 0] = height
        out_ref[k, 1] = east_flow
        out_ref[k, 2] = north_flow


def _vmem():
    return pl.BlockSpec(memory_space=pltpu.VMEM)


def _smem():
    return pl.BlockSpec(memory_space=pltpu.SMEM)


def pack(levels, state, depth, wet_mask):
    local, _, n, _ = state.shape
    return pl.pallas_call(
        pack_kernel,
        out_shape=jax.ShapeDtypeStruct((local, PACK_ROWS, n), jnp.float32),
        in_specs=[_smem()] + [_vmem()] * 3,
        out_specs=_vmem(),
    )(levels, state, depth, wet_mask)


def replay(base, readers, every, green, ids, local):
    group, _, n = every.shape
    rows = group * WIDTH
    return pl.pallas_call(
        replay_kernel,
        out_shape=(
            jax.ShapeDtypeStruct((STEPS, local, WIDTH, n), jnp.float32),
            jax.ShapeDtypeStruct((1, FAULTS), jnp.float32),
        ),
        in_specs=[_smem(), _smem()] + [_vmem()] * 3,
        out_specs=(_vmem(), _vmem()),
        scratch_shapes=[
            pltpu.VMEM((4, rows, rows), jnp.bfloat16),
            pltpu.VMEM((4, 2, rows, n), jnp.float32),
            pltpu.VMEM((rows, n), jnp.float32),
        ],
    )(base, readers, every, green, ids)


def update(levels, mine, state, depth, wet_mask):
    local, _, n, _ = state.shape
    cells = local * n * n
    return pl.pallas_call(
        update_kernel,
        out_shape=jax.ShapeDtypeStruct(state.shape, jnp.float32),
        in_specs=[_smem()] + [_vmem()] * 4,
        out_specs=_vmem(),
        scratch_shapes=[pltpu.VMEM((n, n), jnp.float32)],
        cost_estimate=pl.CostEstimate(
            flops=40 * STEPS * cells, transcendentals=0, bytes_accessed=4 * 8 * cells
        ),
    )(levels, mine, state, depth, wet_mask)


def all_sum(x, axis):
    size = lax.axis_size(axis)
    total = x
    for shift in range(1, size):
        if size & (size - 1) == 0:
            pairs = [(i, i ^ shift) for i in range(size)]
        else:
            pairs = [(i, (i + shift) % size) for i in range(size)]
        total = total + lax.ppermute(x, axis, pairs)
    return total


def shards(adjoint_init, depth, wet_mask, levels, readers, green, fault_ids):
    state = adjoint_init[0]
    local, _, n, _ = state.shape
    base = (lax.axis_index("patch") * local).astype(jnp.int32).reshape(1)
    packed = pack(levels[0], state, depth[0], wet_mask[0])
    every = lax.all_gather(packed, "patch", axis=0, tiled=True)
    mine, partial_grad = replay(base, readers[0], every, green[0], fault_ids[0].reshape(1, -1), local)
    partial_grad = partial_grad.reshape(-1)
    group_grad = lax.all_gather(partial_grad, "patch", axis=0).sum(axis=0)
    fault_grad = all_sum(group_grad, "grp")
    state = update(levels[0], mine, state, depth[0], wet_mask[0])
    return (state[None], fault_grad)


def solution(mesh):
    placed = (
        P("grp", "patch", None, None, None),
        P("grp", "patch", None, None),
        P("grp", "patch", None, None),
        P("grp", "patch"),
        P("grp", None, None),
        P("grp", "patch", None),
        P("grp", "patch"),
    )
    return jax.shard_map(
        shards,
        mesh=mesh,
        in_specs=placed,
        out_specs=(P("grp", "patch", None, None, None), P()),
        check_vma=False,
    )
```

```python
import jax
import jax.numpy as jnp
from jax import lax
from jax.experimental import pallas as pl
from jax.experimental.pallas import tpu as pltpu
from jax.sharding import PartitionSpec as P

SRC_ROWS = 4
STEPS = 4
FAULTS = 2048
WIDTH = 8
HALF = WIDTH // 2
FIELDS = 4
KINDS = 3
NORTH_TILE = FIELDS
SOUTH_TILE = NORTH_TILE + 2
COEF_TILE = SOUTH_TILE + FIELDS
PACK_ROWS = COEF_TILE * WIDTH
HIGH = lax.Precision.HIGHEST


def half_coef_rows(level, shape):
    levels = jnp.full(shape, level, jnp.int32)
    upper = (levels >= 1).astype(jnp.float32) + 2.0 * (levels >= 2).astype(jnp.float32)
    return 0.5 * (0.1 * (1.0 + upper))


def pack_kernel(level_ref, state_ref, depth_ref, wet_ref, out_ref):
    local, _, n, _ = state_ref.shape
    for k in range(local):
        wet = wet_ref[k].astype(jnp.float32)
        fields = (state_ref[k, 0], state_ref[k, 1], state_ref[k, 2], wet * depth_ref[k])
        for f, x in enumerate(fields):
            x_t = x.T
            pair, half = divmod(f, 2)
            at = f * WIDTH
            out_ref[k, at:at + HALF, :] = x_t[0:HALF]
            out_ref[k, at + HALF:at + WIDTH, :] = x_t[n - HALF:n]
            at = (NORTH_TILE + pair) * WIDTH + half * HALF
            out_ref[k, at:at + HALF, :] = x[n - HALF:n]
            at = (SOUTH_TILE + f) * WIDTH
            out_ref[k, at:at + WIDTH, :] = x[0:WIDTH]
        at = COEF_TILE * WIDTH
        out_ref[k, at - 1:at, :] = half_coef_rows(level_ref[k], (1, n))


def replay_kernel(base_ref, readers_ref, every_ref, green_ref, ids_ref, mine_ref, grad_ref,
                  q_ref, ghost_ref, south_ref):
    group, _, n = every_ref.shape
    local = mine_ref.shape[1]
    rows = group * WIDTH
    base = base_ref[0]

    def tile(index):
        return every_ref[:, index * WIDTH:(index + 1) * WIDTH, :]

    def load(kind, f):
        pair, half = divmod(f, 2)
        if kind == 0:
            block = tile(f)
        elif kind == 1:
            block = tile(SOUTH_TILE + f)
        else:
            block = tile(NORTH_TILE + pair)
            if half == 0:
                block = pltpu.roll(block, HALF, 1)
        return block.reshape(rows, n)

    strips = [[load(kind, f) for f in range(FIELDS)] for kind in range(KINDS)]
    coef_row = every_ref[:, COEF_TILE * WIDTH - 1:COEF_TILE * WIDTH, :]
    half_all = jnp.broadcast_to(coef_row, (group, WIDTH, n)).reshape(rows, n)

    lane = lax.broadcasted_iota(jnp.int32, (1, rows), 1)
    sub = lax.broadcasted_iota(jnp.int32, (group, rows), 0)
    column = lax.broadcasted_iota(jnp.int32, (group, rows), 1)
    owner = (lax.broadcasted_iota(jnp.int32, (rows, rows), 0) // WIDTH).astype(jnp.float32)
    listed = readers_ref[...].astype(jnp.float32)
    for t in range(4):
        source = t ^ 1
        edge = 0 if source in (0, 2) else WIDTH - 1
        spot = (column // WIDTH == sub) & ((column & (WIDTH - 1)) == edge)
        value = jnp.sum(jnp.where(spot, listed[:, source:source + 1], 0.0), axis=0, keepdims=True)
        lanes = jnp.where((lane & (WIDTH - 1)) == edge, value, -1.0)
        q_ref[t] = (lanes == owner).astype(jnp.bfloat16)

    srow = lax.broadcasted_iota(jnp.int32, (rows, n), 0) & (WIDTH - 1)
    slane = lax.broadcasted_iota(jnp.int32, (rows, n), 1)

    def across_low(f, ghost):
        return pltpu.roll(f, rows - 1, 0) - jnp.where(srow == 0, ghost, pltpu.roll(f, 1, 0))

    def across_high(f, ghost):
        return jnp.where(srow == WIDTH - 1, ghost, pltpu.roll(f, rows - 1, 0)) - pltpu.roll(f, 1, 0)

    def pick(ghost, offset):
        return jnp.sum(jnp.where(slane == srow + offset, ghost, 0.0), axis=1, keepdims=True)

    def along(f, low, high):
        right = jnp.where(slane == n - 1, high, pltpu.roll(f, n - 1, 1))
        left = jnp.where(slane == 0, low, pltpu.roll(f, 1, 1))
        return right - left

    far = jnp.where(srow >= HALF, n - WIDTH, 0)
    for sweep in range(STEPS):
        face_data = []
        for kind in range(KINDS):
            h, e, nf, dw = strips[kind]
            flux = dw * (e if kind == 0 else nf)
            face_data.append((flux, h))
        pieces = []
        for flux, h in face_data:
            rest = jnp.concatenate([flux, h], axis=1)
            parts = []
            for _ in range(3):
                part = rest.astype(jnp.bfloat16)
                rest = rest - part.astype(jnp.float32)
                parts.append(part)
            pieces.append(parts)
        for t in range(4):
            parts = pieces[(0, 0, 1, 2)[t ^ 1]]
            total = None
            for part in parts:
                term = jnp.dot(q_ref[t], part, preferred_element_type=jnp.float32)
                total = term if total is None else total + term
            ghost_ref[t, 0] = total[:, 0:n]
            ghost_ref[t, 1] = total[:, n:2 * n]
        for k in range(local):
            at = (base + k) * WIDTH
            for t in range(4):
                for c in range(2):
                    mine_ref[sweep, k, 2 * t + c:2 * t + c + 1, :] = ghost_ref[t, c, pl.ds(at, 1), :]

        gw = [ghost_ref[0, c] for c in range(2)]
        ge = [ghost_ref[1, c] for c in range(2)]
        gs = [ghost_ref[2, c] for c in range(2)]
        gn = [ghost_ref[3, c] for c in range(2)]
        advanced = []
        for kind in range(KINDS):
            h, e, nf, dw = strips[kind]
            if sweep == STEPS - 1 and kind != 1:
                advanced.append(strips[kind])
                continue
            wet = jnp.where(dw > 0.0, 1.0, 0.0)
            fx = dw * e
            fy = dw * nf
            if kind == 0:
                def across(f, west, east):
                    upper = jnp.where(srow == WIDTH - 1, east, pltpu.roll(f, rows - 1, 0))
                    lower = jnp.where(srow == 0, west, pltpu.roll(f, 1, 0))
                    return upper - lower
                d_fx = across(fx, gw[0], ge[0])
                d_hx = across(h, gw[1], ge[1])
                d_fy = along(fy, pick(gs[0], far), pick(gn[0], far))
                d_hy = along(h, pick(gs[1], far), pick(gn[1], far))
            else:
                offset = 0 if kind == 1 else n - WIDTH
                across = across_low if kind == 1 else across_high
                ghost = gs if kind == 1 else gn
                d_fy = across(fy, ghost[0])
                d_hy = across(h, ghost[1])
                d_fx = along(fx, pick(gw[0], offset), pick(ge[0], offset))
                d_hx = along(h, pick(gw[1], offset), pick(ge[1], offset))
            new_h = h + half_all * (d_fx + d_fy)
            new_e = wet * (e + half_all * d_hx)
            new_n = wet * (nf + half_all * d_hy)
            advanced.append((new_h, new_e, new_n, dw))
        strips = advanced

    south_ref[...] = strips[1][0]

    subfaults = green_ref.shape[0]

    def project(r, acc):
        j, i = r // SRC_ROWS, r % SRC_ROWS
        block = green_ref[:, pl.ds(pl.multiple_of(r * n, n), n)].astype(jnp.float32)
        shown = south_ref[pl.ds(j * WIDTH + i, 1), :].astype(jnp.bfloat16).astype(jnp.float32)
        return acc + block * shown

    acc = lax.fori_loop(0, group * SRC_ROWS, project, jnp.zeros((subfaults, n), jnp.float32), unroll=8)
    slip = jnp.sum(acc, axis=1, keepdims=True)
    ghost_ref[0, 0] = jnp.zeros((rows, n), jnp.float32)
    ghost_ref[0, 0, 0:1, 0:subfaults] = ids_ref[...].astype(jnp.float32)
    ids = ghost_ref[0, 0, 0:n, :].T[0:subfaults, 0:1]
    faults = grad_ref.shape[1]
    which = lax.broadcasted_iota(jnp.int32, (subfaults, faults), 1).astype(jnp.float32)
    grad_ref[...] = jnp.sum(jnp.where(which == ids, slip, 0.0), axis=0, keepdims=True)


def update_kernel(level_ref, mine_ref, state_ref, depth_ref, wet_ref, out_ref, turn_ref):
    local, _, n, _ = state_ref.shape
    col = lax.broadcasted_iota(jnp.int32, (n, n), 1)
    row = lax.broadcasted_iota(jnp.int32, (n, n), 0)

    def diff_cols(f, west, east):
        right = jnp.where(col == n - 1, east, pltpu.roll(f, n - 1, 1))
        left = jnp.where(col == 0, west, pltpu.roll(f, 1, 1))
        return right - left

    def diff_rows(f, south, north):
        upper = jnp.where(row == n - 1, north, pltpu.roll(f, n - 1, 0))
        lower = jnp.where(row == 0, south, pltpu.roll(f, 1, 0))
        return upper - lower

    turn_ref[...] = jnp.zeros_like(turn_ref)
    for k in range(local):
        half_coef = half_coef_rows(level_ref[k], (1, n))
        wet = wet_ref[k].astype(jnp.float32)
        depth_wet = wet * depth_ref[k]
        height = state_ref[k, 0]
        east_flow = state_ref[k, 1]
        north_flow = state_ref[k, 2]
        for sweep in range(STEPS):
            g = mine_ref[sweep, k]
            turn_ref[0:WIDTH, :] = g
            sides = turn_ref[...].T
            west_fx, west_h = sides[:, 0:1], sides[:, 1:2]
            east_fx, east_h = sides[:, 2:3], sides[:, 3:4]
            flux_x = depth_wet * east_flow
            flux_y = depth_wet * north_flow
            new_height = height + half_coef * (
                diff_cols(flux_x, west_fx, east_fx) + diff_rows(flux_y, g[4:5], g[6:7])
            )
            new_east = wet * (east_flow + half_coef * diff_cols(height, west_h, east_h))
            new_north = wet * (north_flow + half_coef * diff_rows(height, g[5:6], g[7:8]))
            height, east_flow, north_flow = new_height, new_east, new_north
        out_ref[k, 0] = height
        out_ref[k, 1] = east_flow
        out_ref[k, 2] = north_flow


def _vmem():
    return pl.BlockSpec(memory_space=pltpu.VMEM)


def _smem():
    return pl.BlockSpec(memory_space=pltpu.SMEM)


def pack(levels, state, depth, wet_mask):
    local, _, n, _ = state.shape
    return pl.pallas_call(
        pack_kernel,
        out_shape=jax.ShapeDtypeStruct((local, PACK_ROWS, n), jnp.float32),
        in_specs=[_smem()] + [_vmem()] * 3,
        out_specs=_vmem(),
    )(levels, state, depth, wet_mask)


def replay(base, readers, every, green, ids, local):
    group, _, n = every.shape
    rows = group * WIDTH
    return pl.pallas_call(
        replay_kernel,
        out_shape=(
            jax.ShapeDtypeStruct((STEPS, local, WIDTH, n), jnp.float32),
            jax.ShapeDtypeStruct((1, FAULTS), jnp.float32),
        ),
        in_specs=[_smem()] + [_vmem()] * 4,
        out_specs=(_vmem(), _vmem()),
        scratch_shapes=[
            pltpu.VMEM((4, rows, rows), jnp.bfloat16),
            pltpu.VMEM((4, 2, rows, n), jnp.float32),
            pltpu.VMEM((rows, n), jnp.float32),
        ],
    )(base, readers, every, green, ids)


def update(levels, mine, state, depth, wet_mask):
    local, _, n, _ = state.shape
    cells = local * n * n
    return pl.pallas_call(
        update_kernel,
        out_shape=jax.ShapeDtypeStruct(state.shape, jnp.float32),
        in_specs=[_smem()] + [_vmem()] * 4,
        out_specs=_vmem(),
        scratch_shapes=[pltpu.VMEM((n, n), jnp.float32)],
        cost_estimate=pl.CostEstimate(
            flops=40 * STEPS * cells, transcendentals=0, bytes_accessed=4 * 8 * cells
        ),
    )(levels, mine, state, depth, wet_mask)


def all_sum(x, axis):
    size = lax.axis_size(axis)
    total = x
    for shift in range(1, size):
        if size & (size - 1) == 0:
            pairs = [(i, i ^ shift) for i in range(size)]
        else:
            pairs = [(i, (i + shift) % size) for i in range(size)]
        total = total + lax.ppermute(x, axis, pairs)
    return total


def shards(adjoint_init, depth, wet_mask, levels, readers, green, fault_ids):
    state = adjoint_init[0]
    local, _, n, _ = state.shape
    base = (lax.axis_index("patch") * local).astype(jnp.int32).reshape(1)
    packed = pack(levels[0], state, depth[0], wet_mask[0])
    every = lax.all_gather(packed, "patch", axis=0, tiled=True)
    mine, partial_grad = replay(base, readers[0], every, green[0], fault_ids[0].reshape(1, -1), local)
    partial_grad = partial_grad.reshape(-1)
    group_grad = lax.all_gather(partial_grad, "patch", axis=0).sum(axis=0)
    fault_grad = all_sum(group_grad, "grp")
    state = update(levels[0], mine, state, depth[0], wet_mask[0])
    return (state[None], fault_grad)


def solution(mesh):
    placed = (
        P("grp", "patch", None, None, None),
        P("grp", "patch", None, None),
        P("grp", "patch", None, None),
        P("grp", "patch"),
        P("grp", None, None),
        P("grp", "patch", None),
        P("grp", "patch"),
    )
    return jax.shard_map(
        shards,
        mesh=mesh,
        in_specs=placed,
        out_specs=(P("grp", "patch", None, None, None), P()),
        check_vma=False,
    )
```

```python
import jax
import jax.numpy as jnp
from jax import lax
from jax.experimental import pallas as pl
from jax.experimental.pallas import tpu as pltpu
from jax.sharding import PartitionSpec as P

SRC_ROWS = 4
STEPS = 4
FAULTS = 2048
WIDTH = 8
HALF = WIDTH // 2
FIELDS = 4
KINDS = 3
NORTH_TILE = FIELDS
SOUTH_TILE = NORTH_TILE + 2
COEF_TILE = SOUTH_TILE + FIELDS
PACK_ROWS = COEF_TILE * WIDTH
HIGH = lax.Precision.HIGHEST


def half_coef_rows(level, shape):
    levels = jnp.full(shape, level, jnp.int32)
    upper = (levels >= 1).astype(jnp.float32) + 2.0 * (levels >= 2).astype(jnp.float32)
    return 0.5 * (0.1 * (1.0 + upper))


def pack_kernel(level_ref, state_ref, depth_ref, wet_ref, out_ref):
    local, _, n, _ = state_ref.shape
    for k in range(local):
        wet = wet_ref[k].astype(jnp.float32)
        fields = (state_ref[k, 0], state_ref[k, 1], state_ref[k, 2], wet * depth_ref[k])
        for f, x in enumerate(fields):
            x_t = x.T
            pair, half = divmod(f, 2)
            at = f * WIDTH
            out_ref[k, at:at + HALF, :] = x_t[0:HALF]
            out_ref[k, at + HALF:at + WIDTH, :] = x_t[n - HALF:n]
            at = (NORTH_TILE + pair) * WIDTH + half * HALF
            out_ref[k, at:at + HALF, :] = x[n - HALF:n]
            at = (SOUTH_TILE + f) * WIDTH
            out_ref[k, at:at + WIDTH, :] = x[0:WIDTH]
        at = COEF_TILE * WIDTH
        out_ref[k, at - 1:at, :] = half_coef_rows(level_ref[k], (1, n))


def replay_kernel(base_ref, readers_ref, every_ref, green_ref, ids_ref, mine_ref, grad_ref,
                  q_ref, ghost_ref, south_ref):
    group, _, n = every_ref.shape
    local = mine_ref.shape[1]
    rows = group * WIDTH
    base = base_ref[0]

    def tile(index):
        return every_ref[:, index * WIDTH:(index + 1) * WIDTH, :]

    def load(kind, f):
        pair, half = divmod(f, 2)
        if kind == 0:
            block = tile(f)
        elif kind == 1:
            block = tile(SOUTH_TILE + f)
        else:
            block = tile(NORTH_TILE + pair)
            if half == 0:
                block = pltpu.roll(block, HALF, 1)
        return block.reshape(rows, n)

    strips = [[load(kind, f) for f in range(FIELDS)] for kind in range(KINDS)]
    coef_row = every_ref[:, COEF_TILE * WIDTH - 1:COEF_TILE * WIDTH, :]
    half_all = jnp.broadcast_to(coef_row, (group, WIDTH, n)).reshape(rows, n)

    lane = lax.broadcasted_iota(jnp.int32, (1, rows), 1)
    sub = lax.broadcasted_iota(jnp.int32, (group, rows), 0)
    column = lax.broadcasted_iota(jnp.int32, (group, rows), 1)
    owner = (lax.broadcasted_iota(jnp.int32, (rows, rows), 0) // WIDTH).astype(jnp.float32)
    spread = (column // WIDTH == sub).astype(jnp.bfloat16)
    listed = jnp.dot(readers_ref[...].astype(jnp.bfloat16), spread, preferred_element_type=jnp.float32)
    for t in range(4):
        source = t ^ 1
        edge = 0 if source in (0, 2) else WIDTH - 1
        lanes = jnp.where((lane & (WIDTH - 1)) == edge, listed[source:source + 1, :], -1.0)
        q_ref[t] = (lanes == owner).astype(jnp.bfloat16)

    srow = lax.broadcasted_iota(jnp.int32, (rows, n), 0) & (WIDTH - 1)
    slane = lax.broadcasted_iota(jnp.int32, (rows, n), 1)

    def across_low(f, ghost):
        return pltpu.roll(f, rows - 1, 0) - jnp.where(srow == 0, ghost, pltpu.roll(f, 1, 0))

    def across_high(f, ghost):
        return jnp.where(srow == WIDTH - 1, ghost, pltpu.roll(f, rows - 1, 0)) - pltpu.roll(f, 1, 0)

    def pick(ghost, offset):
        return jnp.sum(jnp.where(slane == srow + offset, ghost, 0.0), axis=1, keepdims=True)

    def along(f, low, high):
        right = jnp.where(slane == n - 1, high, pltpu.roll(f, n - 1, 1))
        left = jnp.where(slane == 0, low, pltpu.roll(f, 1, 1))
        return right - left

    far = jnp.where(srow >= HALF, n - WIDTH, 0)
    for sweep in range(STEPS):
        face_data = []
        for kind in range(KINDS):
            h, e, nf, dw = strips[kind]
            flux = dw * (e if kind == 0 else nf)
            face_data.append((flux, h))
        pieces = []
        for flux, h in face_data:
            rest = jnp.concatenate([flux, h], axis=1)
            parts = []
            for _ in range(3):
                part = rest.astype(jnp.bfloat16)
                rest = rest - part.astype(jnp.float32)
                parts.append(part)
            pieces.append(parts)
        for t in range(4):
            parts = pieces[(0, 0, 1, 2)[t ^ 1]]
            total = None
            for part in parts:
                term = jnp.dot(q_ref[t], part, preferred_element_type=jnp.float32)
                total = term if total is None else total + term
            ghost_ref[t, 0] = total[:, 0:n]
            ghost_ref[t, 1] = total[:, n:2 * n]
        for k in range(local):
            at = (base + k) * WIDTH
            for t in range(4):
                for c in range(2):
                    mine_ref[sweep, k, 2 * t + c:2 * t + c + 1, :] = ghost_ref[t, c, pl.ds(at, 1), :]

        gw = [ghost_ref[0, c] for c in range(2)]
        ge = [ghost_ref[1, c] for c in range(2)]
        gs = [ghost_ref[2, c] for c in range(2)]
        gn = [ghost_ref[3, c] for c in range(2)]
        advanced = []
        for kind in range(KINDS):
            h, e, nf, dw = strips[kind]
            if sweep == STEPS - 1 and kind != 1:
                advanced.append(strips[kind])
                continue
            wet = jnp.where(dw > 0.0, 1.0, 0.0)
            fx = dw * e
            fy = dw * nf
            if kind == 0:
                def across(f, west, east):
                    upper = jnp.where(srow == WIDTH - 1, east, pltpu.roll(f, rows - 1, 0))
                    lower = jnp.where(srow == 0, west, pltpu.roll(f, 1, 0))
                    return upper - lower
                d_fx = across(fx, gw[0], ge[0])
                d_hx = across(h, gw[1], ge[1])
                d_fy = along(fy, pick(gs[0], far), pick(gn[0], far))
                d_hy = along(h, pick(gs[1], far), pick(gn[1], far))
            else:
                offset = 0 if kind == 1 else n - WIDTH
                across = across_low if kind == 1 else across_high
                ghost = gs if kind == 1 else gn
                d_fy = across(fy, ghost[0])
                d_hy = across(h, ghost[1])
                d_fx = along(fx, pick(gw[0], offset), pick(ge[0], offset))
                d_hx = along(h, pick(gw[1], offset), pick(ge[1], offset))
            new_h = h + half_all * (d_fx + d_fy)
            new_e = wet * (e + half_all * d_hx)
            new_n = wet * (nf + half_all * d_hy)
            advanced.append((new_h, new_e, new_n, dw))
        strips = advanced

    south_ref[...] = strips[1][0]

    subfaults = green_ref.shape[0]

    def project(r, acc):
        j, i = r // SRC_ROWS, r % SRC_ROWS
        block = green_ref[:, pl.ds(pl.multiple_of(r * n, n), n)].astype(jnp.float32)
        shown = south_ref[pl.ds(j * WIDTH + i, 1), :].astype(jnp.bfloat16).astype(jnp.float32)
        return acc + block * shown

    acc = lax.fori_loop(0, group * SRC_ROWS, project, jnp.zeros((subfaults, n), jnp.float32), unroll=8)
    slip = jnp.sum(acc, axis=1, keepdims=True)
    ghost_ref[0, 0] = jnp.zeros((rows, n), jnp.float32)
    ghost_ref[0, 0, 0:1, 0:subfaults] = ids_ref[...].astype(jnp.float32)
    ids = ghost_ref[0, 0, 0:n, :].T[0:subfaults, 0:1]
    faults = grad_ref.shape[1]
    which = lax.broadcasted_iota(jnp.int32, (subfaults, faults), 1).astype(jnp.float32)
    grad_ref[...] = jnp.sum(jnp.where(which == ids, slip, 0.0), axis=0, keepdims=True)


def update_kernel(level_ref, mine_ref, state_ref, depth_ref, wet_ref, out_ref, turn_ref):
    local, _, n, _ = state_ref.shape
    col = lax.broadcasted_iota(jnp.int32, (n, n), 1)
    row = lax.broadcasted_iota(jnp.int32, (n, n), 0)

    def diff_cols(f, west, east):
        right = jnp.where(col == n - 1, east, pltpu.roll(f, n - 1, 1))
        left = jnp.where(col == 0, west, pltpu.roll(f, 1, 1))
        return right - left

    def diff_rows(f, south, north):
        upper = jnp.where(row == n - 1, north, pltpu.roll(f, n - 1, 0))
        lower = jnp.where(row == 0, south, pltpu.roll(f, 1, 0))
        return upper - lower

    turn_ref[...] = jnp.zeros_like(turn_ref)
    for k in range(local):
        half_coef = half_coef_rows(level_ref[k], (1, n))
        wet = wet_ref[k].astype(jnp.float32)
        depth_wet = wet * depth_ref[k]
        height = state_ref[k, 0]
        east_flow = state_ref[k, 1]
        north_flow = state_ref[k, 2]
        for sweep in range(STEPS):
            g = mine_ref[sweep, k]
            turn_ref[0:WIDTH, :] = g
            sides = turn_ref[...].T
            west_fx, west_h = sides[:, 0:1], sides[:, 1:2]
            east_fx, east_h = sides[:, 2:3], sides[:, 3:4]
            flux_x = depth_wet * east_flow
            flux_y = depth_wet * north_flow
            new_height = height + half_coef * (
                diff_cols(flux_x, west_fx, east_fx) + diff_rows(flux_y, g[4:5], g[6:7])
            )
            new_east = wet * (east_flow + half_coef * diff_cols(height, west_h, east_h))
            new_north = wet * (north_flow + half_coef * diff_rows(height, g[5:6], g[7:8]))
            height, east_flow, north_flow = new_height, new_east, new_north
        out_ref[k, 0] = height
        out_ref[k, 1] = east_flow
        out_ref[k, 2] = north_flow


def _vmem():
    return pl.BlockSpec(memory_space=pltpu.VMEM)


def _smem():
    return pl.BlockSpec(memory_space=pltpu.SMEM)


def pack(levels, state, depth, wet_mask):
    local, _, n, _ = state.shape
    return pl.pallas_call(
        pack_kernel,
        out_shape=jax.ShapeDtypeStruct((local, PACK_ROWS, n), jnp.float32),
        in_specs=[_smem()] + [_vmem()] * 3,
        out_specs=_vmem(),
    )(levels, state, depth, wet_mask)


def replay(base, readers, every, green, ids, local):
    group, _, n = every.shape
    rows = group * WIDTH
    return pl.pallas_call(
        replay_kernel,
        out_shape=(
            jax.ShapeDtypeStruct((STEPS, local, WIDTH, n), jnp.float32),
            jax.ShapeDtypeStruct((1, FAULTS), jnp.float32),
        ),
        in_specs=[_smem()] + [_vmem()] * 4,
        out_specs=(_vmem(), _vmem()),
        scratch_shapes=[
            pltpu.VMEM((4, rows, rows), jnp.bfloat16),
            pltpu.VMEM((4, 2, rows, n), jnp.float32),
            pltpu.VMEM((rows, n), jnp.float32),
        ],
    )(base, readers, every, green, ids)


def update(levels, mine, state, depth, wet_mask):
    local, _, n, _ = state.shape
    cells = local * n * n
    return pl.pallas_call(
        update_kernel,
        out_shape=jax.ShapeDtypeStruct(state.shape, jnp.float32),
        in_specs=[_smem()] + [_vmem()] * 4,
        out_specs=_vmem(),
        scratch_shapes=[pltpu.VMEM((n, n), jnp.float32)],
        cost_estimate=pl.CostEstimate(
            flops=40 * STEPS * cells, transcendentals=0, bytes_accessed=4 * 8 * cells
        ),
    )(levels, mine, state, depth, wet_mask)


def all_sum(x, axis):
    size = lax.axis_size(axis)
    total = x
    for shift in range(1, size):
        if size & (size - 1) == 0:
            pairs = [(i, i ^ shift) for i in range(size)]
        else:
            pairs = [(i, (i + shift) % size) for i in range(size)]
        total = total + lax.ppermute(x, axis, pairs)
    return total


def shards(adjoint_init, depth, wet_mask, levels, readers, green, fault_ids):
    state = adjoint_init[0]
    local, _, n, _ = state.shape
    base = (lax.axis_index("patch") * local).astype(jnp.int32).reshape(1)
    packed = pack(levels[0], state, depth[0], wet_mask[0])
    every = lax.all_gather(packed, "patch", axis=0, tiled=True)
    mine, partial_grad = replay(base, readers[0].T, every, green[0], fault_ids[0].reshape(1, -1), local)
    partial_grad = partial_grad.reshape(-1)
    group_grad = lax.all_gather(partial_grad, "patch", axis=0).sum(axis=0)
    fault_grad = all_sum(group_grad, "grp")
    state = update(levels[0], mine, state, depth[0], wet_mask[0])
    return (state[None], fault_grad)


def solution(mesh):
    placed = (
        P("grp", "patch", None, None, None),
        P("grp", "patch", None, None),
        P("grp", "patch", None, None),
        P("grp", "patch"),
        P("grp", None, None),
        P("grp", "patch", None),
        P("grp", "patch"),
    )
    return jax.shard_map(
        shards,
        mesh=mesh,
        in_specs=placed,
        out_specs=(P("grp", "patch", None, None, None), P()),
        check_vma=False,
    )
```

```python
import jax
import jax.numpy as jnp
from jax import lax
from jax.experimental import pallas as pl
from jax.experimental.pallas import tpu as pltpu
from jax.sharding import PartitionSpec as P

SRC_ROWS = 4
STEPS = 4
FAULTS = 2048
WIDTH = 8
HALF = WIDTH // 2
FIELDS = 4
KINDS = 3
NORTH_TILE = FIELDS
SOUTH_TILE = NORTH_TILE + 2
COEF_TILE = SOUTH_TILE + FIELDS
PACK_ROWS = COEF_TILE * WIDTH
HIGH = lax.Precision.HIGHEST


def half_coef_rows(level, shape):
    levels = jnp.full(shape, level, jnp.int32)
    upper = (levels >= 1).astype(jnp.float32) + 2.0 * (levels >= 2).astype(jnp.float32)
    return 0.5 * (0.1 * (1.0 + upper))


def pack_kernel(level_ref, state_ref, depth_ref, wet_ref, out_ref):
    local, _, n, _ = state_ref.shape
    for k in range(local):
        wet = wet_ref[k].astype(jnp.float32)
        fields = (state_ref[k, 0], state_ref[k, 1], state_ref[k, 2], wet * depth_ref[k])
        for f, x in enumerate(fields):
            x_t = x.T
            pair, half = divmod(f, 2)
            at = f * WIDTH
            out_ref[k, at:at + HALF, :] = x_t[0:HALF]
            out_ref[k, at + HALF:at + WIDTH, :] = x_t[n - HALF:n]
            at = (NORTH_TILE + pair) * WIDTH + half * HALF
            out_ref[k, at:at + HALF, :] = x[n - HALF:n]
            at = (SOUTH_TILE + f) * WIDTH
            out_ref[k, at:at + WIDTH, :] = x[0:WIDTH]
        at = COEF_TILE * WIDTH
        out_ref[k, at - 1:at, :] = half_coef_rows(level_ref[k], (1, n))


def replay_kernel(base_ref, readers_ref, every_ref, green_ref, ids_ref, mine_ref, grad_ref,
                  q_ref, ghost_ref, south_ref):
    group, _, n = every_ref.shape
    local = mine_ref.shape[1]
    rows = group * WIDTH
    base = base_ref[0]

    def tile(index):
        return every_ref[:, index * WIDTH:(index + 1) * WIDTH, :]

    def load(kind, f):
        pair, half = divmod(f, 2)
        if kind == 0:
            block = tile(f)
        elif kind == 1:
            block = tile(SOUTH_TILE + f)
        else:
            block = tile(NORTH_TILE + pair)
            if half == 0:
                block = pltpu.roll(block, HALF, 1)
        return block.reshape(rows, n)

    strips = [[load(kind, f) for f in range(FIELDS)] for kind in range(KINDS)]
    coef_row = every_ref[:, COEF_TILE * WIDTH - 1:COEF_TILE * WIDTH, :]
    half_all = jnp.broadcast_to(coef_row, (group, WIDTH, n)).reshape(rows, n)

    lane = lax.broadcasted_iota(jnp.int32, (1, rows), 1)
    sub = lax.broadcasted_iota(jnp.int32, (group, rows), 0)
    column = lax.broadcasted_iota(jnp.int32, (group, rows), 1)
    owner = (lax.broadcasted_iota(jnp.int32, (rows, rows), 0) // WIDTH).astype(jnp.float32)
    spread = (column // WIDTH == sub).astype(jnp.bfloat16)
    listed = jnp.dot(readers_ref[...].astype(jnp.bfloat16), spread, preferred_element_type=jnp.float32)
    for t in range(4):
        source = t ^ 1
        edge = 0 if source in (0, 2) else WIDTH - 1
        lanes = jnp.where((lane & (WIDTH - 1)) == edge, listed[source:source + 1, :], -1.0)
        q_ref[t] = (lanes == owner).astype(jnp.bfloat16)

    srow = lax.broadcasted_iota(jnp.int32, (rows, n), 0) & (WIDTH - 1)
    slane = lax.broadcasted_iota(jnp.int32, (rows, n), 1)

    def across_low(f, ghost):
        return pltpu.roll(f, rows - 1, 0) - jnp.where(srow == 0, ghost, pltpu.roll(f, 1, 0))

    def across_high(f, ghost):
        return jnp.where(srow == WIDTH - 1, ghost, pltpu.roll(f, rows - 1, 0)) - pltpu.roll(f, 1, 0)

    def pick(ghost, offset):
        return jnp.sum(jnp.where(slane == srow + offset, ghost, 0.0), axis=1, keepdims=True)

    def along(f, low, high):
        right = jnp.where(slane == n - 1, high, pltpu.roll(f, n - 1, 1))
        left = jnp.where(slane == 0, low, pltpu.roll(f, 1, 1))
        return right - left

    far = jnp.where(srow >= HALF, n - WIDTH, 0)
    for sweep in range(STEPS):
        face_data = []
        for kind in range(KINDS):
            h, e, nf, dw = strips[kind]
            flux = dw * (e if kind == 0 else nf)
            face_data.append((flux, h))
        pieces = []
        for flux, h in face_data:
            rest = jnp.concatenate([flux, h], axis=1)
            parts = []
            for _ in range(3):
                part = rest.astype(jnp.bfloat16)
                rest = rest - part.astype(jnp.float32)
                parts.append(part)
            pieces.append(parts)
        for t in range(4):
            parts = pieces[(0, 0, 1, 2)[t ^ 1]]
            total = None
            for part in parts:
                term = jnp.dot(q_ref[t], part, preferred_element_type=jnp.float32)
                total = term if total is None else total + term
            ghost_ref[t, 0] = total[:, 0:n]
            ghost_ref[t, 1] = total[:, n:2 * n]
        for k in range(local):
            at = (base + k) * WIDTH
            for t in range(4):
                for c in range(2):
                    mine_ref[sweep, k, 2 * t + c:2 * t + c + 1, :] = ghost_ref[t, c, pl.ds(at, 1), :]

        gw = [ghost_ref[0, c] for c in range(2)]
        ge = [ghost_ref[1, c] for c in range(2)]
        gs = [ghost_ref[2, c] for c in range(2)]
        gn = [ghost_ref[3, c] for c in range(2)]
        advanced = []
        for kind in range(KINDS):
            h, e, nf, dw = strips[kind]
            if sweep == STEPS - 1 and kind != 1:
                advanced.append(strips[kind])
                continue
            wet = jnp.where(dw > 0.0, 1.0, 0.0)
            fx = dw * e
            fy = dw * nf
            if kind == 0:
                def across(f, west, east):
                    upper = jnp.where(srow == WIDTH - 1, east, pltpu.roll(f, rows - 1, 0))
                    lower = jnp.where(srow == 0, west, pltpu.roll(f, 1, 0))
                    return upper - lower
                d_fx = across(fx, gw[0], ge[0])
                d_hx = across(h, gw[1], ge[1])
                d_fy = along(fy, pick(gs[0], far), pick(gn[0], far))
                d_hy = along(h, pick(gs[1], far), pick(gn[1], far))
            else:
                offset = 0 if kind == 1 else n - WIDTH
                across = across_low if kind == 1 else across_high
                ghost = gs if kind == 1 else gn
                d_fy = across(fy, ghost[0])
                d_hy = across(h, ghost[1])
                d_fx = along(fx, pick(gw[0], offset), pick(ge[0], offset))
                d_hx = along(h, pick(gw[1], offset), pick(ge[1], offset))
            new_h = h + half_all * (d_fx + d_fy)
            new_e = wet * (e + half_all * d_hx)
            new_n = wet * (nf + half_all * d_hy)
            advanced.append((new_h, new_e, new_n, dw))
        strips = advanced

    south_ref[...] = strips[1][0]

    subfaults = green_ref.shape[0]

    def project(r, acc):
        j, i = r // SRC_ROWS, r % SRC_ROWS
        block = green_ref[:, pl.ds(pl.multiple_of(r * n, n), n)].astype(jnp.float32)
        shown = south_ref[pl.ds(j * WIDTH + i, 1), :].astype(jnp.bfloat16).astype(jnp.float32)
        return acc + block * shown

    acc = lax.fori_loop(0, group * SRC_ROWS, project, jnp.zeros((subfaults, n), jnp.float32), unroll=True)
    slip = jnp.sum(acc, axis=1, keepdims=True)
    ghost_ref[0, 0] = jnp.zeros((rows, n), jnp.float32)
    ghost_ref[0, 0, 0:1, 0:subfaults] = ids_ref[...].astype(jnp.float32)
    ids = ghost_ref[0, 0, 0:n, :].T[0:subfaults, 0:1]
    faults = grad_ref.shape[1]
    which = lax.broadcasted_iota(jnp.int32, (subfaults, faults), 1).astype(jnp.float32)
    grad_ref[...] = jnp.sum(jnp.where(which == ids, slip, 0.0), axis=0, keepdims=True)


def update_kernel(level_ref, mine_ref, state_ref, depth_ref, wet_ref, out_ref, turn_ref):
    local, _, n, _ = state_ref.shape
    col = lax.broadcasted_iota(jnp.int32, (n, n), 1)
    row = lax.broadcasted_iota(jnp.int32, (n, n), 0)

    def diff_cols(f, west, east):
        right = jnp.where(col == n - 1, east, pltpu.roll(f, n - 1, 1))
        left = jnp.where(col == 0, west, pltpu.roll(f, 1, 1))
        return right - left

    def diff_rows(f, south, north):
        upper = jnp.where(row == n - 1, north, pltpu.roll(f, n - 1, 0))
        lower = jnp.where(row == 0, south, pltpu.roll(f, 1, 0))
        return upper - lower

    turn_ref[...] = jnp.zeros_like(turn_ref)
    for k in range(local):
        half_coef = half_coef_rows(level_ref[k], (1, n))
        wet = wet_ref[k].astype(jnp.float32)
        depth_wet = wet * depth_ref[k]
        height = state_ref[k, 0]
        east_flow = state_ref[k, 1]
        north_flow = state_ref[k, 2]
        for sweep in range(STEPS):
            g = mine_ref[sweep, k]
            turn_ref[0:WIDTH, :] = g
            sides = turn_ref[...].T
            west_fx, west_h = sides[:, 0:1], sides[:, 1:2]
            east_fx, east_h = sides[:, 2:3], sides[:, 3:4]
            flux_x = depth_wet * east_flow
            flux_y = depth_wet * north_flow
            new_height = height + half_coef * (
                diff_cols(flux_x, west_fx, east_fx) + diff_rows(flux_y, g[4:5], g[6:7])
            )
            new_east = wet * (east_flow + half_coef * diff_cols(height, west_h, east_h))
            new_north = wet * (north_flow + half_coef * diff_rows(height, g[5:6], g[7:8]))
            height, east_flow, north_flow = new_height, new_east, new_north
        out_ref[k, 0] = height
        out_ref[k, 1] = east_flow
        out_ref[k, 2] = north_flow


def _vmem():
    return pl.BlockSpec(memory_space=pltpu.VMEM)


def _smem():
    return pl.BlockSpec(memory_space=pltpu.SMEM)


def pack(levels, state, depth, wet_mask):
    local, _, n, _ = state.shape
    return pl.pallas_call(
        pack_kernel,
        out_shape=jax.ShapeDtypeStruct((local, PACK_ROWS, n), jnp.float32),
        in_specs=[_smem()] + [_vmem()] * 3,
        out_specs=_vmem(),
    )(levels, state, depth, wet_mask)


def replay(base, readers, every, green, ids, local):
    group, _, n = every.shape
    rows = group * WIDTH
    return pl.pallas_call(
        replay_kernel,
        out_shape=(
            jax.ShapeDtypeStruct((STEPS, local, WIDTH, n), jnp.float32),
            jax.ShapeDtypeStruct((1, FAULTS), jnp.float32),
        ),
        in_specs=[_smem()] + [_vmem()] * 4,
        out_specs=(_vmem(), _vmem()),
        scratch_shapes=[
            pltpu.VMEM((4, rows, rows), jnp.bfloat16),
            pltpu.VMEM((4, 2, rows, n), jnp.float32),
            pltpu.VMEM((rows, n), jnp.float32),
        ],
    )(base, readers, every, green, ids)


def update(levels, mine, state, depth, wet_mask):
    local, _, n, _ = state.shape
    cells = local * n * n
    return pl.pallas_call(
        update_kernel,
        out_shape=jax.ShapeDtypeStruct(state.shape, jnp.float32),
        in_specs=[_smem()] + [_vmem()] * 4,
        out_specs=_vmem(),
        scratch_shapes=[pltpu.VMEM((n, n), jnp.float32)],
        cost_estimate=pl.CostEstimate(
            flops=40 * STEPS * cells, transcendentals=0, bytes_accessed=4 * 8 * cells
        ),
    )(levels, mine, state, depth, wet_mask)


def all_sum(x, axis):
    size = lax.axis_size(axis)
    total = x
    for shift in range(1, size):
        if size & (size - 1) == 0:
            pairs = [(i, i ^ shift) for i in range(size)]
        else:
            pairs = [(i, (i + shift) % size) for i in range(size)]
        total = total + lax.ppermute(x, axis, pairs)
    return total


def shards(adjoint_init, depth, wet_mask, levels, readers, green, fault_ids):
    state = adjoint_init[0]
    local, _, n, _ = state.shape
    base = (lax.axis_index("patch") * local).astype(jnp.int32).reshape(1)
    packed = pack(levels[0], state, depth[0], wet_mask[0])
    every = lax.all_gather(packed, "patch", axis=0, tiled=True)
    mine, partial_grad = replay(base, readers[0].T, every, green[0], fault_ids[0].reshape(1, -1), local)
    partial_grad = partial_grad.reshape(-1)
    group_grad = lax.all_gather(partial_grad, "patch", axis=0).sum(axis=0)
    fault_grad = all_sum(group_grad, "grp")
    state = update(levels[0], mine, state, depth[0], wet_mask[0])
    return (state[None], fault_grad)


def solution(mesh):
    placed = (
        P("grp", "patch", None, None, None),
        P("grp", "patch", None, None),
        P("grp", "patch", None, None),
        P("grp", "patch"),
        P("grp", None, None),
        P("grp", "patch", None),
        P("grp", "patch"),
    )
    return jax.shard_map(
        shards,
        mesh=mesh,
        in_specs=placed,
        out_specs=(P("grp", "patch", None, None, None), P()),
        check_vma=False,
    )
```

```python
import jax
import jax.numpy as jnp
from jax import lax
from jax.experimental import pallas as pl
from jax.experimental.pallas import tpu as pltpu
from jax.sharding import PartitionSpec as P

SRC_ROWS = 4
STEPS = 4
FAULTS = 2048
WIDTH = 8
HALF = WIDTH // 2
FIELDS = 4
KINDS = 3
NORTH_TILE = FIELDS
SOUTH_TILE = NORTH_TILE + 2
COEF_TILE = SOUTH_TILE + FIELDS
PACK_ROWS = COEF_TILE * WIDTH
HIGH = lax.Precision.HIGHEST


def half_coef_rows(level, shape):
    levels = jnp.full(shape, level, jnp.int32)
    upper = (levels >= 1).astype(jnp.float32) + 2.0 * (levels >= 2).astype(jnp.float32)
    return 0.5 * (0.1 * (1.0 + upper))


def pack_kernel(level_ref, state_ref, depth_ref, wet_ref, out_ref):
    local, _, n, _ = state_ref.shape
    for k in range(local):
        wet = wet_ref[k].astype(jnp.float32)
        fields = (state_ref[k, 0], state_ref[k, 1], state_ref[k, 2], wet * depth_ref[k])
        for f, x in enumerate(fields):
            x_t = x.T
            pair, half = divmod(f, 2)
            at = f * WIDTH
            out_ref[k, at:at + HALF, :] = x_t[0:HALF]
            out_ref[k, at + HALF:at + WIDTH, :] = x_t[n - HALF:n]
            at = (NORTH_TILE + pair) * WIDTH + half * HALF
            out_ref[k, at:at + HALF, :] = x[n - HALF:n]
            at = (SOUTH_TILE + f) * WIDTH
            out_ref[k, at:at + WIDTH, :] = x[0:WIDTH]
        at = COEF_TILE * WIDTH
        out_ref[k, at - 1:at, :] = half_coef_rows(level_ref[k], (1, n))


def replay_kernel(base_ref, readers_ref, every_ref, green_ref, ids_ref, mine_ref, grad_ref,
                  q_ref, ghost_ref, south_ref):
    group, _, n = every_ref.shape
    local = mine_ref.shape[1]
    rows = group * WIDTH
    base = base_ref[0]

    def tile(index):
        return every_ref[:, index * WIDTH:(index + 1) * WIDTH, :]

    def load(kind, f):
        pair, half = divmod(f, 2)
        if kind == 0:
            block = tile(f)
        elif kind == 1:
            block = tile(SOUTH_TILE + f)
        else:
            block = tile(NORTH_TILE + pair)
            if half == 0:
                block = pltpu.roll(block, HALF, 1)
        return block.reshape(rows, n)

    strips = [[load(kind, f) for f in range(FIELDS)] for kind in range(KINDS)]
    coef_row = every_ref[:, COEF_TILE * WIDTH - 1:COEF_TILE * WIDTH, :]
    half_all = jnp.broadcast_to(coef_row, (group, WIDTH, n)).reshape(rows, n)

    lane = lax.broadcasted_iota(jnp.int32, (1, rows), 1)
    sub = lax.broadcasted_iota(jnp.int32, (group, rows), 0)
    column = lax.broadcasted_iota(jnp.int32, (group, rows), 1)
    owner = (lax.broadcasted_iota(jnp.int32, (rows, rows), 0) // WIDTH).astype(jnp.float32)
    spread = (column // WIDTH == sub).astype(jnp.bfloat16)
    listed = jnp.dot(readers_ref[...].astype(jnp.bfloat16), spread, preferred_element_type=jnp.float32)
    for t in range(4):
        source = t ^ 1
        edge = 0 if source in (0, 2) else WIDTH - 1
        lanes = jnp.where((lane & (WIDTH - 1)) == edge, listed[source:source + 1, :], -1.0)
        q_ref[t] = (lanes == owner).astype(jnp.bfloat16)

    srow = lax.broadcasted_iota(jnp.int32, (rows, n), 0) & (WIDTH - 1)
    slane = lax.broadcasted_iota(jnp.int32, (rows, n), 1)

    def across_low(f, ghost):
        return pltpu.roll(f, rows - 1, 0) - jnp.where(srow == 0, ghost, pltpu.roll(f, 1, 0))

    def across_high(f, ghost):
        return jnp.where(srow == WIDTH - 1, ghost, pltpu.roll(f, rows - 1, 0)) - pltpu.roll(f, 1, 0)

    def pick(ghost, offset):
        return jnp.sum(jnp.where(slane == srow + offset, ghost, 0.0), axis=1, keepdims=True)

    def along(f, low, high):
        right = jnp.where(slane == n - 1, high, pltpu.roll(f, n - 1, 1))
        left = jnp.where(slane == 0, low, pltpu.roll(f, 1, 1))
        return right - left

    far = jnp.where(srow >= HALF, n - WIDTH, 0)
    for sweep in range(STEPS):
        face_data = []
        for kind in range(KINDS):
            h, e, nf, dw = strips[kind]
            flux = dw * (e if kind == 0 else nf)
            face_data.append((flux, h))
        pieces = []
        for flux, h in face_data:
            rest = jnp.concatenate([flux, h], axis=1)
            parts = []
            for _ in range(3):
                part = rest.astype(jnp.bfloat16)
                rest = rest - part.astype(jnp.float32)
                parts.append(part)
            pieces.append(parts)
        for t in range(4):
            parts = pieces[(0, 0, 1, 2)[t ^ 1]]
            total = None
            for part in parts:
                term = jnp.dot(q_ref[t], part, preferred_element_type=jnp.float32)
                total = term if total is None else total + term
            ghost_ref[t, 0] = total[:, 0:n]
            ghost_ref[t, 1] = total[:, n:2 * n]
        for k in range(local):
            at = (base + k) * WIDTH
            for t in range(4):
                for c in range(2):
                    mine_ref[sweep, k, 2 * t + c:2 * t + c + 1, :] = ghost_ref[t, c, pl.ds(at, 1), :]

        gw = [ghost_ref[0, c] for c in range(2)]
        ge = [ghost_ref[1, c] for c in range(2)]
        gs = [ghost_ref[2, c] for c in range(2)]
        gn = [ghost_ref[3, c] for c in range(2)]
        advanced = []
        for kind in range(KINDS):
            h, e, nf, dw = strips[kind]
            if sweep == STEPS - 1 and kind != 1:
                advanced.append(strips[kind])
                continue
            wet = jnp.where(dw > 0.0, 1.0, 0.0)
            fx = dw * e
            fy = dw * nf
            if kind == 0:
                def across(f, west, east):
                    upper = jnp.where(srow == WIDTH - 1, east, pltpu.roll(f, rows - 1, 0))
                    lower = jnp.where(srow == 0, west, pltpu.roll(f, 1, 0))
                    return upper - lower
                d_fx = across(fx, gw[0], ge[0])
                d_hx = across(h, gw[1], ge[1])
                d_fy = along(fy, pick(gs[0], far), pick(gn[0], far))
                d_hy = along(h, pick(gs[1], far), pick(gn[1], far))
            else:
                offset = 0 if kind == 1 else n - WIDTH
                across = across_low if kind == 1 else across_high
                ghost = gs if kind == 1 else gn
                d_fy = across(fy, ghost[0])
                d_hy = across(h, ghost[1])
                d_fx = along(fx, pick(gw[0], offset), pick(ge[0], offset))
                d_hx = along(h, pick(gw[1], offset), pick(ge[1], offset))
            new_h = h + half_all * (d_fx + d_fy)
            new_e = wet * (e + half_all * d_hx)
            new_n = wet * (nf + half_all * d_hy)
            advanced.append((new_h, new_e, new_n, dw))
        strips = advanced

    south_ref[...] = strips[1][0]

    subfaults = green_ref.shape[0]

    def project(r, acc):
        j, i = r // SRC_ROWS, r % SRC_ROWS
        block = green_ref[:, pl.ds(pl.multiple_of(r * n, n), n)].astype(jnp.float32)
        shown = south_ref[pl.ds(j * WIDTH + i, 1), :].astype(jnp.bfloat16).astype(jnp.float32)
        return acc + block * shown

    acc = lax.fori_loop(0, group * SRC_ROWS, project, jnp.zeros((subfaults, n), jnp.float32), unroll=8)
    slip = jnp.sum(acc, axis=1, keepdims=True)
    ghost_ref[0, 0] = jnp.zeros((rows, n), jnp.float32)
    ghost_ref[0, 0, 0:1, 0:subfaults] = ids_ref[...].astype(jnp.float32)
    ids = ghost_ref[0, 0, 0:n, :].T[0:subfaults, 0:1]
    faults = grad_ref.shape[1]
    which = lax.broadcasted_iota(jnp.int32, (subfaults, faults), 1).astype(jnp.float32)
    grad_ref[...] = jnp.sum(jnp.where(which == ids, slip, 0.0), axis=0, keepdims=True)


def update_kernel(level_ref, mine_ref, state_ref, depth_ref, wet_ref, out_ref, turn_ref):
    local, _, n, _ = state_ref.shape
    col = lax.broadcasted_iota(jnp.int32, (n, n), 1)
    row = lax.broadcasted_iota(jnp.int32, (n, n), 0)

    def diff_cols(f, west, east):
        right = jnp.where(col == n - 1, east, pltpu.roll(f, n - 1, 1))
        left = jnp.where(col == 0, west, pltpu.roll(f, 1, 1))
        return right - left

    def diff_rows(f, south, north):
        upper = jnp.where(row == n - 1, north, pltpu.roll(f, n - 1, 0))
        lower = jnp.where(row == 0, south, pltpu.roll(f, 1, 0))
        return upper - lower

    turn_ref[...] = jnp.zeros_like(turn_ref)
    for k in range(local):
        half_coef = half_coef_rows(level_ref[k], (1, n))
        wet = wet_ref[k].astype(jnp.float32)
        depth_wet = wet * depth_ref[k]
        height = state_ref[k, 0]
        east_flow = state_ref[k, 1]
        north_flow = state_ref[k, 2]
        for sweep in range(STEPS):
            g = mine_ref[sweep, k]
            turn_ref[0:WIDTH, :] = g
            sides = turn_ref[...].T
            west_fx, west_h = sides[:, 0:1], sides[:, 1:2]
            east_fx, east_h = sides[:, 2:3], sides[:, 3:4]
            flux_x = depth_wet * east_flow
            flux_y = depth_wet * north_flow
            new_height = height + half_coef * (
                diff_cols(flux_x, west_fx, east_fx) + diff_rows(flux_y, g[4:5], g[6:7])
            )
            new_east = wet * (east_flow + half_coef * diff_cols(height, west_h, east_h))
            new_north = wet * (north_flow + half_coef * diff_rows(height, g[5:6], g[7:8]))
            height, east_flow, north_flow = new_height, new_east, new_north
        out_ref[k, 0] = height
        out_ref[k, 1] = east_flow
        out_ref[k, 2] = north_flow


def _vmem():
    return pl.BlockSpec(memory_space=pltpu.VMEM)


def _smem():
    return pl.BlockSpec(memory_space=pltpu.SMEM)


def pack(levels, state, depth, wet_mask):
    local, _, n, _ = state.shape
    return pl.pallas_call(
        pack_kernel,
        out_shape=jax.ShapeDtypeStruct((local, PACK_ROWS, n), jnp.float32),
        in_specs=[_smem()] + [_vmem()] * 3,
        out_specs=_vmem(),
    )(levels, state, depth, wet_mask)


def replay(base, readers, every, green, ids, local):
    group, _, n = every.shape
    rows = group * WIDTH
    return pl.pallas_call(
        replay_kernel,
        out_shape=(
            jax.ShapeDtypeStruct((STEPS, local, WIDTH, n), jnp.float32),
            jax.ShapeDtypeStruct((1, FAULTS), jnp.float32),
        ),
        in_specs=[_smem()] + [_vmem()] * 4,
        out_specs=(_vmem(), _vmem()),
        scratch_shapes=[
            pltpu.VMEM((4, rows, rows), jnp.bfloat16),
            pltpu.VMEM((4, 2, rows, n), jnp.float32),
            pltpu.VMEM((rows, n), jnp.float32),
        ],
    )(base, readers, every, green, ids)


def update(levels, mine, state, depth, wet_mask):
    local, _, n, _ = state.shape
    cells = local * n * n
    return pl.pallas_call(
        update_kernel,
        out_shape=jax.ShapeDtypeStruct(state.shape, jnp.float32),
        in_specs=[_smem()] + [_vmem()] * 4,
        out_specs=_vmem(),
        scratch_shapes=[pltpu.VMEM((n, n), jnp.float32)],
        cost_estimate=pl.CostEstimate(
            flops=40 * STEPS * cells, transcendentals=0, bytes_accessed=4 * 8 * cells
        ),
    )(levels, mine, state, depth, wet_mask)


def all_sum(x, axis):
    size = lax.axis_size(axis)
    if size & (size - 1) == 0:
        total = x
        step = 1
        while step < size:
            total = total + lax.ppermute(total, axis, [(i, i ^ step) for i in range(size)])
            step *= 2
        return total
    total = x
    for shift in range(1, size):
        pairs = [(i, (i + shift) % size) for i in range(size)]
        total = total + lax.ppermute(x, axis, pairs)
    return total


def shards(adjoint_init, depth, wet_mask, levels, readers, green, fault_ids):
    state = adjoint_init[0]
    local, _, n, _ = state.shape
    base = (lax.axis_index("patch") * local).astype(jnp.int32).reshape(1)
    packed = pack(levels[0], state, depth[0], wet_mask[0])
    every = lax.all_gather(packed, "patch", axis=0, tiled=True)
    mine, partial_grad = replay(base, readers[0].T, every, green[0], fault_ids[0].reshape(1, -1), local)
    partial_grad = partial_grad.reshape(-1)
    group_grad = lax.all_gather(partial_grad, "patch", axis=0).sum(axis=0)
    fault_grad = all_sum(group_grad, "grp")
    state = update(levels[0], mine, state, depth[0], wet_mask[0])
    return (state[None], fault_grad)


def solution(mesh):
    placed = (
        P("grp", "patch", None, None, None),
        P("grp", "patch", None, None),
        P("grp", "patch", None, None),
        P("grp", "patch"),
        P("grp", None, None),
        P("grp", "patch", None),
        P("grp", "patch"),
    )
    return jax.shard_map(
        shards,
        mesh=mesh,
        in_specs=placed,
        out_specs=(P("grp", "patch", None, None, None), P()),
        check_vma=False,
    )
```

```python
import jax
import jax.numpy as jnp
from jax import lax
from jax.experimental import pallas as pl
from jax.experimental.pallas import tpu as pltpu
from jax.sharding import PartitionSpec as P

SRC_ROWS = 4
STEPS = 4
FAULTS = 2048
WIDTH = 8
HALF = WIDTH // 2
FIELDS = 4
KINDS = 3
NORTH_TILE = FIELDS
SOUTH_TILE = NORTH_TILE + 2
COEF_TILE = SOUTH_TILE + FIELDS
PACK_ROWS = COEF_TILE * WIDTH
HIGH = lax.Precision.HIGHEST


def half_coef_rows(level, shape):
    levels = jnp.full(shape, level, jnp.int32)
    upper = (levels >= 1).astype(jnp.float32) + 2.0 * (levels >= 2).astype(jnp.float32)
    return 0.5 * (0.1 * (1.0 + upper))


def pack_kernel(level_ref, state_ref, depth_ref, wet_ref, out_ref):
    local, _, n, _ = state_ref.shape
    for k in range(local):
        wet = wet_ref[k].astype(jnp.float32)
        fields = (state_ref[k, 0], state_ref[k, 1], state_ref[k, 2], wet * depth_ref[k])
        for f, x in enumerate(fields):
            x_t = x.T
            pair, half = divmod(f, 2)
            at = f * WIDTH
            out_ref[k, at:at + HALF, :] = x_t[0:HALF]
            out_ref[k, at + HALF:at + WIDTH, :] = x_t[n - HALF:n]
            at = (NORTH_TILE + pair) * WIDTH + half * HALF
            out_ref[k, at:at + HALF, :] = x[n - HALF:n]
            at = (SOUTH_TILE + f) * WIDTH
            out_ref[k, at:at + WIDTH, :] = x[0:WIDTH]
        at = COEF_TILE * WIDTH
        out_ref[k, at - 1:at, :] = half_coef_rows(level_ref[k], (1, n))


def replay_kernel(base_ref, readers_ref, every_ref, green_ref, ids_ref, mine_ref, grad_ref,
                  q_ref, ghost_ref, south_ref):
    group, _, n = every_ref.shape
    local = mine_ref.shape[1]
    rows = group * WIDTH
    base = base_ref[0]

    def tile(index):
        return every_ref[:, index * WIDTH:(index + 1) * WIDTH, :]

    def load(kind, f):
        pair, half = divmod(f, 2)
        if kind == 0:
            block = tile(f)
        elif kind == 1:
            block = tile(SOUTH_TILE + f)
        else:
            block = tile(NORTH_TILE + pair)
            if half == 0:
                block = pltpu.roll(block, HALF, 1)
        return block.reshape(rows, n)

    strips = [[load(kind, f) for f in range(FIELDS)] for kind in range(KINDS)]
    coef_row = every_ref[:, COEF_TILE * WIDTH - 1:COEF_TILE * WIDTH, :]
    half_all = jnp.broadcast_to(coef_row, (group, WIDTH, n)).reshape(rows, n)

    lane = lax.broadcasted_iota(jnp.int32, (1, rows), 1)
    sub = lax.broadcasted_iota(jnp.int32, (group, rows), 0)
    column = lax.broadcasted_iota(jnp.int32, (group, rows), 1)
    owner = (lax.broadcasted_iota(jnp.int32, (rows, rows), 0) // WIDTH).astype(jnp.float32)
    spread = (column // WIDTH == sub).astype(jnp.bfloat16)
    listed = jnp.dot(readers_ref[...].astype(jnp.bfloat16), spread, preferred_element_type=jnp.float32)
    for t in range(4):
        source = t ^ 1
        edge = 0 if source in (0, 2) else WIDTH - 1
        lanes = jnp.where((lane & (WIDTH - 1)) == edge, listed[source:source + 1, :], -1.0)
        q_ref[t] = (lanes == owner).astype(jnp.bfloat16)

    srow = lax.broadcasted_iota(jnp.int32, (rows, n), 0) & (WIDTH - 1)
    slane = lax.broadcasted_iota(jnp.int32, (rows, n), 1)

    def across_low(f, ghost):
        return pltpu.roll(f, rows - 1, 0) - jnp.where(srow == 0, ghost, pltpu.roll(f, 1, 0))

    def across_high(f, ghost):
        return jnp.where(srow == WIDTH - 1, ghost, pltpu.roll(f, rows - 1, 0)) - pltpu.roll(f, 1, 0)

    def pick(ghost, offset):
        return jnp.sum(jnp.where(slane == srow + offset, ghost, 0.0), axis=1, keepdims=True)

    def along(f, low, high):
        right = jnp.where(slane == n - 1, high, pltpu.roll(f, n - 1, 1))
        left = jnp.where(slane == 0, low, pltpu.roll(f, 1, 1))
        return right - left

    far = jnp.where(srow >= HALF, n - WIDTH, 0)
    for sweep in range(STEPS):
        face_data = []
        for kind in range(KINDS):
            h, e, nf, dw = strips[kind]
            flux = dw * (e if kind == 0 else nf)
            face_data.append((flux, h))
        pieces = []
        for flux, h in face_data:
            rest = jnp.concatenate([flux, h], axis=1)
            parts = []
            for _ in range(3):
                part = rest.astype(jnp.bfloat16)
                rest = rest - part.astype(jnp.float32)
                parts.append(part)
            pieces.append(parts)
        for t in range(4):
            parts = pieces[(0, 0, 1, 2)[t ^ 1]]
            total = None
            for part in parts:
                term = jnp.dot(q_ref[t], part, preferred_element_type=jnp.float32)
                total = term if total is None else total + term
            ghost_ref[t, 0] = total[:, 0:n]
            ghost_ref[t, 1] = total[:, n:2 * n]
        for k in range(local):
            at = (base + k) * WIDTH
            for t in range(4):
                for c in range(2):
                    mine_ref[sweep, k, 2 * t + c:2 * t + c + 1, :] = ghost_ref[t, c, pl.ds(at, 1), :]

        gw = [ghost_ref[0, c] for c in range(2)]
        ge = [ghost_ref[1, c] for c in range(2)]
        gs = [ghost_ref[2, c] for c in range(2)]
        gn = [ghost_ref[3, c] for c in range(2)]
        advanced = []
        for kind in range(KINDS):
            h, e, nf, dw = strips[kind]
            if sweep == STEPS - 1 and kind != 1:
                advanced.append(strips[kind])
                continue
            wet = jnp.where(dw > 0.0, 1.0, 0.0)
            fx = dw * e
            fy = dw * nf
            if kind == 0:
                def across(f, west, east):
                    upper = jnp.where(srow == WIDTH - 1, east, pltpu.roll(f, rows - 1, 0))
                    lower = jnp.where(srow == 0, west, pltpu.roll(f, 1, 0))
                    return upper - lower
                d_fx = across(fx, gw[0], ge[0])
                d_hx = across(h, gw[1], ge[1])
                d_fy = along(fy, pick(gs[0], far), pick(gn[0], far))
                d_hy = along(h, pick(gs[1], far), pick(gn[1], far))
            else:
                offset = 0 if kind == 1 else n - WIDTH
                across = across_low if kind == 1 else across_high
                ghost = gs if kind == 1 else gn
                d_fy = across(fy, ghost[0])
                d_hy = across(h, ghost[1])
                d_fx = along(fx, pick(gw[0], offset), pick(ge[0], offset))
                d_hx = along(h, pick(gw[1], offset), pick(ge[1], offset))
            new_h = h + half_all * (d_fx + d_fy)
            new_e = wet * (e + half_all * d_hx)
            new_n = wet * (nf + half_all * d_hy)
            advanced.append((new_h, new_e, new_n, dw))
        strips = advanced

    south_ref[...] = strips[1][0]

    subfaults = green_ref.shape[0]

    def project(r, acc):
        j, i = r // SRC_ROWS, r % SRC_ROWS
        block = green_ref[:, pl.ds(pl.multiple_of(r * n, n), n)].astype(jnp.float32)
        shown = south_ref[pl.ds(j * WIDTH + i, 1), :].astype(jnp.bfloat16).astype(jnp.float32)
        return acc + block * shown

    acc = lax.fori_loop(0, group * SRC_ROWS, project, jnp.zeros((subfaults, n), jnp.float32), unroll=4)
    slip = jnp.sum(acc, axis=1, keepdims=True)
    ghost_ref[0, 0] = jnp.zeros((rows, n), jnp.float32)
    ghost_ref[0, 0, 0:1, 0:subfaults] = ids_ref[...].astype(jnp.float32)
    ids = ghost_ref[0, 0, 0:n, :].T[0:subfaults, 0:1]
    faults = grad_ref.shape[1]
    which = lax.broadcasted_iota(jnp.int32, (subfaults, faults), 1).astype(jnp.float32)
    grad_ref[...] = jnp.sum(jnp.where(which == ids, slip, 0.0), axis=0, keepdims=True)


def update_kernel(level_ref, mine_ref, state_ref, depth_ref, wet_ref, out_ref, turn_ref):
    local, _, n, _ = state_ref.shape
    col = lax.broadcasted_iota(jnp.int32, (n, n), 1)
    row = lax.broadcasted_iota(jnp.int32, (n, n), 0)

    def diff_cols(f, west, east):
        right = jnp.where(col == n - 1, east, pltpu.roll(f, n - 1, 1))
        left = jnp.where(col == 0, west, pltpu.roll(f, 1, 1))
        return right - left

    def diff_rows(f, south, north):
        upper = jnp.where(row == n - 1, north, pltpu.roll(f, n - 1, 0))
        lower = jnp.where(row == 0, south, pltpu.roll(f, 1, 0))
        return upper - lower

    turn_ref[...] = jnp.zeros_like(turn_ref)
    for k in range(local):
        half_coef = half_coef_rows(level_ref[k], (1, n))
        wet = wet_ref[k].astype(jnp.float32)
        depth_wet = wet * depth_ref[k]
        height = state_ref[k, 0]
        east_flow = state_ref[k, 1]
        north_flow = state_ref[k, 2]
        for sweep in range(STEPS):
            g = mine_ref[sweep, k]
            turn_ref[0:WIDTH, :] = g
            sides = turn_ref[...].T
            west_fx, west_h = sides[:, 0:1], sides[:, 1:2]
            east_fx, east_h = sides[:, 2:3], sides[:, 3:4]
            flux_x = depth_wet * east_flow
            flux_y = depth_wet * north_flow
            new_height = height + half_coef * (
                diff_cols(flux_x, west_fx, east_fx) + diff_rows(flux_y, g[4:5], g[6:7])
            )
            new_east = wet * (east_flow + half_coef * diff_cols(height, west_h, east_h))
            new_north = wet * (north_flow + half_coef * diff_rows(height, g[5:6], g[7:8]))
            height, east_flow, north_flow = new_height, new_east, new_north
        out_ref[k, 0] = height
        out_ref[k, 1] = east_flow
        out_ref[k, 2] = north_flow


def _vmem():
    return pl.BlockSpec(memory_space=pltpu.VMEM)


def _smem():
    return pl.BlockSpec(memory_space=pltpu.SMEM)


def pack(levels, state, depth, wet_mask):
    local, _, n, _ = state.shape
    return pl.pallas_call(
        pack_kernel,
        out_shape=jax.ShapeDtypeStruct((local, PACK_ROWS, n), jnp.float32),
        in_specs=[_smem()] + [_vmem()] * 3,
        out_specs=_vmem(),
    )(levels, state, depth, wet_mask)


def replay(base, readers, every, green, ids, local):
    group, _, n = every.shape
    rows = group * WIDTH
    return pl.pallas_call(
        replay_kernel,
        out_shape=(
            jax.ShapeDtypeStruct((STEPS, local, WIDTH, n), jnp.float32),
            jax.ShapeDtypeStruct((1, FAULTS), jnp.float32),
        ),
        in_specs=[_smem()] + [_vmem()] * 4,
        out_specs=(_vmem(), _vmem()),
        scratch_shapes=[
            pltpu.VMEM((4, rows, rows), jnp.bfloat16),
            pltpu.VMEM((4, 2, rows, n), jnp.float32),
            pltpu.VMEM((rows, n), jnp.float32),
        ],
    )(base, readers, every, green, ids)


def update(levels, mine, state, depth, wet_mask):
    local, _, n, _ = state.shape
    cells = local * n * n
    return pl.pallas_call(
        update_kernel,
        out_shape=jax.ShapeDtypeStruct(state.shape, jnp.float32),
        in_specs=[_smem()] + [_vmem()] * 4,
        out_specs=_vmem(),
        scratch_shapes=[pltpu.VMEM((n, n), jnp.float32)],
        cost_estimate=pl.CostEstimate(
            flops=40 * STEPS * cells, transcendentals=0, bytes_accessed=4 * 8 * cells
        ),
    )(levels, mine, state, depth, wet_mask)


def all_sum(x, axis):
    size = lax.axis_size(axis)
    total = x
    for shift in range(1, size):
        if size & (size - 1) == 0:
            pairs = [(i, i ^ shift) for i in range(size)]
        else:
            pairs = [(i, (i + shift) % size) for i in range(size)]
        total = total + lax.ppermute(x, axis, pairs)
    return total


def shards(adjoint_init, depth, wet_mask, levels, readers, green, fault_ids):
    state = adjoint_init[0]
    local, _, n, _ = state.shape
    base = (lax.axis_index("patch") * local).astype(jnp.int32).reshape(1)
    packed = pack(levels[0], state, depth[0], wet_mask[0])
    every = lax.all_gather(packed, "patch", axis=0, tiled=True)
    mine, partial_grad = replay(base, readers[0].T, every, green[0], fault_ids[0].reshape(1, -1), local)
    partial_grad = partial_grad.reshape(-1)
    group_grad = lax.all_gather(partial_grad, "patch", axis=0).sum(axis=0)
    fault_grad = all_sum(group_grad, "grp")
    state = update(levels[0], mine, state, depth[0], wet_mask[0])
    return (state[None], fault_grad)


def solution(mesh):
    placed = (
        P("grp", "patch", None, None, None),
        P("grp", "patch", None, None),
        P("grp", "patch", None, None),
        P("grp", "patch"),
        P("grp", None, None),
        P("grp", "patch", None),
        P("grp", "patch"),
    )
    return jax.shard_map(
        shards,
        mesh=mesh,
        in_specs=placed,
        out_specs=(P("grp", "patch", None, None, None), P()),
        check_vma=False,
    )
```
